32 devices in a mesh: dp: 8 (over z, core), shard: 4 (over y, x).
Axes of the slice: x: 2, y: 2, z: 4, core: 2. Of those that a mesh axis runs over, the one named last changes fastest.
Arguments:
- grad_partials: bfloat16 [8, 32, 256, 256], P('dp', 'shard'), may hold values from -8 to 8
- owners: int32 [32, 1], P('shard'), may hold values from 0 to 7; in each aligned block of 8 rows (0 to 7, 8 to 15, ...) at most 2 rows name the same one
- weight_blocks: int32 [9], replicated, may hold values from 1 to 8, 32 in all
- stats_left: float32 [8, 4, 2, 256, 256], P('dp', 'shard'), may hold values from -6 to 6
- stats_right: float32 [8, 4, 2, 256, 256], P('dp', 'shard'), may hold values from -6 to 6
- root_left: bfloat16 [8, 4, 2, 256, 256], P('dp', 'shard'), may hold values from -0.375 to 0.375
- root_right: bfloat16 [8, 4, 2, 256, 256], P('dp', 'shard'), may hold values from -0.375 to 0.375
- second_moment: float32 [8, 4, 2, 256, 256], P('dp', 'shard'), may hold values from 0.0015 to 0.6
- master: float32 [8, 4, 2, 256, 256], P('dp', 'shard'), may hold values from -6 to 6
Outputs:
- new_left: float32 [8, 4, 2, 256, 256], P('dp', 'shard')
- new_right: float32 [8, 4, 2, 256, 256], P('dp', 'shard')
- new_moment: float32 [8, 4, 2, 256, 256], P('dp', 'shard')
- new_master: float32 [8, 4, 2, 256, 256], P('dp', 'shard')
- regathered: bfloat16 [32, 256, 256], P('shard')
The draws below stay inside these ranges and needn't reach their ends.
Inputs may be any that keep to these rules, and one draw needn't show every extreme that they name: `owners`: in each aligned block of 8 rows (one column) no dp index is named more than 2 times; some column names one exactly 2 times. `weight_blocks`: sums to 32; the largest is 8.
All inputs are finite; a program needn't handle non-finite values.
Results may differ from the reference program's by a relative error of at most 0.0047.
Values may be sent and summed in bfloat16 or wider, within the bound.
No kernel may reach another device: no remote copies, remote signals or barrier semaphores. Data moves between devices by JAX's collectives and lax.ppermute only.
A program may use at most 128 MiB of HBM per device.

```python
import math
import jax
import jax.numpy as jnp
import numpy as np
from jax import lax

BS = 256
BPO = 1
NW = 9
SLOTS = 2
BPS = 8
NBLK = 32
N_DP = 8
N_SHARD = 4


def draw_grad_partials(key, part):
    key_rows, key_cols, key_noise = jax.random.split(key, 3)
    replicas = BPS // BPO
    row_scale = jnp.exp(jax.random.uniform(key_rows, (NBLK, BS, 1), jnp.float32, -1.15, 1.15))
    col_scale = jnp.exp(jax.random.uniform(key_cols, (NBLK, 1, BS), jnp.float32, -1.15, 1.15))
    noise = jnp.clip(jax.random.normal(key_noise, (replicas, NBLK, BS, BS), jnp.float32), -5.0, 5.0)
    values = noise * row_scale[None] * col_scale[None] * (0.15 * replicas ** (-0.5))
    return values.astype(jnp.bfloat16)


def draw_second_moment(key, part):
    key_block, key_entry = jax.random.split(jax.random.fold_in(key, 7), 2)
    rise = jnp.arange(N_DP, dtype=jnp.float32) / (N_DP - 1.0)
    rise_scale = jnp.exp(rise * 2.302585)[:, None, None, None, None]
    block_log = jax.random.uniform(key_block, (N_DP, N_SHARD, SLOTS, 1, 1), jnp.float32, 0.0, 2.302585)
    block_scale = 0.003 * jnp.exp(block_log)
    entry = jnp.exp(jax.random.uniform(key_entry, (N_DP, N_SHARD, SLOTS, BS, BS), jnp.float32, -0.693147, 0.693147))
    return (entry * block_scale * rise_scale).astype(jnp.float32)


def block_levels(rng, shape, pieces, smallest, top_value):
    gain, own = 1.0, jax.random.fold_in(rng, 6)
    for position, blocks in pieces:
        heights = jnp.exp(jax.random.uniform(jax.random.fold_in(own, position), (blocks,), jnp.float32, smallest / len(pieces), top_value / len(pieces)))
        gain = gain * jnp.repeat(heights, shape[position] // blocks).reshape([-1 if axis == position else 1 for axis in range(len(shape))])
    return gain


def length_profile(count, total, reach, slope):
    portions = [(1 << 20) // math.isqrt(rank ** slope) + 1 for rank in range(2, count + 1)]
    surplus, given = total - reach - (count - 1), [1] * (count - 1)
    while surplus > 0:
        candidates = [i for i in range(count - 1) if given[i] < reach]
        pool, budget = sum([portions[i] for i in candidates]), surplus
        for i in candidates:
            addition = min(reach - given[i], max(1, budget * portions[i] // pool), surplus)
            given[i] = given[i] + addition
            surplus = surplus - addition
    return np.array([reach] + given)


def uneven_parts(key, amount, total, bound, skew):
    if amount == 2:
        one = jax.random.randint(key, (), max(1, total - bound), min(bound, total - 1) + 1)
        return jnp.stack([one, total - one])
    lengths = jnp.asarray(length_profile(amount, total, bound, skew), jnp.int32)
    pairs = (amount - 1) // 2
    source_of, sink = lengths[1:1 + 2 * pairs:2], lengths[2:2 + 2 * pairs:2]
    margin = jnp.minimum(source_of - 1, bound - sink)
    moved = jax.random.randint(jax.random.fold_in(key, 1), (pairs,), 0, 1 << 20) % (margin + 1)
    lengths = lengths.at[1:1 + 2 * pairs:2].set(source_of - moved).at[2:2 + 2 * pairs:2].set(sink + moved)
    return lengths[jax.random.permutation(jax.random.fold_in(key, 2), amount)]


def deal_out(key, own, number, rows, count, top, limit, lean):
    order = jax.random.permutation(key, count)
    crowded, usual = load_shares(count, rows * top, limit, lean, True), load_shares(count, rows * top, limit, lean, False)
    places = jnp.arange(count)

    def named(lengths, offset_by):
        used = int((lengths > 0).sum())
        fixed = max(1, used // 4)
        shifted = fixed + (places - fixed + offset_by * (used - fixed)) % max(1, count - fixed)
        return jnp.zeros((count,), jnp.int32).at[order[jnp.where(places < fixed, places, shifted)]].set(jnp.asarray(lengths, jnp.int32))

    lengths = jnp.where(number % 4 == 0, named(crowded, number // 4), named(usual, number - number // 4 - 1))
    mixed = jax.random.permutation(jax.random.fold_in(own, 3), count)
    source_of, receiver = mixed[0:count // 2 * 2:2], mixed[1:count // 2 * 2:2]
    slack = jnp.minimum(lengths[source_of] - 1, limit - lengths[receiver]) // 2
    slack = jnp.where((source_of == order[0]) | (receiver == order[0]) | (lengths[receiver] == 0), 0, jnp.maximum(slack, 0))
    shifted = jax.random.randint(jax.random.fold_in(own, 4), (count // 2,), 0, 1 << 20) % (slack + 1)
    lengths = lengths.at[source_of].add(-shifted).at[receiver].add(shifted)
    items = jnp.searchsorted(jnp.cumsum(lengths), jnp.arange(rows * top), side="right").astype(jnp.int32)
    listing = items.reshape(top, rows).T
    listing = listing[jax.random.permutation(jax.random.fold_in(own, 1), rows)]
    offset_by = jax.random.randint(jax.random.fold_in(own, 2), (rows, 1), 0, top)
    return jnp.take_along_axis(listing, (jnp.arange(top)[None, :] + offset_by) % top, axis=1)


def load_shares(number_of, total, reach, lean, full):
    portions = [(1 << 20) // math.isqrt(grade ** lean) + 1 for grade in range(1, number_of + 1)]
    largest = reach if full else min(reach, max(-(-total // number_of), total * portions[0] // sum(portions)))
    least = 1 if total - largest >= number_of - 1 else 0
    holding, rest = [largest] + [least] * (number_of - 1), total - largest - least * (number_of - 1)
    while rest > 0:
        free = [i for i in range(1, number_of) if holding[i] < largest] or [i for i in range(1, number_of) if holding[i] < reach]
        whole, left = sum([portions[i] for i in free]), rest
        for i in free:
            more = min(reach - holding[i], max(1, left * portions[i] // whole), rest)
            holding[i] = holding[i] + more
            rest = rest - more
    return np.array(holding)


def bell_draw(key, dims, scale, limit, shards=(), kind=jnp.bfloat16):
    array = scale * jax.random.normal(key, dims, jnp.float32)
    if shards:
        array = array * block_levels(key, dims, shards, -0.22, 0.18)
    return jnp.clip(array, -limit, limit).astype(kind)


def setup_inputs(seed: int = 0) -> dict:
    streams_of = jax.random.split(jax.random.key(seed), 10)
    grad_partials = draw_grad_partials(jax.random.fold_in(streams_of[9], 71), 0)
    owners_keys = jax.random.split(jax.random.fold_in(streams_of[1], 1), NBLK // BPS)
    owners_turns = jax.random.permutation(jax.random.fold_in(streams_of[1], 3), NBLK // BPS)
    owners = jax.vmap(lambda own, number: deal_out(jax.random.fold_in(streams_of[1], 2), own, number, BPS, N_DP, 1, SLOTS, 2))(owners_keys, owners_turns).reshape((NBLK, 1))
    weight_blocks = uneven_parts(streams_of[2], NW, NBLK, NBLK // 4, 2).astype(jnp.int32)
    stats_left = bell_draw(streams_of[3], (N_DP, N_SHARD, SLOTS, BS, BS), 1.0, 6.0, ((0, 8), (1, 4)), jnp.float32)
    stats_right = bell_draw(streams_of[4], (N_DP, N_SHARD, SLOTS, BS, BS), 1.0, 6.0, ((0, 8), (1, 4)), jnp.float32)
    root_left = bell_draw(streams_of[5], (N_DP, N_SHARD, SLOTS, BS, BS), BS ** -0.5, 0.375, ((0, 8), (1, 4)))
    root_right = bell_draw(streams_of[6], (N_DP, N_SHARD, SLOTS, BS, BS), BS ** -0.5, 0.375, ((0, 8), (1, 4)))
    second_moment = draw_second_moment(jax.random.fold_in(streams_of[9], 71), 0)
    master = bell_draw(streams_of[8], (N_DP, N_SHARD, SLOTS, BS, BS), 1.0, 6.0, ((0, 8), (1, 4)), jnp.float32)
    return {"grad_partials": grad_partials, "owners": owners, "weight_blocks": weight_blocks, "stats_left": stats_left, "stats_right": stats_right, "root_left": root_left, "root_right": root_right, "second_moment": second_moment, "master": master}


BETA = 0.95
RATE = 0.3
ADAM_EPS = 1e-08
NORM_EPS = 1e-06

def reference(grad_partials, owners, weight_blocks, stats_left, stats_right, root_left, root_right, second_moment, master):
    zeros_sum = jnp.zeros((NBLK, BS, BS), jnp.float32)
    summed = lax.fori_loop(0, N_DP, lambda m, acc: acc + grad_partials[m].astype(jnp.float32), zeros_sum)
    owner_of = owners[:, 0].astype(jnp.int32)
    blocks = jnp.arange(NBLK, dtype=jnp.int32)
    column = blocks // BPS
    keyed = column * N_DP + owner_of
    onehot = (keyed[:, None] == jnp.arange(N_SHARD * N_DP, dtype=jnp.int32)[None, :]).astype(jnp.int32)
    slot_rank = lax.optimization_barrier(jnp.sum((jnp.cumsum(onehot, axis=0) - onehot) * onehot, axis=1)).astype(jnp.int32)
    ends = jnp.cumsum(weight_blocks.astype(jnp.int32))
    weight_id = lax.optimization_barrier(jnp.sum((blocks[:, None] >= ends[None, :]).astype(jnp.int32), axis=1))
    left = stats_left[owner_of, column, slot_rank]
    right = stats_right[owner_of, column, slot_rank]
    root_l = root_left[owner_of, column, slot_rank].astype(jnp.float32)
    root_r = root_right[owner_of, column, slot_rank].astype(jnp.float32)
    moment = second_moment[owner_of, column, slot_rank]
    weights = master[owner_of, column, slot_rank]
    hp = lax.Precision.HIGHEST
    lnew = BETA * left + (1.0 - BETA) * jnp.einsum('bij,bkj->bik', summed, summed, precision=hp)
    rnew = BETA * right + (1.0 - BETA) * jnp.einsum('bji,bjk->bik', summed, summed, precision=hp)
    grad_half = summed.astype(jnp.bfloat16).astype(jnp.float32)
    inner = jnp.einsum('bij,bjk->bik', root_l, grad_half, precision=hp).astype(jnp.bfloat16).astype(jnp.float32)
    precond = jnp.einsum('bij,bjk->bik', inner, root_r, precision=hp)
    vnew = BETA * moment + (1.0 - BETA) * summed * summed
    adam = summed / (jnp.sqrt(vnew) + ADAM_EPS)
    adam_sq = lax.optimization_barrier(jnp.sum(adam * adam, axis=(1, 2)))
    prec_sq = lax.optimization_barrier(jnp.sum(precond * precond, axis=(1, 2)))
    member = (weight_id[:, None] == jnp.arange(NW, dtype=jnp.int32)[None, :]).astype(jnp.float32)
    norm_adam = lax.optimization_barrier(jnp.sum(member * adam_sq[:, None], axis=0))
    norm_prec = lax.optimization_barrier(jnp.sum(member * prec_sq[:, None], axis=0))
    scales = jnp.sqrt(norm_adam / (norm_prec + NORM_EPS))
    block_scale = lax.optimization_barrier(jnp.sum(member * scales[None, :], axis=1))
    wnew = weights - RATE * block_scale[:, None, None] * precond
    new_left = stats_left.at[owner_of, column, slot_rank].set(lnew)
    new_right = stats_right.at[owner_of, column, slot_rank].set(rnew)
    new_moment = second_moment.at[owner_of, column, slot_rank].set(vnew)
    new_master = master.at[owner_of, column, slot_rank].set(wnew)
    return (new_left, new_right, new_moment, new_master, wnew.astype(jnp.bfloat16))
```

```python
import jax
import jax.numpy as jnp
from jax import lax
from jax.sharding import PartitionSpec as P

BETA = 0.95
RATE = 0.3
ADAM_EPS = 1e-08
NORM_EPS = 1e-06


def butterfly_sum(x, axis):
    size = lax.axis_size(axis)
    if size & (size - 1):
        return lax.psum(x, axis)
    step = 1
    while step < size:
        x = x + lax.ppermute(x, axis, [(i, i ^ step) for i in range(size)])
        step *= 2
    return x


def local(
    grad_partials,
    owners,
    weight_blocks,
    stats_left,
    stats_right,
    root_left,
    root_right,
    second_moment,
    master,
):
    replica = lax.axis_index("dp")
    column = lax.axis_index("shard")
    replicas = lax.axis_size("dp")
    local_grads = grad_partials[0]
    column_blocks = local_grads.shape[0]
    slot_count = stats_left.shape[2]
    owner_of = owners[:, 0]
    onehot = (owner_of[:, None] == jnp.arange(replicas, dtype=jnp.int32)[None, :]).astype(jnp.int32)
    slot_rank = jnp.sum((jnp.cumsum(onehot, axis=0) - onehot) * onehot, axis=1)
    matches = (owner_of[None, None, :] == jnp.arange(replicas, dtype=jnp.int32)[:, None, None]) & (
        slot_rank[None, None, :] == jnp.arange(slot_count, dtype=jnp.int32)[None, :, None]
    )
    slot_table = jnp.sum(
        matches.astype(jnp.int32) * jnp.arange(column_blocks, dtype=jnp.int32)[None, None, :],
        axis=2,
    )
    slot_live = jnp.any(matches, axis=2)
    my_table = lax.dynamic_index_in_dim(slot_table, replica, 0, keepdims=False)
    my_live = lax.dynamic_index_in_dim(slot_live, replica, 0, keepdims=False)
    live_float = my_live.astype(jnp.float32)[:, None, None]
    summed = lax.psum(local_grads.astype(jnp.float32), "dp")
    owned_grad = jnp.take(summed, my_table, axis=0) * live_float
    left = stats_left[0, 0]
    right = stats_right[0, 0]
    moment = second_moment[0, 0]
    weights = master[0, 0]
    global_block = column * column_blocks + my_table
    ends = jnp.cumsum(weight_blocks)
    weight_id = jnp.sum((global_block[:, None] >= ends[None, :]).astype(jnp.int32), axis=1)
    member = (
        weight_id[:, None] == jnp.arange(weight_blocks.shape[0], dtype=jnp.int32)[None, :]
    ).astype(jnp.float32) * my_live.astype(jnp.float32)[:, None]
    vnew = BETA * moment + (1.0 - BETA) * owned_grad * owned_grad
    adam = owned_grad / (jnp.sqrt(vnew) + ADAM_EPS)
    adam_terms = jnp.sum(member * jnp.sum(adam * adam, axis=(1, 2))[:, None], axis=0)
    highest = lax.Precision.HIGHEST
    lnew = BETA * left + (1.0 - BETA) * jnp.einsum(
        "sij,skj->sik", owned_grad, owned_grad, precision=highest
    )
    rnew = BETA * right + (1.0 - BETA) * jnp.einsum(
        "sji,sjk->sik", owned_grad, owned_grad, precision=highest
    )
    grad_half = owned_grad.astype(jnp.bfloat16)
    inner = jnp.einsum(
        "sij,sjk->sik", root_left[0, 0], grad_half, preferred_element_type=jnp.float32
    ).astype(jnp.bfloat16)
    precond = jnp.einsum(
        "sij,sjk->sik", inner, root_right[0, 0], preferred_element_type=jnp.float32
    )
    prec_terms = jnp.sum(member * jnp.sum(precond * precond, axis=(1, 2))[:, None], axis=0)
    norms = butterfly_sum(butterfly_sum(jnp.stack([adam_terms, prec_terms]), "dp"), "shard")
    norm_adam = norms[0]
    norm_prec = norms[1]
    scales = jnp.sqrt(norm_adam / (norm_prec + NORM_EPS))
    slot_scale = jnp.sum(member * scales[None, :], axis=1)
    wnew = weights - RATE * slot_scale[:, None, None] * precond
    live_mask = my_live[:, None, None]
    out_left = jnp.where(live_mask, lnew, left)
    out_right = jnp.where(live_mask, rnew, right)
    out_moment = jnp.where(live_mask, vnew, moment)
    out_master = jnp.where(live_mask, wnew, weights)
    gathered = lax.all_gather(out_master.astype(jnp.bfloat16), "dp", axis=0, tiled=True)
    regathered = jnp.take(gathered, owner_of * slot_count + slot_rank, axis=0)
    return (
        out_left[None, None],
        out_right[None, None],
        out_moment[None, None],
        out_master[None, None],
        regathered,
    )


def solution(mesh):
    in_specs = (
        P("dp", "shard", None, None),
        P("shard", None),
        P(),
        P("dp", "shard", None, None, None),
        P("dp", "shard", None, None, None),
        P("dp", "shard", None, None, None),
        P("dp", "shard", None, None, None),
        P("dp", "shard", None, None, None),
        P("dp", "shard", None, None, None),
    )
    out_specs = (
        P("dp", "shard", None, None, None),
        P("dp", "shard", None, None, None),
        P("dp", "shard", None, None, None),
        P("dp", "shard", None, None, None),
        P("shard", None, None),
    )
    return jax.shard_map(local, mesh=mesh, in_specs=in_specs, out_specs=out_specs, check_vma=False)
```

```python
import jax
import jax.numpy as jnp
from jax import lax
from jax.sharding import PartitionSpec as P

BETA = 0.95
RATE = 0.3
ADAM_EPS = 1e-08
NORM_EPS = 1e-06


def butterfly_sum(x, axis):
    size = lax.axis_size(axis)
    if size & (size - 1):
        return lax.psum(x, axis)
    step = 1
    while step < size:
        x = x + lax.ppermute(x, axis, [(i, i ^ step) for i in range(size)])
        step *= 2
    return x


def local(
    grad_partials,
    owners,
    weight_blocks,
    stats_left,
    stats_right,
    root_left,
    root_right,
    second_moment,
    master,
):
    replica = lax.axis_index("dp")
    column = lax.axis_index("shard")
    replicas = lax.axis_size("dp")
    local_grads = grad_partials[0]
    column_blocks = local_grads.shape[0]
    slot_count = stats_left.shape[2]
    owner_of = owners[:, 0]
    onehot = (owner_of[:, None] == jnp.arange(replicas, dtype=jnp.int32)[None, :]).astype(jnp.int32)
    slot_rank = jnp.sum((jnp.cumsum(onehot, axis=0) - onehot) * onehot, axis=1)
    matches = (owner_of[None, None, :] == jnp.arange(replicas, dtype=jnp.int32)[:, None, None]) & (
        slot_rank[None, None, :] == jnp.arange(slot_count, dtype=jnp.int32)[None, :, None]
    )
    slot_table = jnp.sum(
        matches.astype(jnp.int32) * jnp.arange(column_blocks, dtype=jnp.int32)[None, None, :],
        axis=2,
    )
    slot_live = jnp.any(matches, axis=2)
    my_table = lax.dynamic_index_in_dim(slot_table, replica, 0, keepdims=False)
    my_live = lax.dynamic_index_in_dim(slot_live, replica, 0, keepdims=False)
    live_float = my_live.astype(jnp.float32)[:, None, None]
    by_owner = jnp.take(local_grads, slot_table.reshape(-1), axis=0).reshape(
        (replicas, slot_count) + local_grads.shape[1:]
    )
    received = lax.all_to_all(by_owner, "dp", 0, 0, tiled=True)
    owned_grad = jnp.sum(received.astype(jnp.float32), axis=0) * live_float
    left = stats_left[0, 0]
    right = stats_right[0, 0]
    moment = second_moment[0, 0]
    weights = master[0, 0]
    global_block = column * column_blocks + my_table
    ends = jnp.cumsum(weight_blocks)
    weight_id = jnp.sum((global_block[:, None] >= ends[None, :]).astype(jnp.int32), axis=1)
    member = (
        weight_id[:, None] == jnp.arange(weight_blocks.shape[0], dtype=jnp.int32)[None, :]
    ).astype(jnp.float32) * my_live.astype(jnp.float32)[:, None]
    vnew = BETA * moment + (1.0 - BETA) * owned_grad * owned_grad
    adam = owned_grad / (jnp.sqrt(vnew) + ADAM_EPS)
    adam_terms = jnp.sum(member * jnp.sum(adam * adam, axis=(1, 2))[:, None], axis=0)
    highest = lax.Precision.HIGHEST
    lnew = BETA * left + (1.0 - BETA) * jnp.einsum(
        "sij,skj->sik", owned_grad, owned_grad, precision=highest
    )
    rnew = BETA * right + (1.0 - BETA) * jnp.einsum(
        "sji,sjk->sik", owned_grad, owned_grad, precision=highest
    )
    grad_half = owned_grad.astype(jnp.bfloat16)
    inner = jnp.einsum(
        "sij,sjk->sik", root_left[0, 0], grad_half, preferred_element_type=jnp.float32
    ).astype(jnp.bfloat16)
    precond = jnp.einsum(
        "sij,sjk->sik", inner, root_right[0, 0], preferred_element_type=jnp.float32
    )
    prec_terms = jnp.sum(member * jnp.sum(precond * precond, axis=(1, 2))[:, None], axis=0)
    norms = butterfly_sum(butterfly_sum(jnp.stack([adam_terms, prec_terms]), "dp"), "shard")
    norm_adam = norms[0]
    norm_prec = norms[1]
    scales = jnp.sqrt(norm_adam / (norm_prec + NORM_EPS))
    slot_scale = jnp.sum(member * scales[None, :], axis=1)
    wnew = weights - RATE * slot_scale[:, None, None] * precond
    live_mask = my_live[:, None, None]
    out_left = jnp.where(live_mask, lnew, left)
    out_right = jnp.where(live_mask, rnew, right)
    out_moment = jnp.where(live_mask, vnew, moment)
    out_master = jnp.where(live_mask, wnew, weights)
    gathered = lax.all_gather(out_master.astype(jnp.bfloat16), "dp", axis=0, tiled=True)
    regathered = jnp.take(gathered, owner_of * slot_count + slot_rank, axis=0)
    return (
        out_left[None, None],
        out_right[None, None],
        out_moment[None, None],
        out_master[None, None],
        regathered,
    )


def solution(mesh):
    in_specs = (
        P("dp", "shard", None, None),
        P("shard", None),
        P(),
        P("dp", "shard", None, None, None),
        P("dp", "shard", None, None, None),
        P("dp", "shard", None, None, None),
        P("dp", "shard", None, None, None),
        P("dp", "shard", None, None, None),
        P("dp", "shard", None, None, None),
    )
    out_specs = (
        P("dp", "shard", None, None, None),
        P("dp", "shard", None, None, None),
        P("dp", "shard", None, None, None),
        P("dp", "shard", None, None, None),
        P("shard", None, None),
    )
    return jax.shard_map(local, mesh=mesh, in_specs=in_specs, out_specs=out_specs, check_vma=False)
```

```python
import jax
import jax.numpy as jnp
from jax import lax
from jax.sharding import PartitionSpec as P

BETA = 0.95
RATE = 0.3
ADAM_EPS = 1e-08
NORM_EPS = 1e-06


def butterfly_sum(x, axis):
    size = lax.axis_size(axis)
    if size & (size - 1):
        return lax.psum(x, axis)
    step = 1
    while step < size:
        x = x + lax.ppermute(x, axis, [(i, i ^ step) for i in range(size)])
        step *= 2
    return x


def gather_blocks(mine, owner_of, slot_rank, replica):
    size = lax.axis_size("dp")
    slot_count = mine.shape[0]
    if size % 2 or size < 4:
        gathered = lax.all_gather(mine, "dp", axis=0, tiled=True)
        return jnp.take(gathered, owner_of * slot_count + slot_rank, axis=0)
    chips = size // 2
    rightward = [(i, i + 2) for i in range(size - 2)]
    leftward = [(i + 2, i) for i in range(size - 2)]
    partner = [(i, i ^ 1) for i in range(size)]
    from_left = [None] * chips
    from_right = [None] * chips
    from_left[0] = mine
    from_right[0] = mine
    near_left = [None] * chips
    near_right = [None] * chips
    near_left[0] = lax.ppermute(mine, "dp", partner)
    near_right[0] = near_left[0]
    for step in range(1, chips):
        from_left[step] = lax.ppermute(from_left[step - 1], "dp", rightward)
        from_right[step] = lax.ppermute(from_right[step - 1], "dp", leftward)
        near_left[step] = lax.ppermute(from_left[step], "dp", partner)
        near_right[step] = lax.ppermute(from_right[step], "dp", partner)
    same_core = from_left[::-1] + from_right[1:]
    other_core = near_left[::-1] + near_right[1:]
    pieces = jnp.stack(same_core + other_core)
    chip, core = replica // 2, replica % 2
    owner_chip, owner_core = owner_of // 2, owner_of % 2
    offset = owner_chip - chip + chips - 1
    which = jnp.where(owner_core == core, 0, 1)
    index = (which * (2 * chips - 1) + offset) * slot_count + slot_rank
    return jnp.take(pieces.reshape((-1,) + mine.shape[1:]), index, axis=0)


def local(
    grad_partials,
    owners,
    weight_blocks,
    stats_left,
    stats_right,
    root_left,
    root_right,
    second_moment,
    master,
):
    replica = lax.axis_index("dp")
    column = lax.axis_index("shard")
    replicas = lax.axis_size("dp")
    local_grads = grad_partials[0]
    column_blocks = local_grads.shape[0]
    slot_count = stats_left.shape[2]
    owner_of = owners[:, 0]
    onehot = (owner_of[:, None] == jnp.arange(replicas, dtype=jnp.int32)[None, :]).astype(jnp.int32)
    slot_rank = jnp.sum((jnp.cumsum(onehot, axis=0) - onehot) * onehot, axis=1)
    matches = (owner_of[None, None, :] == jnp.arange(replicas, dtype=jnp.int32)[:, None, None]) & (
        slot_rank[None, None, :] == jnp.arange(slot_count, dtype=jnp.int32)[None, :, None]
    )
    slot_table = jnp.sum(
        matches.astype(jnp.int32) * jnp.arange(column_blocks, dtype=jnp.int32)[None, None, :],
        axis=2,
    )
    slot_live = jnp.any(matches, axis=2)
    my_table = lax.dynamic_index_in_dim(slot_table, replica, 0, keepdims=False)
    my_live = lax.dynamic_index_in_dim(slot_live, replica, 0, keepdims=False)
    live_float = my_live.astype(jnp.float32)[:, None, None]
    by_owner = jnp.take(local_grads, slot_table.reshape(-1), axis=0).reshape(
        (replicas, slot_count) + local_grads.shape[1:]
    )
    received = lax.all_to_all(by_owner, "dp", 0, 0, tiled=True)
    owned_grad = jnp.sum(received.astype(jnp.float32), axis=0) * live_float
    left = stats_left[0, 0]
    right = stats_right[0, 0]
    moment = second_moment[0, 0]
    weights = master[0, 0]
    global_block = column * column_blocks + my_table
    ends = jnp.cumsum(weight_blocks)
    weight_id = jnp.sum((global_block[:, None] >= ends[None, :]).astype(jnp.int32), axis=1)
    member = (
        weight_id[:, None] == jnp.arange(weight_blocks.shape[0], dtype=jnp.int32)[None, :]
    ).astype(jnp.float32) * my_live.astype(jnp.float32)[:, None]
    vnew = BETA * moment + (1.0 - BETA) * owned_grad * owned_grad
    adam = owned_grad / (jnp.sqrt(vnew) + ADAM_EPS)
    adam_terms = jnp.sum(member * jnp.sum(adam * adam, axis=(1, 2))[:, None], axis=0)
    highest = lax.Precision.HIGHEST
    lnew = BETA * left + (1.0 - BETA) * jnp.einsum(
        "sij,skj->sik", owned_grad, owned_grad, precision=highest
    )
    rnew = BETA * right + (1.0 - BETA) * jnp.einsum(
        "sji,sjk->sik", owned_grad, owned_grad, precision=highest
    )
    grad_half = owned_grad.astype(jnp.bfloat16)
    inner = jnp.einsum(
        "sij,sjk->sik", root_left[0, 0], grad_half, preferred_element_type=jnp.float32
    ).astype(jnp.bfloat16)
    precond = jnp.einsum(
        "sij,sjk->sik", inner, root_right[0, 0], preferred_element_type=jnp.float32
    )
    prec_terms = jnp.sum(member * jnp.sum(precond * precond, axis=(1, 2))[:, None], axis=0)
    norms = butterfly_sum(butterfly_sum(jnp.stack([adam_terms, prec_terms]), "dp"), "shard")
    norm_adam = norms[0]
    norm_prec = norms[1]
    scales = jnp.sqrt(norm_adam / (norm_prec + NORM_EPS))
    slot_scale = jnp.sum(member * scales[None, :], axis=1)
    wnew = weights - RATE * slot_scale[:, None, None] * precond
    live_mask = my_live[:, None, None]
    out_left = jnp.where(live_mask, lnew, left)
    out_right = jnp.where(live_mask, rnew, right)
    out_moment = jnp.where(live_mask, vnew, moment)
    out_master = jnp.where(live_mask, wnew, weights)
    regathered = gather_blocks(out_master.astype(jnp.bfloat16), owner_of, slot_rank, replica)
    return (
        out_left[None, None],
        out_right[None, None],
        out_moment[None, None],
        out_master[None, None],
        regathered,
    )


def solution(mesh):
    in_specs = (
        P("dp", "shard", None, None),
        P("shard", None),
        P(),
        P("dp", "shard", None, None, None),
        P("dp", "shard", None, None, None),
        P("dp", "shard", None, None, None),
        P("dp", "shard", None, None, None),
        P("dp", "shard", None, None, None),
        P("dp", "shard", None, None, None),
    )
    out_specs = (
        P("dp", "shard", None, None, None),
        P("dp", "shard", None, None, None),
        P("dp", "shard", None, None, None),
        P("dp", "shard", None, None, None),
        P("shard", None, None),
    )
    return jax.shard_map(local, mesh=mesh, in_specs=in_specs, out_specs=out_specs, check_vma=False)
```

```python
import jax
import jax.numpy as jnp
from jax import lax
from jax.experimental import pallas as pl
from jax.experimental.pallas import tpu as pltpu
from jax.sharding import PartitionSpec as P

BETA = 0.95
RATE = 0.3
ADAM_EPS = 1e-08
NORM_EPS = 1e-06


def butterfly_sum(x, axis):
    size = lax.axis_size(axis)
    if size & (size - 1):
        return lax.psum(x, axis)
    step = 1
    while step < size:
        x = x + lax.ppermute(x, axis, [(i, i ^ step) for i in range(size)])
        step *= 2
    return x


def gather_blocks(mine, owner_of, slot_rank, replica):
    size = lax.axis_size("dp")
    slot_count = mine.shape[0]
    if size % 2 or size < 4:
        gathered = lax.all_gather(mine, "dp", axis=0, tiled=True)
        return jnp.take(gathered, owner_of * slot_count + slot_rank, axis=0)
    chips = size // 2
    rightward = [(i, i + 2) for i in range(size - 2)]
    leftward = [(i + 2, i) for i in range(size - 2)]
    partner = [(i, i ^ 1) for i in range(size)]
    from_left = [None] * chips
    from_right = [None] * chips
    from_left[0] = mine
    from_right[0] = mine
    near_left = [None] * chips
    near_right = [None] * chips
    near_left[0] = lax.ppermute(mine, "dp", partner)
    near_right[0] = near_left[0]
    for step in range(1, chips):
        from_left[step] = lax.ppermute(from_left[step - 1], "dp", rightward)
        from_right[step] = lax.ppermute(from_right[step - 1], "dp", leftward)
        near_left[step] = lax.ppermute(from_left[step], "dp", partner)
        near_right[step] = lax.ppermute(from_right[step], "dp", partner)
    pieces = from_left[::-1] + from_right[1:] + near_left[::-1] + near_right[1:]
    chip, core = replica // 2, replica % 2
    owner_chip, owner_core = owner_of // 2, owner_of % 2
    offset = owner_chip - chip + chips - 1
    which = jnp.where(owner_core == core, 0, 1)
    source = jnp.clip(which * (2 * chips - 1) + offset, 0, len(pieces) - 1)
    table = jnp.stack([source, jnp.clip(slot_rank, 0, slot_count - 1)], axis=1).astype(jnp.int32)
    return pick_blocks(table, pieces)


def pick_kernel(table_ref, *refs):
    pieces, out_ref, sems = refs[:-2], refs[-2], refs[-1]

    def start(block, carry):
        for index, piece in enumerate(pieces):
            @pl.when(table_ref[block, 0] == index)
            def _():
                pltpu.make_async_copy(piece.at[table_ref[block, 1]], out_ref.at[block], sems.at[block]).start()

        return carry

    def finish(block, carry):
        pltpu.make_async_copy(pieces[0].at[0], out_ref.at[block], sems.at[block]).wait()
        return carry

    lax.fori_loop(0, out_ref.shape[0], start, 0)
    lax.fori_loop(0, out_ref.shape[0], finish, 0)


def pick_blocks(table, pieces):
    blocks = table.shape[0]
    return pl.pallas_call(
        pick_kernel,
        out_shape=jax.ShapeDtypeStruct((blocks,) + pieces[0].shape[1:], pieces[0].dtype),
        in_specs=[pl.BlockSpec(memory_space=pltpu.SMEM)] + [pl.BlockSpec(memory_space=pl.ANY)] * len(pieces),
        out_specs=pl.BlockSpec(memory_space=pl.ANY),
        scratch_shapes=[pltpu.SemaphoreType.DMA((blocks,))],
    )(table, *pieces)


def local(
    grad_partials,
    owners,
    weight_blocks,
    stats_left,
    stats_right,
    root_left,
    root_right,
    second_moment,
    master,
):
    replica = lax.axis_index("dp")
    column = lax.axis_index("shard")
    replicas = lax.axis_size("dp")
    local_grads = grad_partials[0]
    column_blocks = local_grads.shape[0]
    slot_count = stats_left.shape[2]
    owner_of = owners[:, 0]
    onehot = (owner_of[:, None] == jnp.arange(replicas, dtype=jnp.int32)[None, :]).astype(jnp.int32)
    slot_rank = jnp.sum((jnp.cumsum(onehot, axis=0) - onehot) * onehot, axis=1)
    matches = (owner_of[None, None, :] == jnp.arange(replicas, dtype=jnp.int32)[:, None, None]) & (
        slot_rank[None, None, :] == jnp.arange(slot_count, dtype=jnp.int32)[None, :, None]
    )
    slot_table = jnp.sum(
        matches.astype(jnp.int32) * jnp.arange(column_blocks, dtype=jnp.int32)[None, None, :],
        axis=2,
    )
    slot_live = jnp.any(matches, axis=2)
    my_table = lax.dynamic_index_in_dim(slot_table, replica, 0, keepdims=False)
    my_live = lax.dynamic_index_in_dim(slot_live, replica, 0, keepdims=False)
    live_float = my_live.astype(jnp.float32)[:, None, None]
    by_owner = jnp.take(local_grads, slot_table.reshape(-1), axis=0).reshape(
        (replicas, slot_count) + local_grads.shape[1:]
    )
    received = lax.all_to_all(by_owner, "dp", 0, 0, tiled=True)
    owned_grad = jnp.sum(received.astype(jnp.float32), axis=0) * live_float
    left = stats_left[0, 0]
    right = stats_right[0, 0]
    moment = second_moment[0, 0]
    weights = master[0, 0]
    global_block = column * column_blocks + my_table
    ends = jnp.cumsum(weight_blocks)
    weight_id = jnp.sum((global_block[:, None] >= ends[None, :]).astype(jnp.int32), axis=1)
    member = (
        weight_id[:, None] == jnp.arange(weight_blocks.shape[0], dtype=jnp.int32)[None, :]
    ).astype(jnp.float32) * my_live.astype(jnp.float32)[:, None]
    vnew = BETA * moment + (1.0 - BETA) * owned_grad * owned_grad
    adam = owned_grad / (jnp.sqrt(vnew) + ADAM_EPS)
    adam_terms = jnp.sum(member * jnp.sum(adam * adam, axis=(1, 2))[:, None], axis=0)
    highest = lax.Precision.HIGHEST
    lnew = BETA * left + (1.0 - BETA) * jnp.einsum(
        "sij,skj->sik", owned_grad, owned_grad, precision=highest
    )
    rnew = BETA * right + (1.0 - BETA) * jnp.einsum(
        "sji,sjk->sik", owned_grad, owned_grad, precision=highest
    )
    grad_half = owned_grad.astype(jnp.bfloat16)
    inner = jnp.einsum(
        "sij,sjk->sik", root_left[0, 0], grad_half, preferred_element_type=jnp.float32
    ).astype(jnp.bfloat16)
    precond = jnp.einsum(
        "sij,sjk->sik", inner, root_right[0, 0], preferred_element_type=jnp.float32
    )
    prec_terms = jnp.sum(member * jnp.sum(precond * precond, axis=(1, 2))[:, None], axis=0)
    norms = butterfly_sum(butterfly_sum(jnp.stack([adam_terms, prec_terms]), "dp"), "shard")
    norm_adam = norms[0]
    norm_prec = norms[1]
    scales = jnp.sqrt(norm_adam / (norm_prec + NORM_EPS))
    slot_scale = jnp.sum(member * scales[None, :], axis=1)
    wnew = weights - RATE * slot_scale[:, None, None] * precond
    live_mask = my_live[:, None, None]
    out_left = jnp.where(live_mask, lnew, left)
    out_right = jnp.where(live_mask, rnew, right)
    out_moment = jnp.where(live_mask, vnew, moment)
    out_master = jnp.where(live_mask, wnew, weights)
    regathered = gather_blocks(out_master.astype(jnp.bfloat16), owner_of, slot_rank, replica)
    return (
        out_left[None, None],
        out_right[None, None],
        out_moment[None, None],
        out_master[None, None],
        regathered,
    )


def solution(mesh):
    in_specs = (
        P("dp", "shard", None, None),
        P("shard", None),
        P(),
        P("dp", "shard", None, None, None),
        P("dp", "shard", None, None, None),
        P("dp", "shard", None, None, None),
        P("dp", "shard", None, None, None),
        P("dp", "shard", None, None, None),
        P("dp", "shard", None, None, None),
    )
    out_specs = (
        P("dp", "shard", None, None, None),
        P("dp", "shard", None, None, None),
        P("dp", "shard", None, None, None),
        P("dp", "shard", None, None, None),
        P("shard", None, None),
    )
    return jax.shard_map(local, mesh=mesh, in_specs=in_specs, out_specs=out_specs, check_vma=False)
```

```python
import jax
import jax.numpy as jnp
from jax import lax
from jax.experimental import pallas as pl
from jax.experimental.pallas import tpu as pltpu
from jax.sharding import PartitionSpec as P

BETA = 0.95
RATE = 0.3
ADAM_EPS = 1e-08
NORM_EPS = 1e-06


def butterfly_sum(x, axis):
    size = lax.axis_size(axis)
    if size & (size - 1):
        return lax.psum(x, axis)
    step = 1
    while step < size:
        x = x + lax.ppermute(x, axis, [(i, i ^ step) for i in range(size)])
        step *= 2
    return x


def gather_blocks(mine, owner_of, slot_rank, replica):
    size = lax.axis_size("dp")
    slot_count = mine.shape[0]
    if size % 2 or size < 4:
        gathered = lax.all_gather(mine, "dp", axis=0, tiled=True)
        return jnp.take(gathered, owner_of * slot_count + slot_rank, axis=0)
    chips = size // 2
    rightward = [(i, i + 2) for i in range(size - 2)]
    leftward = [(i + 2, i) for i in range(size - 2)]
    partner = [(i, i ^ 1) for i in range(size)]
    from_left = [None] * chips
    from_right = [None] * chips
    from_left[0] = mine
    from_right[0] = mine
    near_left = [None] * chips
    near_right = [None] * chips
    near_left[0] = lax.ppermute(mine, "dp", partner)
    near_right[0] = near_left[0]
    for step in range(1, chips):
        from_left[step] = lax.ppermute(from_left[step - 1], "dp", rightward)
        from_right[step] = lax.ppermute(from_right[step - 1], "dp", leftward)
        near_left[step] = lax.ppermute(from_left[step], "dp", partner)
        near_right[step] = lax.ppermute(from_right[step], "dp", partner)
    pieces = from_left[::-1] + from_right[1:] + near_left[::-1] + near_right[1:]
    chip, core = replica // 2, replica % 2
    owner_chip, owner_core = owner_of // 2, owner_of % 2
    offset = owner_chip - chip + chips - 1
    which = jnp.where(owner_core == core, 0, 1)
    source = jnp.clip(which * (2 * chips - 1) + offset, 0, len(pieces) - 1)
    table = jnp.stack([source, jnp.clip(slot_rank, 0, slot_count - 1)], axis=1).astype(jnp.int32)
    return pick_blocks(table, pieces)


def pick_kernel(table_ref, *refs):
    pieces, out_ref, sems = refs[:-2], refs[-2], refs[-1]

    def start(block, carry):
        for index, piece in enumerate(pieces):
            @pl.when(table_ref[block, 0] == index)
            def _():
                pltpu.make_async_copy(piece.at[table_ref[block, 1]], out_ref.at[block], sems.at[block]).start()

        return carry

    def finish(block, carry):
        pltpu.make_async_copy(pieces[0].at[0], out_ref.at[block], sems.at[block]).wait()
        return carry

    lax.fori_loop(0, out_ref.shape[0], start, 0)
    lax.fori_loop(0, out_ref.shape[0], finish, 0)


def pick_blocks(table, pieces):
    blocks = table.shape[0]
    return pl.pallas_call(
        pick_kernel,
        out_shape=jax.ShapeDtypeStruct((blocks,) + pieces[0].shape[1:], pieces[0].dtype),
        in_specs=[pl.BlockSpec(memory_space=pltpu.SMEM)] + [pl.BlockSpec(memory_space=pl.ANY)] * len(pieces),
        out_specs=pl.BlockSpec(memory_space=pltpu.VMEM),
        scratch_shapes=[pltpu.SemaphoreType.DMA((blocks,))],
    )(table, *pieces)


def local(
    grad_partials,
    owners,
    weight_blocks,
    stats_left,
    stats_right,
    root_left,
    root_right,
    second_moment,
    master,
):
    replica = lax.axis_index("dp")
    column = lax.axis_index("shard")
    replicas = lax.axis_size("dp")
    local_grads = grad_partials[0]
    column_blocks = local_grads.shape[0]
    slot_count = stats_left.shape[2]
    owner_of = owners[:, 0]
    onehot = (owner_of[:, None] == jnp.arange(replicas, dtype=jnp.int32)[None, :]).astype(jnp.int32)
    slot_rank = jnp.sum((jnp.cumsum(onehot, axis=0) - onehot) * onehot, axis=1)
    matches = (owner_of[None, None, :] == jnp.arange(replicas, dtype=jnp.int32)[:, None, None]) & (
        slot_rank[None, None, :] == jnp.arange(slot_count, dtype=jnp.int32)[None, :, None]
    )
    slot_table = jnp.sum(
        matches.astype(jnp.int32) * jnp.arange(column_blocks, dtype=jnp.int32)[None, None, :],
        axis=2,
    )
    slot_live = jnp.any(matches, axis=2)
    my_table = lax.dynamic_index_in_dim(slot_table, replica, 0, keepdims=False)
    my_live = lax.dynamic_index_in_dim(slot_live, replica, 0, keepdims=False)
    live_float = my_live.astype(jnp.float32)[:, None, None]
    by_owner = jnp.take(local_grads, slot_table.reshape(-1), axis=0).reshape(
        (replicas, slot_count) + local_grads.shape[1:]
    )
    received = lax.all_to_all(by_owner, "dp", 0, 0, tiled=True)
    owned_grad = jnp.sum(received.astype(jnp.float32), axis=0) * live_float
    left = stats_left[0, 0]
    right = stats_right[0, 0]
    moment = second_moment[0, 0]
    weights = master[0, 0]
    global_block = column * column_blocks + my_table
    ends = jnp.cumsum(weight_blocks)
    weight_id = jnp.sum((global_block[:, None] >= ends[None, :]).astype(jnp.int32), axis=1)
    member = (
        weight_id[:, None] == jnp.arange(weight_blocks.shape[0], dtype=jnp.int32)[None, :]
    ).astype(jnp.float32) * my_live.astype(jnp.float32)[:, None]
    vnew = BETA * moment + (1.0 - BETA) * owned_grad * owned_grad
    adam = owned_grad / (jnp.sqrt(vnew) + ADAM_EPS)
    adam_terms = jnp.sum(member * jnp.sum(adam * adam, axis=(1, 2))[:, None], axis=0)
    highest = lax.Precision.HIGHEST
    lnew = BETA * left + (1.0 - BETA) * jnp.einsum(
        "sij,skj->sik", owned_grad, owned_grad, precision=highest
    )
    rnew = BETA * right + (1.0 - BETA) * jnp.einsum(
        "sji,sjk->sik", owned_grad, owned_grad, precision=highest
    )
    grad_half = owned_grad.astype(jnp.bfloat16)
    inner = jnp.einsum(
        "sij,sjk->sik", root_left[0, 0], grad_half, preferred_element_type=jnp.float32
    ).astype(jnp.bfloat16)
    precond = jnp.einsum(
        "sij,sjk->sik", inner, root_right[0, 0], preferred_element_type=jnp.float32
    )
    prec_terms = jnp.sum(member * jnp.sum(precond * precond, axis=(1, 2))[:, None], axis=0)
    norms = butterfly_sum(butterfly_sum(jnp.stack([adam_terms, prec_terms]), "dp"), "shard")
    norm_adam = norms[0]
    norm_prec = norms[1]
    scales = jnp.sqrt(norm_adam / (norm_prec + NORM_EPS))
    slot_scale = jnp.sum(member * scales[None, :], axis=1)
    wnew = weights - RATE * slot_scale[:, None, None] * precond
    live_mask = my_live[:, None, None]
    out_left = jnp.where(live_mask, lnew, left)
    out_right = jnp.where(live_mask, rnew, right)
    out_moment = jnp.where(live_mask, vnew, moment)
    out_master = jnp.where(live_mask, wnew, weights)
    regathered = gather_blocks(out_master.astype(jnp.bfloat16), owner_of, slot_rank, replica)
    return (
        out_left[None, None],
        out_right[None, None],
        out_moment[None, None],
        out_master[None, None],
        regathered,
    )


def solution(mesh):
    in_specs = (
        P("dp", "shard", None, None),
        P("shard", None),
        P(),
        P("dp", "shard", None, None, None),
        P("dp", "shard", None, None, None),
        P("dp", "shard", None, None, None),
        P("dp", "shard", None, None, None),
        P("dp", "shard", None, None, None),
        P("dp", "shard", None, None, None),
    )
    out_specs = (
        P("dp", "shard", None, None, None),
        P("dp", "shard", None, None, None),
        P("dp", "shard", None, None, None),
        P("dp", "shard", None, None, None),
        P("shard", None, None),
    )
    return jax.shard_map(local, mesh=mesh, in_specs=in_specs, out_specs=out_specs, check_vma=False)
```

```python
import jax
import jax.numpy as jnp
from jax import lax
from jax.experimental import pallas as pl
from jax.experimental.pallas import tpu as pltpu
from jax.sharding import PartitionSpec as P

BETA = 0.95
RATE = 0.3
ADAM_EPS = 1e-08
NORM_EPS = 1e-06


def spread_sum(x, axis):
    size = lax.axis_size(axis)
    here = lax.axis_index(axis)
    received = [x] + [
        lax.ppermute(x, axis, [(i, (i + shift) % size) for i in range(size)]) for shift in range(1, size)
    ]
    by_source = jnp.take(jnp.stack(received), (here - jnp.arange(size)) % size, axis=0)
    return jnp.sum(by_source, axis=0)


def gather_blocks(mine, owner_of, slot_rank, replica):
    size = lax.axis_size("dp")
    slot_count = mine.shape[0]
    if size % 2 or size < 4:
        gathered = lax.all_gather(mine, "dp", axis=0, tiled=True)
        return jnp.take(gathered, owner_of * slot_count + slot_rank, axis=0)
    chips = size // 2
    rightward = [(i, i + 2) for i in range(size - 2)]
    leftward = [(i + 2, i) for i in range(size - 2)]
    partner = [(i, i ^ 1) for i in range(size)]
    from_left = [None] * chips
    from_right = [None] * chips
    from_left[0] = mine
    from_right[0] = mine
    near_left = [None] * chips
    near_right = [None] * chips
    near_left[0] = lax.ppermute(mine, "dp", partner)
    near_right[0] = near_left[0]
    for step in range(1, chips):
        from_left[step] = lax.ppermute(from_left[step - 1], "dp", rightward)
        from_right[step] = lax.ppermute(from_right[step - 1], "dp", leftward)
        near_left[step] = lax.ppermute(from_left[step], "dp", partner)
        near_right[step] = lax.ppermute(from_right[step], "dp", partner)
    pieces = from_left[::-1] + from_right[1:] + near_left[::-1] + near_right[1:]
    chip, core = replica // 2, replica % 2
    owner_chip, owner_core = owner_of // 2, owner_of % 2
    offset = owner_chip - chip + chips - 1
    which = jnp.where(owner_core == core, 0, 1)
    source = jnp.clip(which * (2 * chips - 1) + offset, 0, len(pieces) - 1)
    table = jnp.stack([source, jnp.clip(slot_rank, 0, slot_count - 1)], axis=1).astype(jnp.int32)
    return pick_blocks(table, pieces)


def pick_kernel(table_ref, *refs):
    pieces, out_ref, sems = refs[:-2], refs[-2], refs[-1]

    def start(block, carry):
        for index, piece in enumerate(pieces):
            @pl.when(table_ref[block, 0] == index)
            def _():
                pltpu.make_async_copy(piece.at[table_ref[block, 1]], out_ref.at[block], sems.at[block]).start()

        return carry

    def finish(block, carry):
        pltpu.make_async_copy(pieces[0].at[0], out_ref.at[block], sems.at[block]).wait()
        return carry

    lax.fori_loop(0, out_ref.shape[0], start, 0)
    lax.fori_loop(0, out_ref.shape[0], finish, 0)


def pick_blocks(table, pieces):
    blocks = table.shape[0]
    return pl.pallas_call(
        pick_kernel,
        out_shape=jax.ShapeDtypeStruct((blocks,) + pieces[0].shape[1:], pieces[0].dtype),
        in_specs=[pl.BlockSpec(memory_space=pltpu.SMEM)] + [pl.BlockSpec(memory_space=pl.ANY)] * len(pieces),
        out_specs=pl.BlockSpec(memory_space=pltpu.VMEM),
        scratch_shapes=[pltpu.SemaphoreType.DMA((blocks,))],
    )(table, *pieces)


def local(
    grad_partials,
    owners,
    weight_blocks,
    stats_left,
    stats_right,
    root_left,
    root_right,
    second_moment,
    master,
):
    replica = lax.axis_index("dp")
    column = lax.axis_index("shard")
    replicas = lax.axis_size("dp")
    local_grads = grad_partials[0]
    column_blocks = local_grads.shape[0]
    slot_count = stats_left.shape[2]
    owner_of = owners[:, 0]
    onehot = (owner_of[:, None] == jnp.arange(replicas, dtype=jnp.int32)[None, :]).astype(jnp.int32)
    slot_rank = jnp.sum((jnp.cumsum(onehot, axis=0) - onehot) * onehot, axis=1)
    matches = (owner_of[None, None, :] == jnp.arange(replicas, dtype=jnp.int32)[:, None, None]) & (
        slot_rank[None, None, :] == jnp.arange(slot_count, dtype=jnp.int32)[None, :, None]
    )
    slot_table = jnp.sum(
        matches.astype(jnp.int32) * jnp.arange(column_blocks, dtype=jnp.int32)[None, None, :],
        axis=2,
    )
    slot_live = jnp.any(matches, axis=2)
    my_table = lax.dynamic_index_in_dim(slot_table, replica, 0, keepdims=False)
    my_live = lax.dynamic_index_in_dim(slot_live, replica, 0, keepdims=False)
    live_float = my_live.astype(jnp.float32)[:, None, None]
    by_owner = jnp.take(local_grads, slot_table.reshape(-1), axis=0).reshape(
        (replicas, slot_count) + local_grads.shape[1:]
    )
    received = lax.all_to_all(by_owner, "dp", 0, 0, tiled=True)
    owned_grad = jnp.sum(received.astype(jnp.float32), axis=0) * live_float
    left = stats_left[0, 0]
    right = stats_right[0, 0]
    moment = second_moment[0, 0]
    weights = master[0, 0]
    global_block = column * column_blocks + my_table
    ends = jnp.cumsum(weight_blocks)
    weight_id = jnp.sum((global_block[:, None] >= ends[None, :]).astype(jnp.int32), axis=1)
    member = (
        weight_id[:, None] == jnp.arange(weight_blocks.shape[0], dtype=jnp.int32)[None, :]
    ).astype(jnp.float32) * my_live.astype(jnp.float32)[:, None]
    vnew = BETA * moment + (1.0 - BETA) * owned_grad * owned_grad
    adam = owned_grad / (jnp.sqrt(vnew) + ADAM_EPS)
    adam_terms = jnp.sum(member * jnp.sum(adam * adam, axis=(1, 2))[:, None], axis=0)
    highest = lax.Precision.HIGHEST
    lnew = BETA * left + (1.0 - BETA) * jnp.einsum(
        "sij,skj->sik", owned_grad, owned_grad, precision=highest
    )
    rnew = BETA * right + (1.0 - BETA) * jnp.einsum(
        "sji,sjk->sik", owned_grad, owned_grad, precision=highest
    )
    grad_half = owned_grad.astype(jnp.bfloat16)
    inner = jnp.einsum(
        "sij,sjk->sik", root_left[0, 0], grad_half, preferred_element_type=jnp.float32
    ).astype(jnp.bfloat16)
    precond = jnp.einsum(
        "sij,sjk->sik", inner, root_right[0, 0], preferred_element_type=jnp.float32
    )
    prec_terms = jnp.sum(member * jnp.sum(precond * precond, axis=(1, 2))[:, None], axis=0)
    norms = spread_sum(spread_sum(jnp.stack([adam_terms, prec_terms]), "dp"), "shard")
    norms, lnew, rnew = lax.optimization_barrier((norms, lnew, rnew))
    norm_adam = norms[0]
    norm_prec = norms[1]
    scales = jnp.sqrt(norm_adam / (norm_prec + NORM_EPS))
    slot_scale = jnp.sum(member * scales[None, :], axis=1)
    wnew = weights - RATE * slot_scale[:, None, None] * precond
    live_mask = my_live[:, None, None]
    out_left = jnp.where(live_mask, lnew, left)
    out_right = jnp.where(live_mask, rnew, right)
    out_moment = jnp.where(live_mask, vnew, moment)
    out_master = jnp.where(live_mask, wnew, weights)
    regathered = gather_blocks(out_master.astype(jnp.bfloat16), owner_of, slot_rank, replica)
    return (
        out_left[None, None],
        out_right[None, None],
        out_moment[None, None],
        out_master[None, None],
        regathered,
    )


def solution(mesh):
    in_specs = (
        P("dp", "shard", None, None),
        P("shard", None),
        P(),
        P("dp", "shard", None, None, None),
        P("dp", "shard", None, None, None),
        P("dp", "shard", None, None, None),
        P("dp", "shard", None, None, None),
        P("dp", "shard", None, None, None),
        P("dp", "shard", None, None, None),
    )
    out_specs = (
        P("dp", "shard", None, None, None),
        P("dp", "shard", None, None, None),
        P("dp", "shard", None, None, None),
        P("dp", "shard", None, None, None),
        P("shard", None, None),
    )
    return jax.shard_map(local, mesh=mesh, in_specs=in_specs, out_specs=out_specs, check_vma=False)
```

```python
import jax
import jax.numpy as jnp
from jax import lax
from jax.experimental import pallas as pl
from jax.experimental.pallas import tpu as pltpu
from jax.sharding import PartitionSpec as P

BETA = 0.95
RATE = 0.3
ADAM_EPS = 1e-08
NORM_EPS = 1e-06


def butterfly_sum(x, axis):
    size = lax.axis_size(axis)
    if size & (size - 1):
        return lax.psum(x, axis)
    step = 1
    while step < size:
        x = x + lax.ppermute(x, axis, [(i, i ^ step) for i in range(size)])
        step *= 2
    return x


def gather_blocks(mine, owner_of, slot_rank, replica):
    size = lax.axis_size("dp")
    slot_count = mine.shape[0]
    if size % 2 or size < 4:
        gathered = lax.all_gather(mine, "dp", axis=0, tiled=True)
        return jnp.take(gathered, owner_of * slot_count + slot_rank, axis=0)
    chips = size // 2
    rightward = [(i, i + 2) for i in range(size - 2)]
    leftward = [(i + 2, i) for i in range(size - 2)]
    partner = [(i, i ^ 1) for i in range(size)]
    from_left = [None] * chips
    from_right = [None] * chips
    from_left[0] = mine
    from_right[0] = mine
    near_left = [None] * chips
    near_right = [None] * chips
    near_left[0] = lax.ppermute(mine, "dp", partner)
    near_right[0] = near_left[0]
    for step in range(1, chips):
        from_left[step] = lax.ppermute(from_left[step - 1], "dp", rightward)
        from_right[step] = lax.ppermute(from_right[step - 1], "dp", leftward)
        near_left[step] = lax.ppermute(from_left[step], "dp", partner)
        near_right[step] = lax.ppermute(from_right[step], "dp", partner)
    pieces = from_left[::-1] + from_right[1:] + near_left[::-1] + near_right[1:]
    chip, core = replica // 2, replica % 2
    owner_chip, owner_core = owner_of // 2, owner_of % 2
    offset = owner_chip - chip + chips - 1
    which = jnp.where(owner_core == core, 0, 1)
    source = jnp.clip(which * (2 * chips - 1) + offset, 0, len(pieces) - 1)
    table = jnp.stack([source, jnp.clip(slot_rank, 0, slot_count - 1)], axis=1).astype(jnp.int32)
    return pick_blocks(table, pieces)


def pick_kernel(table_ref, *refs):
    pieces, out_ref, sems = refs[:-2], refs[-2], refs[-1]

    def start(block, carry):
        for index, piece in enumerate(pieces):
            @pl.when(table_ref[block, 0] == index)
            def _():
                pltpu.make_async_copy(piece.at[table_ref[block, 1]], out_ref.at[block], sems.at[block]).start()

        return carry

    def finish(block, carry):
        pltpu.make_async_copy(pieces[0].at[0], out_ref.at[block], sems.at[block]).wait()
        return carry

    lax.fori_loop(0, out_ref.shape[0], start, 0)
    lax.fori_loop(0, out_ref.shape[0], finish, 0)


def pick_blocks(table, pieces):
    blocks = table.shape[0]
    return pl.pallas_call(
        pick_kernel,
        out_shape=jax.ShapeDtypeStruct((blocks,) + pieces[0].shape[1:], pieces[0].dtype),
        in_specs=[pl.BlockSpec(memory_space=pltpu.SMEM)] + [pl.BlockSpec(memory_space=pl.ANY)] * len(pieces),
        out_specs=pl.BlockSpec(memory_space=pltpu.VMEM),
        scratch_shapes=[pltpu.SemaphoreType.DMA((blocks,))],
    )(table, *pieces)


def local(
    grad_partials,
    owners,
    weight_blocks,
    stats_left,
    stats_right,
    root_left,
    root_right,
    second_moment,
    master,
):
    replica = lax.axis_index("dp")
    column = lax.axis_index("shard")
    replicas = lax.axis_size("dp")
    local_grads = grad_partials[0]
    column_blocks = local_grads.shape[0]
    slot_count = stats_left.shape[2]
    owner_of = owners[:, 0]
    onehot = (owner_of[:, None] == jnp.arange(replicas, dtype=jnp.int32)[None, :]).astype(jnp.int32)
    slot_rank = jnp.sum((jnp.cumsum(onehot, axis=0) - onehot) * onehot, axis=1)
    matches = (owner_of[None, None, :] == jnp.arange(replicas, dtype=jnp.int32)[:, None, None]) & (
        slot_rank[None, None, :] == jnp.arange(slot_count, dtype=jnp.int32)[None, :, None]
    )
    slot_table = jnp.sum(
        matches.astype(jnp.int32) * jnp.arange(column_blocks, dtype=jnp.int32)[None, None, :],
        axis=2,
    )
    slot_live = jnp.any(matches, axis=2)
    my_table = lax.dynamic_index_in_dim(slot_table, replica, 0, keepdims=False)
    my_live = lax.dynamic_index_in_dim(slot_live, replica, 0, keepdims=False)
    live_float = my_live.astype(jnp.float32)[:, None, None]
    by_owner = jnp.take(local_grads, slot_table.reshape(-1), axis=0).reshape(
        (replicas, slot_count) + local_grads.shape[1:]
    )
    received = lax.all_to_all(by_owner, "dp", 0, 0, tiled=True)
    owned_grad = jnp.sum(received.astype(jnp.float32), axis=0) * live_float
    left = stats_left[0, 0]
    right = stats_right[0, 0]
    moment = second_moment[0, 0]
    weights = master[0, 0]
    global_block = column * column_blocks + my_table
    ends = jnp.cumsum(weight_blocks)
    weight_id = jnp.sum((global_block[:, None] >= ends[None, :]).astype(jnp.int32), axis=1)
    member = (
        weight_id[:, None] == jnp.arange(weight_blocks.shape[0], dtype=jnp.int32)[None, :]
    ).astype(jnp.float32) * my_live.astype(jnp.float32)[:, None]
    vnew = BETA * moment + (1.0 - BETA) * owned_grad * owned_grad
    adam = owned_grad / (jnp.sqrt(vnew) + ADAM_EPS)
    adam_terms = jnp.sum(member * jnp.sum(adam * adam, axis=(1, 2))[:, None], axis=0)
    highest = lax.Precision.HIGHEST
    lnew = BETA * left + (1.0 - BETA) * jnp.einsum(
        "sij,skj->sik", owned_grad, owned_grad, precision=highest
    )
    rnew = BETA * right + (1.0 - BETA) * jnp.einsum(
        "sji,sjk->sik", owned_grad, owned_grad, precision=highest
    )
    grad_half = owned_grad.astype(jnp.bfloat16)
    inner = jnp.einsum(
        "sij,sjk->sik", root_left[0, 0], grad_half, preferred_element_type=jnp.float32
    ).astype(jnp.bfloat16)
    precond = jnp.einsum(
        "sij,sjk->sik", inner, root_right[0, 0], preferred_element_type=jnp.float32
    )
    prec_terms = jnp.sum(member * jnp.sum(precond * precond, axis=(1, 2))[:, None], axis=0)
    norms = butterfly_sum(butterfly_sum(jnp.stack([adam_terms, prec_terms]), "dp"), "shard")
    norms, lnew, rnew = lax.optimization_barrier((norms, lnew, rnew))
    norm_adam = norms[0]
    norm_prec = norms[1]
    scales = jnp.sqrt(norm_adam / (norm_prec + NORM_EPS))
    slot_scale = jnp.sum(member * scales[None, :], axis=1)
    wnew = weights - RATE * slot_scale[:, None, None] * precond
    live_mask = my_live[:, None, None]
    out_left = jnp.where(live_mask, lnew, left)
    out_right = jnp.where(live_mask, rnew, right)
    out_moment = jnp.where(live_mask, vnew, moment)
    out_master = jnp.where(live_mask, wnew, weights)
    regathered = gather_blocks(out_master.astype(jnp.bfloat16), owner_of, slot_rank, replica)
    return (
        out_left[None, None],
        out_right[None, None],
        out_moment[None, None],
        out_master[None, None],
        regathered,
    )


def solution(mesh):
    in_specs = (
        P("dp", "shard", None, None),
        P("shard", None),
        P(),
        P("dp", "shard", None, None, None),
        P("dp", "shard", None, None, None),
        P("dp", "shard", None, None, None),
        P("dp", "shard", None, None, None),
        P("dp", "shard", None, None, None),
        P("dp", "shard", None, None, None),
    )
    out_specs = (
        P("dp", "shard", None, None, None),
        P("dp", "shard", None, None, None),
        P("dp", "shard", None, None, None),
        P("dp", "shard", None, None, None),
        P("shard", None, None),
    )
    return jax.shard_map(local, mesh=mesh, in_specs=in_specs, out_specs=out_specs, check_vma=False)
```

```python
import jax
import jax.numpy as jnp
from jax import lax
from jax.experimental import pallas as pl
from jax.experimental.pallas import tpu as pltpu
from jax.sharding import PartitionSpec as P

BETA = 0.95
RATE = 0.3
ADAM_EPS = 1e-08
NORM_EPS = 1e-06


def butterfly_sum(x, axis):
    size = lax.axis_size(axis)
    if size & (size - 1):
        return lax.psum(x, axis)
    step = 1
    while step < size:
        x = x + lax.ppermute(x, axis, [(i, i ^ step) for i in range(size)])
        step *= 2
    return x


def gather_blocks(mine, owner_of, slot_rank, replica):
    size = lax.axis_size("dp")
    slot_count = mine.shape[0]
    if size % 2 or size < 4:
        gathered = lax.all_gather(mine, "dp", axis=0, tiled=True)
        return jnp.take(gathered, owner_of * slot_count + slot_rank, axis=0)
    chips = size // 2
    rightward = [(i, i + 2) for i in range(size - 2)]
    leftward = [(i + 2, i) for i in range(size - 2)]
    partner = [(i, i ^ 1) for i in range(size)]
    from_left = [None] * chips
    from_right = [None] * chips
    from_left[0] = mine
    from_right[0] = mine
    near_left = [None] * chips
    near_right = [None] * chips
    near_left[0] = lax.ppermute(mine, "dp", partner)
    near_right[0] = near_left[0]
    for step in range(1, chips):
        from_left[step] = lax.ppermute(from_left[step - 1], "dp", rightward)
        from_right[step] = lax.ppermute(from_right[step - 1], "dp", leftward)
        near_left[step] = lax.ppermute(from_left[step], "dp", partner)
        near_right[step] = lax.ppermute(from_right[step], "dp", partner)
    pieces = from_left[::-1] + from_right[1:] + near_left[::-1] + near_right[1:]
    chip, core = replica // 2, replica % 2
    owner_chip, owner_core = owner_of // 2, owner_of % 2
    offset = owner_chip - chip + chips - 1
    which = jnp.where(owner_core == core, 0, 1)
    source = jnp.clip(which * (2 * chips - 1) + offset, 0, len(pieces) - 1)
    table = jnp.stack([source, jnp.clip(slot_rank, 0, slot_count - 1)], axis=1).astype(jnp.int32)
    return pick_blocks(table, pieces)


def pick_kernel(table_ref, *refs):
    pieces, out_ref, sems = refs[:-2], refs[-2], refs[-1]

    def start(block, carry):
        for index, piece in enumerate(pieces):
            @pl.when(table_ref[block, 0] == index)
            def _():
                pltpu.make_async_copy(piece.at[table_ref[block, 1]], out_ref.at[block], sems.at[block]).start()

        return carry

    def finish(block, carry):
        pltpu.make_async_copy(pieces[0].at[0], out_ref.at[block], sems.at[block]).wait()
        return carry

    lax.fori_loop(0, out_ref.shape[0], start, 0)
    lax.fori_loop(0, out_ref.shape[0], finish, 0)


def pick_blocks(table, pieces):
    blocks = table.shape[0]
    return pl.pallas_call(
        pick_kernel,
        out_shape=jax.ShapeDtypeStruct((blocks,) + pieces[0].shape[1:], pieces[0].dtype),
        in_specs=[pl.BlockSpec(memory_space=pltpu.SMEM)] + [pl.BlockSpec(memory_space=pl.ANY)] * len(pieces),
        out_specs=pl.BlockSpec(memory_space=pltpu.VMEM),
        scratch_shapes=[pltpu.SemaphoreType.DMA((blocks,))],
    )(table, *pieces)


def local(
    grad_partials,
    owners,
    weight_blocks,
    stats_left,
    stats_right,
    root_left,
    root_right,
    second_moment,
    master,
):
    replica = lax.axis_index("dp")
    column = lax.axis_index("shard")
    replicas = lax.axis_size("dp")
    local_grads = grad_partials[0]
    column_blocks = local_grads.shape[0]
    slot_count = stats_left.shape[2]
    owner_of = owners[:, 0]
    block_ids = jnp.arange(column_blocks, dtype=jnp.int32)
    earlier = (owner_of[None, :] == owner_of[:, None]) & (block_ids[None, :] < block_ids[:, None])
    slot_rank = jnp.sum(earlier.astype(jnp.int32), axis=1)
    matches = (owner_of[None, None, :] == jnp.arange(replicas, dtype=jnp.int32)[:, None, None]) & (
        slot_rank[None, None, :] == jnp.arange(slot_count, dtype=jnp.int32)[None, :, None]
    )
    slot_table = jnp.sum(
        matches.astype(jnp.int32) * jnp.arange(column_blocks, dtype=jnp.int32)[None, None, :],
        axis=2,
    )
    slot_live = jnp.any(matches, axis=2)
    my_table = lax.dynamic_index_in_dim(slot_table, replica, 0, keepdims=False)
    my_live = lax.dynamic_index_in_dim(slot_live, replica, 0, keepdims=False)
    live_float = my_live.astype(jnp.float32)[:, None, None]
    by_owner = jnp.take(local_grads, slot_table.reshape(-1), axis=0, mode="clip").reshape(
        (replicas, slot_count) + local_grads.shape[1:]
    )
    received = lax.all_to_all(by_owner, "dp", 0, 0, tiled=True)
    owned_grad = jnp.sum(received.astype(jnp.float32), axis=0) * live_float
    left = stats_left[0, 0]
    right = stats_right[0, 0]
    moment = second_moment[0, 0]
    weights = master[0, 0]
    global_block = column * column_blocks + my_table
    ends = jnp.cumsum(weight_blocks)
    weight_id = jnp.sum((global_block[:, None] >= ends[None, :]).astype(jnp.int32), axis=1)
    member = (
        weight_id[:, None] == jnp.arange(weight_blocks.shape[0], dtype=jnp.int32)[None, :]
    ).astype(jnp.float32) * my_live.astype(jnp.float32)[:, None]
    vnew = BETA * moment + (1.0 - BETA) * owned_grad * owned_grad
    adam = owned_grad / (jnp.sqrt(vnew) + ADAM_EPS)
    adam_terms = jnp.sum(member * jnp.sum(adam * adam, axis=(1, 2))[:, None], axis=0)
    highest = lax.Precision.HIGHEST
    lnew = BETA * left + (1.0 - BETA) * jnp.einsum(
        "sij,skj->sik", owned_grad, owned_grad, precision=highest
    )
    rnew = BETA * right + (1.0 - BETA) * jnp.einsum(
        "sji,sjk->sik", owned_grad, owned_grad, precision=highest
    )
    grad_half = owned_grad.astype(jnp.bfloat16)
    inner = jnp.einsum(
        "sij,sjk->sik", root_left[0, 0], grad_half, preferred_element_type=jnp.float32
    ).astype(jnp.bfloat16)
    precond = jnp.einsum(
        "sij,sjk->sik", inner, root_right[0, 0], preferred_element_type=jnp.float32
    )
    prec_terms = jnp.sum(member * jnp.sum(precond * precond, axis=(1, 2))[:, None], axis=0)
    norms = butterfly_sum(butterfly_sum(jnp.stack([adam_terms, prec_terms]), "dp"), "shard")
    norm_adam = norms[0]
    norm_prec = norms[1]
    scales = jnp.sqrt(norm_adam / (norm_prec + NORM_EPS))
    slot_scale = jnp.sum(member * scales[None, :], axis=1)
    wnew = weights - RATE * slot_scale[:, None, None] * precond
    live_mask = my_live[:, None, None]
    out_left = jnp.where(live_mask, lnew, left)
    out_right = jnp.where(live_mask, rnew, right)
    out_moment = jnp.where(live_mask, vnew, moment)
    out_master = jnp.where(live_mask, wnew, weights)
    regathered = gather_blocks(out_master.astype(jnp.bfloat16), owner_of, slot_rank, replica)
    return (
        out_left[None, None],
        out_right[None, None],
        out_moment[None, None],
        out_master[None, None],
        regathered,
    )


def solution(mesh):
    in_specs = (
        P("dp", "shard", None, None),
        P("shard", None),
        P(),
        P("dp", "shard", None, None, None),
        P("dp", "shard", None, None, None),
        P("dp", "shard", None, None, None),
        P("dp", "shard", None, None, None),
        P("dp", "shard", None, None, None),
        P("dp", "shard", None, None, None),
    )
    out_specs = (
        P("dp", "shard", None, None, None),
        P("dp", "shard", None, None, None),
        P("dp", "shard", None, None, None),
        P("dp", "shard", None, None, None),
        P("shard", None, None),
    )
    return jax.shard_map(local, mesh=mesh, in_specs=in_specs, out_specs=out_specs, check_vma=False)
```

```python
import jax
import jax.numpy as jnp
from jax import lax
from jax.experimental import pallas as pl
from jax.experimental.pallas import tpu as pltpu
from jax.sharding import PartitionSpec as P

BETA = 0.95
RATE = 0.3
ADAM_EPS = 1e-08
NORM_EPS = 1e-06


def butterfly_sum(x, axis):
    size = lax.axis_size(axis)
    if size & (size - 1):
        return lax.psum(x, axis)
    step = 1
    while step < size:
        x = x + lax.ppermute(x, axis, [(i, i ^ step) for i in range(size)])
        step *= 2
    return x


def gather_blocks(mine, owner_of, slot_rank, replica):
    size = lax.axis_size("dp")
    slot_count = mine.shape[0]
    if size % 2 or size < 4:
        gathered = lax.all_gather(mine, "dp", axis=0, tiled=True)
        return jnp.take(gathered, owner_of * slot_count + slot_rank, axis=0)
    chips = size // 2
    partner = [(i, i ^ 1) for i in range(size)]
    same_core = []
    for offset in range(1 - chips, chips):
        if offset == 0:
            same_core.append(mine)
            continue
        pairs = [(i, i - 2 * offset) for i in range(size) if 0 <= i - 2 * offset < size]
        same_core.append(lax.ppermute(mine, "dp", pairs))
    other_core = [lax.ppermute(piece, "dp", partner) for piece in same_core]
    pieces = same_core + other_core
    chip, core = replica // 2, replica % 2
    owner_chip, owner_core = owner_of // 2, owner_of % 2
    offset = owner_chip - chip + chips - 1
    which = jnp.where(owner_core == core, 0, 1)
    source = jnp.clip(which * (2 * chips - 1) + offset, 0, len(pieces) - 1)
    table = jnp.stack([source, jnp.clip(slot_rank, 0, slot_count - 1)], axis=1).astype(jnp.int32)
    return pick_blocks(table, pieces)


def pick_kernel(table_ref, *refs):
    pieces, out_ref, sems = refs[:-2], refs[-2], refs[-1]

    def start(block, carry):
        for index, piece in enumerate(pieces):
            @pl.when(table_ref[block, 0] == index)
            def _():
                pltpu.make_async_copy(piece.at[table_ref[block, 1]], out_ref.at[block], sems.at[block]).start()

        return carry

    def finish(block, carry):
        pltpu.make_async_copy(pieces[0].at[0], out_ref.at[block], sems.at[block]).wait()
        return carry

    lax.fori_loop(0, out_ref.shape[0], start, 0)
    lax.fori_loop(0, out_ref.shape[0], finish, 0)


def pick_blocks(table, pieces):
    blocks = table.shape[0]
    return pl.pallas_call(
        pick_kernel,
        out_shape=jax.ShapeDtypeStruct((blocks,) + pieces[0].shape[1:], pieces[0].dtype),
        in_specs=[pl.BlockSpec(memory_space=pltpu.SMEM)] + [pl.BlockSpec(memory_space=pl.ANY)] * len(pieces),
        out_specs=pl.BlockSpec(memory_space=pltpu.VMEM),
        scratch_shapes=[pltpu.SemaphoreType.DMA((blocks,))],
    )(table, *pieces)


def local(
    grad_partials,
    owners,
    weight_blocks,
    stats_left,
    stats_right,
    root_left,
    root_right,
    second_moment,
    master,
):
    replica = lax.axis_index("dp")
    column = lax.axis_index("shard")
    replicas = lax.axis_size("dp")
    local_grads = grad_partials[0]
    column_blocks = local_grads.shape[0]
    slot_count = stats_left.shape[2]
    owner_of = owners[:, 0]
    block_ids = jnp.arange(column_blocks, dtype=jnp.int32)
    earlier = (owner_of[None, :] == owner_of[:, None]) & (block_ids[None, :] < block_ids[:, None])
    slot_rank = jnp.sum(earlier.astype(jnp.int32), axis=1)
    matches = (owner_of[None, None, :] == jnp.arange(replicas, dtype=jnp.int32)[:, None, None]) & (
        slot_rank[None, None, :] == jnp.arange(slot_count, dtype=jnp.int32)[None, :, None]
    )
    slot_table = jnp.sum(
        matches.astype(jnp.int32) * jnp.arange(column_blocks, dtype=jnp.int32)[None, None, :],
        axis=2,
    )
    slot_live = jnp.any(matches, axis=2)
    my_table = lax.dynamic_index_in_dim(slot_table, replica, 0, keepdims=False)
    my_live = lax.dynamic_index_in_dim(slot_live, replica, 0, keepdims=False)
    live_float = my_live.astype(jnp.float32)[:, None, None]
    by_owner = jnp.take(local_grads, slot_table.reshape(-1), axis=0, mode="clip").reshape(
        (replicas, slot_count) + local_grads.shape[1:]
    )
    received = lax.all_to_all(by_owner, "dp", 0, 0, tiled=True)
    owned_grad = jnp.sum(received.astype(jnp.float32), axis=0) * live_float
    left = stats_left[0, 0]
    right = stats_right[0, 0]
    moment = second_moment[0, 0]
    weights = master[0, 0]
    global_block = column * column_blocks + my_table
    ends = jnp.cumsum(weight_blocks)
    weight_id = jnp.sum((global_block[:, None] >= ends[None, :]).astype(jnp.int32), axis=1)
    member = (
        weight_id[:, None] == jnp.arange(weight_blocks.shape[0], dtype=jnp.int32)[None, :]
    ).astype(jnp.float32) * my_live.astype(jnp.float32)[:, None]
    vnew = BETA * moment + (1.0 - BETA) * owned_grad * owned_grad
    adam = owned_grad / (jnp.sqrt(vnew) + ADAM_EPS)
    adam_terms = jnp.sum(member * jnp.sum(adam * adam, axis=(1, 2))[:, None], axis=0)
    highest = lax.Precision.HIGHEST
    lnew = BETA * left + (1.0 - BETA) * jnp.einsum(
        "sij,skj->sik", owned_grad, owned_grad, precision=highest
    )
    rnew = BETA * right + (1.0 - BETA) * jnp.einsum(
        "sji,sjk->sik", owned_grad, owned_grad, precision=highest
    )
    grad_half = owned_grad.astype(jnp.bfloat16)
    inner = jnp.einsum(
        "sij,sjk->sik", root_left[0, 0], grad_half, preferred_element_type=jnp.float32
    ).astype(jnp.bfloat16)
    precond = jnp.einsum(
        "sij,sjk->sik", inner, root_right[0, 0], preferred_element_type=jnp.float32
    )
    prec_terms = jnp.sum(member * jnp.sum(precond * precond, axis=(1, 2))[:, None], axis=0)
    norms = butterfly_sum(butterfly_sum(jnp.stack([adam_terms, prec_terms]), "dp"), "shard")
    norm_adam = norms[0]
    norm_prec = norms[1]
    scales = jnp.sqrt(norm_adam / (norm_prec + NORM_EPS))
    slot_scale = jnp.sum(member * scales[None, :], axis=1)
    wnew = weights - RATE * slot_scale[:, None, None] * precond
    live_mask = my_live[:, None, None]
    out_left = jnp.where(live_mask, lnew, left)
    out_right = jnp.where(live_mask, rnew, right)
    out_moment = jnp.where(live_mask, vnew, moment)
    out_master = jnp.where(live_mask, wnew, weights)
    regathered = gather_blocks(out_master.astype(jnp.bfloat16), owner_of, slot_rank, replica)
    return (
        out_left[None, None],
        out_right[None, None],
        out_moment[None, None],
        out_master[None, None],
        regathered,
    )


def solution(mesh):
    in_specs = (
        P("dp", "shard", None, None),
        P("shard", None),
        P(),
        P("dp", "shard", None, None, None),
        P("dp", "shard", None, None, None),
        P("dp", "shard", None, None, None),
        P("dp", "shard", None, None, None),
        P("dp", "shard", None, None, None),
        P("dp", "shard", None, None, None),
    )
    out_specs = (
        P("dp", "shard", None, None, None),
        P("dp", "shard", None, None, None),
        P("dp", "shard", None, None, None),
        P("dp", "shard", None, None, None),
        P("shard", None, None),
    )
    return jax.shard_map(local, mesh=mesh, in_specs=in_specs, out_specs=out_specs, check_vma=False)
```

```python
import jax
import jax.numpy as jnp
from jax import lax
from jax.experimental import pallas as pl
from jax.experimental.pallas import tpu as pltpu
from jax.sharding import PartitionSpec as P

BETA = 0.95
RATE = 0.3
ADAM_EPS = 1e-08
NORM_EPS = 1e-06


def butterfly_sum(x, axis):
    size = lax.axis_size(axis)
    if size & (size - 1):
        return lax.psum(x, axis)
    step = 1
    while step < size:
        x = x + lax.ppermute(x, axis, [(i, i ^ step) for i in range(size)])
        step *= 2
    return x


def gather_blocks(mine, owner_of, slot_rank, replica):
    size = lax.axis_size("dp")
    slot_count = mine.shape[0]
    if size % 2 or size < 4:
        gathered = lax.all_gather(mine, "dp", axis=0, tiled=True)
        return jnp.take(gathered, owner_of * slot_count + slot_rank, axis=0)
    chips = size // 2
    rightward = [(i, i + 2) for i in range(size - 2)]
    leftward = [(i + 2, i) for i in range(size - 2)]
    from_left = [mine]
    from_right = [mine]
    for step in range(1, chips):
        from_left.append(lax.ppermute(from_left[-1], "dp", rightward))
        from_right.append(lax.ppermute(from_right[-1], "dp", leftward))
    pieces = from_left[::-1] + from_right[1:]
    chip, core = replica // 2, replica % 2
    owner_chip, owner_core = owner_of // 2, owner_of % 2
    source = jnp.clip(owner_chip - chip + chips - 1, 0, len(pieces) - 1)
    table = jnp.stack([source, jnp.clip(slot_rank, 0, slot_count - 1)], axis=1).astype(jnp.int32)
    line_blocks = pick_blocks(table, pieces)
    other_blocks = lax.ppermute(line_blocks, "dp", [(i, i ^ 1) for i in range(size)])
    return jnp.where((owner_core == core)[:, None, None], line_blocks, other_blocks)


def pick_kernel(table_ref, *refs):
    pieces, out_ref, sems = refs[:-2], refs[-2], refs[-1]

    def start(block, carry):
        for index, piece in enumerate(pieces):
            @pl.when(table_ref[block, 0] == index)
            def _():
                pltpu.make_async_copy(piece.at[table_ref[block, 1]], out_ref.at[block], sems.at[block]).start()

        return carry

    def finish(block, carry):
        pltpu.make_async_copy(pieces[0].at[0], out_ref.at[block], sems.at[block]).wait()
        return carry

    lax.fori_loop(0, out_ref.shape[0], start, 0)
    lax.fori_loop(0, out_ref.shape[0], finish, 0)


def pick_blocks(table, pieces):
    blocks = table.shape[0]
    return pl.pallas_call(
        pick_kernel,
        out_shape=jax.ShapeDtypeStruct((blocks,) + pieces[0].shape[1:], pieces[0].dtype),
        in_specs=[pl.BlockSpec(memory_space=pltpu.SMEM)] + [pl.BlockSpec(memory_space=pl.ANY)] * len(pieces),
        out_specs=pl.BlockSpec(memory_space=pltpu.VMEM),
        scratch_shapes=[pltpu.SemaphoreType.DMA((blocks,))],
    )(table, *pieces)


def local(
    grad_partials,
    owners,
    weight_blocks,
    stats_left,
    stats_right,
    root_left,
    root_right,
    second_moment,
    master,
):
    replica = lax.axis_index("dp")
    column = lax.axis_index("shard")
    replicas = lax.axis_size("dp")
    local_grads = grad_partials[0]
    column_blocks = local_grads.shape[0]
    slot_count = stats_left.shape[2]
    owner_of = owners[:, 0]
    block_ids = jnp.arange(column_blocks, dtype=jnp.int32)
    earlier = (owner_of[None, :] == owner_of[:, None]) & (block_ids[None, :] < block_ids[:, None])
    slot_rank = jnp.sum(earlier.astype(jnp.int32), axis=1)
    matches = (owner_of[None, None, :] == jnp.arange(replicas, dtype=jnp.int32)[:, None, None]) & (
        slot_rank[None, None, :] == jnp.arange(slot_count, dtype=jnp.int32)[None, :, None]
    )
    slot_table = jnp.sum(
        matches.astype(jnp.int32) * jnp.arange(column_blocks, dtype=jnp.int32)[None, None, :],
        axis=2,
    )
    slot_live = jnp.any(matches, axis=2)
    my_table = lax.dynamic_index_in_dim(slot_table, replica, 0, keepdims=False)
    my_live = lax.dynamic_index_in_dim(slot_live, replica, 0, keepdims=False)
    live_float = my_live.astype(jnp.float32)[:, None, None]
    by_owner = jnp.take(local_grads, slot_table.reshape(-1), axis=0, mode="clip").reshape(
        (replicas, slot_count) + local_grads.shape[1:]
    )
    received = lax.all_to_all(by_owner, "dp", 0, 0, tiled=True)
    owned_grad = jnp.sum(received.astype(jnp.float32), axis=0) * live_float
    left = stats_left[0, 0]
    right = stats_right[0, 0]
    moment = second_moment[0, 0]
    weights = master[0, 0]
    global_block = column * column_blocks + my_table
    ends = jnp.cumsum(weight_blocks)
    weight_id = jnp.sum((global_block[:, None] >= ends[None, :]).astype(jnp.int32), axis=1)
    member = (
        weight_id[:, None] == jnp.arange(weight_blocks.shape[0], dtype=jnp.int32)[None, :]
    ).astype(jnp.float32) * my_live.astype(jnp.float32)[:, None]
    vnew = BETA * moment + (1.0 - BETA) * owned_grad * owned_grad
    adam = owned_grad / (jnp.sqrt(vnew) + ADAM_EPS)
    adam_terms = jnp.sum(member * jnp.sum(adam * adam, axis=(1, 2))[:, None], axis=0)
    highest = lax.Precision.HIGHEST
    lnew = BETA * left + (1.0 - BETA) * jnp.einsum(
        "sij,skj->sik", owned_grad, owned_grad, precision=highest
    )
    rnew = BETA * right + (1.0 - BETA) * jnp.einsum(
        "sji,sjk->sik", owned_grad, owned_grad, precision=highest
    )
    grad_half = owned_grad.astype(jnp.bfloat16)
    inner = jnp.einsum(
        "sij,sjk->sik", root_left[0, 0], grad_half, preferred_element_type=jnp.float32
    ).astype(jnp.bfloat16)
    precond = jnp.einsum(
        "sij,sjk->sik", inner, root_right[0, 0], preferred_element_type=jnp.float32
    )
    prec_terms = jnp.sum(member * jnp.sum(precond * precond, axis=(1, 2))[:, None], axis=0)
    norms = butterfly_sum(butterfly_sum(jnp.stack([adam_terms, prec_terms]), "dp"), "shard")
    norm_adam = norms[0]
    norm_prec = norms[1]
    scales = jnp.sqrt(norm_adam / (norm_prec + NORM_EPS))
    slot_scale = jnp.sum(member * scales[None, :], axis=1)
    wnew = weights - RATE * slot_scale[:, None, None] * precond
    live_mask = my_live[:, None, None]
    out_left = jnp.where(live_mask, lnew, left)
    out_right = jnp.where(live_mask, rnew, right)
    out_moment = jnp.where(live_mask, vnew, moment)
    out_master = jnp.where(live_mask, wnew, weights)
    regathered = gather_blocks(out_master.astype(jnp.bfloat16), owner_of, slot_rank, replica)
    return (
        out_left[None, None],
        out_right[None, None],
        out_moment[None, None],
        out_master[None, None],
        regathered,
    )


def solution(mesh):
    in_specs = (
        P("dp", "shard", None, None),
        P("shard", None),
        P(),
        P("dp", "shard", None, None, None),
        P("dp", "shard", None, None, None),
        P("dp", "shard", None, None, None),
        P("dp", "shard", None, None, None),
        P("dp", "shard", None, None, None),
        P("dp", "shard", None, None, None),
    )
    out_specs = (
        P("dp", "shard", None, None, None),
        P("dp", "shard", None, None, None),
        P("dp", "shard", None, None, None),
        P("dp", "shard", None, None, None),
        P("shard", None, None),
    )
    return jax.shard_map(local, mesh=mesh, in_specs=in_specs, out_specs=out_specs, check_vma=False)
```

```python
import jax
import jax.numpy as jnp
from jax import lax
from jax.experimental import pallas as pl
from jax.experimental.pallas import tpu as pltpu
from jax.sharding import PartitionSpec as P

BETA = 0.95
RATE = 0.3
ADAM_EPS = 1e-08
NORM_EPS = 1e-06


def butterfly_sum(x, axis):
    size = lax.axis_size(axis)
    if size & (size - 1):
        return lax.psum(x, axis)
    step = 1
    while step < size:
        x = x + lax.ppermute(x, axis, [(i, i ^ step) for i in range(size)])
        step *= 2
    return x


def gather_blocks(mine, owner_of, slot_rank, replica):
    size = lax.axis_size("dp")
    slot_count = mine.shape[0]
    if size % 2 or size < 4:
        gathered = lax.all_gather(mine, "dp", axis=0, tiled=True)
        return jnp.take(gathered, owner_of * slot_count + slot_rank, axis=0)
    chips = size // 2
    rightward = [(i, i + 2) for i in range(size - 2)]
    leftward = [(i + 2, i) for i in range(size - 2)]
    partner = [(i, i ^ 1) for i in range(size)]
    from_left = [None] * chips
    from_right = [None] * chips
    from_left[0] = mine
    from_right[0] = mine
    near_left = [None] * chips
    near_right = [None] * chips
    near_left[0] = lax.ppermute(mine, "dp", partner)
    near_right[0] = near_left[0]
    for step in range(1, chips):
        from_left[step] = lax.ppermute(from_left[step - 1], "dp", rightward)
        from_right[step] = lax.ppermute(from_right[step - 1], "dp", leftward)
        near_left[step] = lax.ppermute(from_left[step], "dp", partner)
        near_right[step] = lax.ppermute(from_right[step], "dp", partner)
    pieces = from_left[::-1] + from_right[1:] + near_left[::-1] + near_right[1:]
    chip, core = replica // 2, replica % 2
    owner_chip, owner_core = owner_of // 2, owner_of % 2
    offset = owner_chip - chip + chips - 1
    which = jnp.where(owner_core == core, 0, 1)
    source = jnp.clip(which * (2 * chips - 1) + offset, 0, len(pieces) - 1)
    table = jnp.stack([source, jnp.clip(slot_rank, 0, slot_count - 1)], axis=1).astype(jnp.int32)
    return pick_blocks(table, pieces)


def pick_kernel(table_ref, *refs):
    pieces, out_ref, sems = refs[:-2], refs[-2], refs[-1]

    def start(block, carry):
        for index, piece in enumerate(pieces):
            @pl.when(table_ref[block, 0] == index)
            def _():
                pltpu.make_async_copy(piece.at[table_ref[block, 1]], out_ref.at[block], sems.at[block]).start()

        return carry

    def finish(block, carry):
        pltpu.make_async_copy(pieces[0].at[0], out_ref.at[block], sems.at[block]).wait()
        return carry

    lax.fori_loop(0, out_ref.shape[0], start, 0)
    lax.fori_loop(0, out_ref.shape[0], finish, 0)


def pick_blocks(table, pieces):
    blocks = table.shape[0]
    return pl.pallas_call(
        pick_kernel,
        out_shape=jax.ShapeDtypeStruct((blocks,) + pieces[0].shape[1:], pieces[0].dtype),
        in_specs=[pl.BlockSpec(memory_space=pltpu.SMEM)] + [pl.BlockSpec(memory_space=pl.ANY)] * len(pieces),
        out_specs=pl.BlockSpec(memory_space=pltpu.VMEM),
        scratch_shapes=[pltpu.SemaphoreType.DMA((blocks,))],
    )(table, *pieces)


def local(
    grad_partials,
    owners,
    weight_blocks,
    stats_left,
    stats_right,
    root_left,
    root_right,
    second_moment,
    master,
):
    replica = lax.axis_index("dp")
    column = lax.axis_index("shard")
    replicas = lax.axis_size("dp")
    local_grads = grad_partials[0]
    column_blocks = local_grads.shape[0]
    slot_count = stats_left.shape[2]
    owner_of = owners[:, 0]
    block_ids = jnp.arange(column_blocks, dtype=jnp.int32)
    earlier = (owner_of[None, :] == owner_of[:, None]) & (block_ids[None, :] < block_ids[:, None])
    slot_rank = jnp.sum(earlier.astype(jnp.int32), axis=1)
    matches = (owner_of[None, None, :] == jnp.arange(replicas, dtype=jnp.int32)[:, None, None]) & (
        slot_rank[None, None, :] == jnp.arange(slot_count, dtype=jnp.int32)[None, :, None]
    )
    slot_table = jnp.sum(
        matches.astype(jnp.int32) * jnp.arange(column_blocks, dtype=jnp.int32)[None, None, :],
        axis=2,
    )
    slot_live = jnp.any(matches, axis=2)
    my_table = lax.dynamic_index_in_dim(slot_table, replica, 0, keepdims=False)
    my_live = lax.dynamic_index_in_dim(slot_live, replica, 0, keepdims=False)
    live_float = my_live.astype(jnp.float32)[:, None, None]
    by_owner = jnp.take(local_grads, slot_table.reshape(-1), axis=0, mode="clip").reshape(
        (replicas, slot_count) + local_grads.shape[1:]
    )
    received = lax.all_to_all(by_owner, "dp", 0, 0, tiled=True)
    owned_grad = jnp.sum(received.astype(jnp.float32), axis=0) * live_float
    left = stats_left[0, 0]
    right = stats_right[0, 0]
    moment = second_moment[0, 0]
    weights = master[0, 0]
    global_block = column * column_blocks + my_table
    ends = jnp.cumsum(weight_blocks)
    weight_id = jnp.sum((global_block[:, None] >= ends[None, :]).astype(jnp.int32), axis=1)
    member = (
        weight_id[:, None] == jnp.arange(weight_blocks.shape[0], dtype=jnp.int32)[None, :]
    ).astype(jnp.float32) * my_live.astype(jnp.float32)[:, None]
    vnew = BETA * moment + (1.0 - BETA) * owned_grad * owned_grad
    adam = owned_grad / (jnp.sqrt(vnew) + ADAM_EPS)
    adam_terms = jnp.sum(member * jnp.sum(adam * adam, axis=(1, 2))[:, None], axis=0)
    highest = lax.Precision.HIGH
    lnew = BETA * left + (1.0 - BETA) * jnp.einsum(
        "sij,skj->sik", owned_grad, owned_grad, precision=highest
    )
    rnew = BETA * right + (1.0 - BETA) * jnp.einsum(
        "sji,sjk->sik", owned_grad, owned_grad, precision=highest
    )
    grad_half = owned_grad.astype(jnp.bfloat16)
    inner = jnp.einsum(
        "sij,sjk->sik", root_left[0, 0], grad_half, preferred_element_type=jnp.float32
    ).astype(jnp.bfloat16)
    precond = jnp.einsum(
        "sij,sjk->sik", inner, root_right[0, 0], preferred_element_type=jnp.float32
    )
    prec_terms = jnp.sum(member * jnp.sum(precond * precond, axis=(1, 2))[:, None], axis=0)
    norms = butterfly_sum(butterfly_sum(jnp.stack([adam_terms, prec_terms]), "dp"), "shard")
    norm_adam = norms[0]
    norm_prec = norms[1]
    scales = jnp.sqrt(norm_adam / (norm_prec + NORM_EPS))
    slot_scale = jnp.sum(member * scales[None, :], axis=1)
    wnew = weights - RATE * slot_scale[:, None, None] * precond
    live_mask = my_live[:, None, None]
    out_left = jnp.where(live_mask, lnew, left)
    out_right = jnp.where(live_mask, rnew, right)
    out_moment = jnp.where(live_mask, vnew, moment)
    out_master = jnp.where(live_mask, wnew, weights)
    regathered = gather_blocks(out_master.astype(jnp.bfloat16), owner_of, slot_rank, replica)
    return (
        out_left[None, None],
        out_right[None, None],
        out_moment[None, None],
        out_master[None, None],
        regathered,
    )


def solution(mesh):
    in_specs = (
        P("dp", "shard", None, None),
        P("shard", None),
        P(),
        P("dp", "shard", None, None, None),
        P("dp", "shard", None, None, None),
        P("dp", "shard", None, None, None),
        P("dp", "shard", None, None, None),
        P("dp", "shard", None, None, None),
        P("dp", "shard", None, None, None),
    )
    out_specs = (
        P("dp", "shard", None, None, None),
        P("dp", "shard", None, None, None),
        P("dp", "shard", None, None, None),
        P("dp", "shard", None, None, None),
        P("shard", None, None),
    )
    return jax.shard_map(local, mesh=mesh, in_specs=in_specs, out_specs=out_specs, check_vma=False)
```

```python
import jax
import jax.numpy as jnp
from jax import lax
from jax.experimental import pallas as pl
from jax.experimental.pallas import tpu as pltpu
from jax.sharding import PartitionSpec as P

BETA = 0.95
RATE = 0.3
ADAM_EPS = 1e-08
NORM_EPS = 1e-06


def butterfly_sum(x, axis):
    size = lax.axis_size(axis)
    if size & (size - 1):
        return lax.psum(x, axis)
    step = 1
    while step < size:
        x = x + lax.ppermute(x, axis, [(i, i ^ step) for i in range(size)])
        step *= 2
    return x


def gather_blocks(mine, owner_of, slot_rank, replica):
    size = lax.axis_size("dp")
    slot_count = mine.shape[0]
    if size % 2 or size < 4:
        gathered = lax.all_gather(mine, "dp", axis=0, tiled=True)
        return jnp.take(gathered, owner_of * slot_count + slot_rank, axis=0)
    chips = size // 2
    rightward = [(i, i + 2) for i in range(size - 2)]
    leftward = [(i + 2, i) for i in range(size - 2)]
    partner = [(i, i ^ 1) for i in range(size)]
    from_left = [None] * chips
    from_right = [None] * chips
    from_left[0] = mine
    from_right[0] = mine
    near_left = [None] * chips
    near_right = [None] * chips
    near_left[0] = lax.ppermute(mine, "dp", partner)
    near_right[0] = near_left[0]
    for step in range(1, chips):
        from_left[step] = lax.ppermute(from_left[step - 1], "dp", rightward)
        from_right[step] = lax.ppermute(from_right[step - 1], "dp", leftward)
        near_left[step] = lax.ppermute(from_left[step], "dp", partner)
        near_right[step] = lax.ppermute(from_right[step], "dp", partner)
    pieces = from_left[::-1] + from_right[1:] + near_left[::-1] + near_right[1:]
    chip, core = replica // 2, replica % 2
    owner_chip, owner_core = owner_of // 2, owner_of % 2
    offset = owner_chip - chip + chips - 1
    which = jnp.where(owner_core == core, 0, 1)
    source = jnp.clip(which * (2 * chips - 1) + offset, 0, len(pieces) - 1)
    table = jnp.stack([source, jnp.clip(slot_rank, 0, slot_count - 1)], axis=1).astype(jnp.int32)
    return pick_blocks(table, pieces)


def pick_kernel(table_ref, *refs):
    pieces, out_ref, sems = refs[:-2], refs[-2], refs[-1]

    def start(block, carry):
        for index, piece in enumerate(pieces):
            @pl.when(table_ref[block, 0] == index)
            def _():
                pltpu.make_async_copy(piece.at[table_ref[block, 1]], out_ref.at[block], sems.at[block]).start()

        return carry

    def finish(block, carry):
        pltpu.make_async_copy(pieces[0].at[0], out_ref.at[block], sems.at[block]).wait()
        return carry

    lax.fori_loop(0, out_ref.shape[0], start, 0)
    lax.fori_loop(0, out_ref.shape[0], finish, 0)


def pick_blocks(table, pieces):
    blocks = table.shape[0]
    return pl.pallas_call(
        pick_kernel,
        out_shape=jax.ShapeDtypeStruct((blocks,) + pieces[0].shape[1:], pieces[0].dtype),
        in_specs=[pl.BlockSpec(memory_space=pltpu.SMEM)] + [pl.BlockSpec(memory_space=pl.ANY)] * len(pieces),
        out_specs=pl.BlockSpec(memory_space=pltpu.VMEM),
        scratch_shapes=[pltpu.SemaphoreType.DMA((blocks,))],
    )(table, *pieces)


def local(
    grad_partials,
    owners,
    weight_blocks,
    stats_left,
    stats_right,
    root_left,
    root_right,
    second_moment,
    master,
):
    replica = lax.axis_index("dp")
    column = lax.axis_index("shard")
    replicas = lax.axis_size("dp")
    local_grads = grad_partials[0]
    column_blocks = local_grads.shape[0]
    slot_count = stats_left.shape[2]
    owner_of = owners[:, 0]
    block_ids = jnp.arange(column_blocks, dtype=jnp.int32)
    earlier = (owner_of[None, :] == owner_of[:, None]) & (block_ids[None, :] < block_ids[:, None])
    slot_rank = jnp.sum(earlier.astype(jnp.int32), axis=1)
    matches = (owner_of[None, None, :] == jnp.arange(replicas, dtype=jnp.int32)[:, None, None]) & (
        slot_rank[None, None, :] == jnp.arange(slot_count, dtype=jnp.int32)[None, :, None]
    )
    slot_table = jnp.sum(
        matches.astype(jnp.int32) * jnp.arange(column_blocks, dtype=jnp.int32)[None, None, :],
        axis=2,
    )
    slot_live = jnp.any(matches, axis=2)
    my_table = lax.dynamic_index_in_dim(slot_table, replica, 0, keepdims=False)
    my_live = lax.dynamic_index_in_dim(slot_live, replica, 0, keepdims=False)
    live_float = my_live.astype(jnp.float32)[:, None, None]
    by_owner = jnp.take(local_grads, slot_table.reshape(-1), axis=0, mode="clip").reshape(
        (replicas, slot_count) + local_grads.shape[1:]
    )
    received = [lax.all_to_all(by_owner[:, slot], "dp", 0, 0, tiled=True) for slot in range(slot_count)]
    owned_grad = jnp.stack([jnp.sum(part.astype(jnp.float32), axis=0) for part in received]) * live_float
    left = stats_left[0, 0]
    right = stats_right[0, 0]
    moment = second_moment[0, 0]
    weights = master[0, 0]
    global_block = column * column_blocks + my_table
    ends = jnp.cumsum(weight_blocks)
    weight_id = jnp.sum((global_block[:, None] >= ends[None, :]).astype(jnp.int32), axis=1)
    member = (
        weight_id[:, None] == jnp.arange(weight_blocks.shape[0], dtype=jnp.int32)[None, :]
    ).astype(jnp.float32) * my_live.astype(jnp.float32)[:, None]
    vnew = BETA * moment + (1.0 - BETA) * owned_grad * owned_grad
    adam = owned_grad / (jnp.sqrt(vnew) + ADAM_EPS)
    adam_terms = jnp.sum(member * jnp.sum(adam * adam, axis=(1, 2))[:, None], axis=0)
    highest = lax.Precision.HIGHEST
    lnew = BETA * left + (1.0 - BETA) * jnp.einsum(
        "sij,skj->sik", owned_grad, owned_grad, precision=highest
    )
    rnew = BETA * right + (1.0 - BETA) * jnp.einsum(
        "sji,sjk->sik", owned_grad, owned_grad, precision=highest
    )
    grad_half = owned_grad.astype(jnp.bfloat16)
    inner = jnp.einsum(
        "sij,sjk->sik", root_left[0, 0], grad_half, preferred_element_type=jnp.float32
    ).astype(jnp.bfloat16)
    precond = jnp.einsum(
        "sij,sjk->sik", inner, root_right[0, 0], preferred_element_type=jnp.float32
    )
    prec_terms = jnp.sum(member * jnp.sum(precond * precond, axis=(1, 2))[:, None], axis=0)
    norms = butterfly_sum(butterfly_sum(jnp.stack([adam_terms, prec_terms]), "dp"), "shard")
    norm_adam = norms[0]
    norm_prec = norms[1]
    scales = jnp.sqrt(norm_adam / (norm_prec + NORM_EPS))
    slot_scale = jnp.sum(member * scales[None, :], axis=1)
    wnew = weights - RATE * slot_scale[:, None, None] * precond
    live_mask = my_live[:, None, None]
    out_left = jnp.where(live_mask, lnew, left)
    out_right = jnp.where(live_mask, rnew, right)
    out_moment = jnp.where(live_mask, vnew, moment)
    out_master = jnp.where(live_mask, wnew, weights)
    regathered = gather_blocks(out_master.astype(jnp.bfloat16), owner_of, slot_rank, replica)
    return (
        out_left[None, None],
        out_right[None, None],
        out_moment[None, None],
        out_master[None, None],
        regathered,
    )


def solution(mesh):
    in_specs = (
        P("dp", "shard", None, None),
        P("shard", None),
        P(),
        P("dp", "shard", None, None, None),
        P("dp", "shard", None, None, None),
        P("dp", "shard", None, None, None),
        P("dp", "shard", None, None, None),
        P("dp", "shard", None, None, None),
        P("dp", "shard", None, None, None),
    )
    out_specs = (
        P("dp", "shard", None, None, None),
        P("dp", "shard", None, None, None),
        P("dp", "shard", None, None, None),
        P("dp", "shard", None, None, None),
        P("shard", None, None),
    )
    return jax.shard_map(local, mesh=mesh, in_specs=in_specs, out_specs=out_specs, check_vma=False)
```

```python
import jax
import jax.numpy as jnp
from jax import lax
from jax.experimental import pallas as pl
from jax.experimental.pallas import tpu as pltpu
from jax.sharding import PartitionSpec as P

BETA = 0.95
RATE = 0.3
ADAM_EPS = 1e-08
NORM_EPS = 1e-06


def butterfly_sum(x, axis):
    size = lax.axis_size(axis)
    if size & (size - 1):
        return lax.psum(x, axis)
    step = 1
    while step < size:
        x = x + lax.ppermute(x, axis, [(i, i ^ step) for i in range(size)])
        step *= 2
    return x


def gather_blocks(mine, owner_of, slot_rank, replica):
    size = lax.axis_size("dp")
    slot_count = mine.shape[0]
    if size % 2 or size < 4:
        gathered = lax.all_gather(mine, "dp", axis=0, tiled=True)
        return jnp.take(gathered, owner_of * slot_count + slot_rank, axis=0)
    chips = size // 2
    reach = chips // 2

    def shifted(piece, offset):
        pairs = [(i, i - 2 * offset) for i in range(size) if 0 <= i - 2 * offset < size]
        return lax.ppermute(piece, "dp", pairs)

    by_offset = {0: mine}
    for distance in range(1, reach + 1):
        for sign in (-1, 1):
            by_offset[sign * distance] = shifted(mine, sign * distance)
    for distance in range(reach + 1, chips):
        for sign in (-1, 1):
            by_offset[sign * distance] = shifted(by_offset[sign * (distance - reach)], sign * reach)
    same_core = [by_offset[offset] for offset in range(1 - chips, chips)]
    partner = [(i, i ^ 1) for i in range(size)]
    other_core = [lax.ppermute(piece, "dp", partner) for piece in same_core]
    pieces = same_core + other_core
    chip, core = replica // 2, replica % 2
    owner_chip, owner_core = owner_of // 2, owner_of % 2
    offset = owner_chip - chip + chips - 1
    which = jnp.where(owner_core == core, 0, 1)
    source = jnp.clip(which * (2 * chips - 1) + offset, 0, len(pieces) - 1)
    table = jnp.stack([source, jnp.clip(slot_rank, 0, slot_count - 1)], axis=1).astype(jnp.int32)
    return pick_blocks(table, pieces)


def pick_kernel(table_ref, *refs):
    pieces, out_ref, sems = refs[:-2], refs[-2], refs[-1]

    def start(block, carry):
        for index, piece in enumerate(pieces):
            @pl.when(table_ref[block, 0] == index)
            def _():
                pltpu.make_async_copy(piece.at[table_ref[block, 1]], out_ref.at[block], sems.at[block]).start()

        return carry

    def finish(block, carry):
        pltpu.make_async_copy(pieces[0].at[0], out_ref.at[block], sems.at[block]).wait()
        return carry

    lax.fori_loop(0, out_ref.shape[0], start, 0)
    lax.fori_loop(0, out_ref.shape[0], finish, 0)


def pick_blocks(table, pieces):
    blocks = table.shape[0]
    return pl.pallas_call(
        pick_kernel,
        out_shape=jax.ShapeDtypeStruct((blocks,) + pieces[0].shape[1:], pieces[0].dtype),
        in_specs=[pl.BlockSpec(memory_space=pltpu.SMEM)] + [pl.BlockSpec(memory_space=pl.ANY)] * len(pieces),
        out_specs=pl.BlockSpec(memory_space=pltpu.VMEM),
        scratch_shapes=[pltpu.SemaphoreType.DMA((blocks,))],
    )(table, *pieces)


def local(
    grad_partials,
    owners,
    weight_blocks,
    stats_left,
    stats_right,
    root_left,
    root_right,
    second_moment,
    master,
):
    replica = lax.axis_index("dp")
    column = lax.axis_index("shard")
    replicas = lax.axis_size("dp")
    local_grads = grad_partials[0]
    column_blocks = local_grads.shape[0]
    slot_count = stats_left.shape[2]
    owner_of = owners[:, 0]
    block_ids = jnp.arange(column_blocks, dtype=jnp.int32)
    earlier = (owner_of[None, :] == owner_of[:, None]) & (block_ids[None, :] < block_ids[:, None])
    slot_rank = jnp.sum(earlier.astype(jnp.int32), axis=1)
    matches = (owner_of[None, None, :] == jnp.arange(replicas, dtype=jnp.int32)[:, None, None]) & (
        slot_rank[None, None, :] == jnp.arange(slot_count, dtype=jnp.int32)[None, :, None]
    )
    slot_table = jnp.sum(
        matches.astype(jnp.int32) * jnp.arange(column_blocks, dtype=jnp.int32)[None, None, :],
        axis=2,
    )
    slot_live = jnp.any(matches, axis=2)
    my_table = lax.dynamic_index_in_dim(slot_table, replica, 0, keepdims=False)
    my_live = lax.dynamic_index_in_dim(slot_live, replica, 0, keepdims=False)
    live_float = my_live.astype(jnp.float32)[:, None, None]
    by_owner = jnp.take(local_grads, slot_table.reshape(-1), axis=0, mode="clip").reshape(
        (replicas, slot_count) + local_grads.shape[1:]
    )
    received = lax.all_to_all(by_owner, "dp", 0, 0, tiled=True)
    owned_grad = jnp.sum(received.astype(jnp.float32), axis=0) * live_float
    left = stats_left[0, 0]
    right = stats_right[0, 0]
    moment = second_moment[0, 0]
    weights = master[0, 0]
    global_block = column * column_blocks + my_table
    ends = jnp.cumsum(weight_blocks)
    weight_id = jnp.sum((global_block[:, None] >= ends[None, :]).astype(jnp.int32), axis=1)
    member = (
        weight_id[:, None] == jnp.arange(weight_blocks.shape[0], dtype=jnp.int32)[None, :]
    ).astype(jnp.float32) * my_live.astype(jnp.float32)[:, None]
    vnew = BETA * moment + (1.0 - BETA) * owned_grad * owned_grad
    adam = owned_grad / (jnp.sqrt(vnew) + ADAM_EPS)
    adam_terms = jnp.sum(member * jnp.sum(adam * adam, axis=(1, 2))[:, None], axis=0)
    highest = lax.Precision.HIGHEST
    lnew = BETA * left + (1.0 - BETA) * jnp.einsum(
        "sij,skj->sik", owned_grad, owned_grad, precision=highest
    )
    rnew = BETA * right + (1.0 - BETA) * jnp.einsum(
        "sji,sjk->sik", owned_grad, owned_grad, precision=highest
    )
    grad_half = owned_grad.astype(jnp.bfloat16)
    inner = jnp.einsum(
        "sij,sjk->sik", root_left[0, 0], grad_half, preferred_element_type=jnp.float32
    ).astype(jnp.bfloat16)
    precond = jnp.einsum(
        "sij,sjk->sik", inner, root_right[0, 0], preferred_element_type=jnp.float32
    )
    prec_terms = jnp.sum(member * jnp.sum(precond * precond, axis=(1, 2))[:, None], axis=0)
    norms = butterfly_sum(butterfly_sum(jnp.stack([adam_terms, prec_terms]), "dp"), "shard")
    norm_adam = norms[0]
    norm_prec = norms[1]
    scales = jnp.sqrt(norm_adam / (norm_prec + NORM_EPS))
    slot_scale = jnp.sum(member * scales[None, :], axis=1)
    wnew = weights - RATE * slot_scale[:, None, None] * precond
    live_mask = my_live[:, None, None]
    out_left = jnp.where(live_mask, lnew, left)
    out_right = jnp.where(live_mask, rnew, right)
    out_moment = jnp.where(live_mask, vnew, moment)
    out_master = jnp.where(live_mask, wnew, weights)
    regathered = gather_blocks(out_master.astype(jnp.bfloat16), owner_of, slot_rank, replica)
    return (
        out_left[None, None],
        out_right[None, None],
        out_moment[None, None],
        out_master[None, None],
        regathered,
    )


def solution(mesh):
    in_specs = (
        P("dp", "shard", None, None),
        P("shard", None),
        P(),
        P("dp", "shard", None, None, None),
        P("dp", "shard", None, None, None),
        P("dp", "shard", None, None, None),
        P("dp", "shard", None, None, None),
        P("dp", "shard", None, None, None),
        P("dp", "shard", None, None, None),
    )
    out_specs = (
        P("dp", "shard", None, None, None),
        P("dp", "shard", None, None, None),
        P("dp", "shard", None, None, None),
        P("dp", "shard", None, None, None),
        P("shard", None, None),
    )
    return jax.shard_map(local, mesh=mesh, in_specs=in_specs, out_specs=out_specs, check_vma=False)
```

```python
import jax
import jax.numpy as jnp
from jax import lax
from jax.experimental import pallas as pl
from jax.experimental.pallas import tpu as pltpu
from jax.sharding import PartitionSpec as P

BETA = 0.95
RATE = 0.3
ADAM_EPS = 1e-08
NORM_EPS = 1e-06


def butterfly_sum(x, axis):
    size = lax.axis_size(axis)
    if size & (size - 1):
        return lax.psum(x, axis)
    step = 1
    while step < size:
        x = x + lax.ppermute(x, axis, [(i, i ^ step) for i in range(size)])
        step *= 2
    return x


def mesh_sum(x):
    rows, cols = lax.axis_size("dp"), lax.axis_size("shard")
    if rows & (rows - 1) or cols & (cols - 1):
        return butterfly_sum(butterfly_sum(x, "dp"), "shard")
    row_masks = [cols * (1 << k) for k in range(rows.bit_length() - 1)][::-1]
    col_masks = [1 << k for k in range(cols.bit_length() - 1)]
    size = rows * cols
    for k in range(max(len(row_masks), len(col_masks))):
        masks = row_masks[k:k + 1] + col_masks[k:k + 1]
        if len(masks) == 2:
            masks.append(masks[0] ^ masks[1])
        total = x
        for mask in masks:
            total = total + lax.ppermute(x, ("dp", "shard"), [(i, i ^ mask) for i in range(size)])
        x = total
    return x


def gather_blocks(mine, owner_of, slot_rank, replica):
    size = lax.axis_size("dp")
    slot_count = mine.shape[0]
    if size % 2 or size < 4:
        gathered = lax.all_gather(mine, "dp", axis=0, tiled=True)
        return jnp.take(gathered, owner_of * slot_count + slot_rank, axis=0)
    chips = size // 2
    rightward = [(i, i + 2) for i in range(size - 2)]
    leftward = [(i + 2, i) for i in range(size - 2)]
    partner = [(i, i ^ 1) for i in range(size)]
    from_left = [None] * chips
    from_right = [None] * chips
    from_left[0] = mine
    from_right[0] = mine
    near_left = [None] * chips
    near_right = [None] * chips
    near_left[0] = lax.ppermute(mine, "dp", partner)
    near_right[0] = near_left[0]
    for step in range(1, chips):
        from_left[step] = lax.ppermute(from_left[step - 1], "dp", rightward)
        from_right[step] = lax.ppermute(from_right[step - 1], "dp", leftward)
        near_left[step] = lax.ppermute(from_left[step], "dp", partner)
        near_right[step] = lax.ppermute(from_right[step], "dp", partner)
    pieces = from_left[::-1] + from_right[1:] + near_left[::-1] + near_right[1:]
    chip, core = replica // 2, replica % 2
    owner_chip, owner_core = owner_of // 2, owner_of % 2
    offset = owner_chip - chip + chips - 1
    which = jnp.where(owner_core == core, 0, 1)
    source = jnp.clip(which * (2 * chips - 1) + offset, 0, len(pieces) - 1)
    table = jnp.stack([source, jnp.clip(slot_rank, 0, slot_count - 1)], axis=1).astype(jnp.int32)
    return pick_blocks(table, pieces)


def pick_kernel(table_ref, *refs):
    pieces, out_ref, sems = refs[:-2], refs[-2], refs[-1]

    def start(block, carry):
        for index, piece in enumerate(pieces):
            @pl.when(table_ref[block, 0] == index)
            def _():
                pltpu.make_async_copy(piece.at[table_ref[block, 1]], out_ref.at[block], sems.at[block]).start()

        return carry

    def finish(block, carry):
        pltpu.make_async_copy(pieces[0].at[0], out_ref.at[block], sems.at[block]).wait()
        return carry

    lax.fori_loop(0, out_ref.shape[0], start, 0)
    lax.fori_loop(0, out_ref.shape[0], finish, 0)


def pick_blocks(table, pieces):
    blocks = table.shape[0]
    return pl.pallas_call(
        pick_kernel,
        out_shape=jax.ShapeDtypeStruct((blocks,) + pieces[0].shape[1:], pieces[0].dtype),
        in_specs=[pl.BlockSpec(memory_space=pltpu.SMEM)] + [pl.BlockSpec(memory_space=pl.ANY)] * len(pieces),
        out_specs=pl.BlockSpec(memory_space=pltpu.VMEM),
        scratch_shapes=[pltpu.SemaphoreType.DMA((blocks,))],
    )(table, *pieces)


def local(
    grad_partials,
    owners,
    weight_blocks,
    stats_left,
    stats_right,
    root_left,
    root_right,
    second_moment,
    master,
):
    replica = lax.axis_index("dp")
    column = lax.axis_index("shard")
    replicas = lax.axis_size("dp")
    local_grads = grad_partials[0]
    column_blocks = local_grads.shape[0]
    slot_count = stats_left.shape[2]
    owner_of = owners[:, 0]
    block_ids = jnp.arange(column_blocks, dtype=jnp.int32)
    earlier = (owner_of[None, :] == owner_of[:, None]) & (block_ids[None, :] < block_ids[:, None])
    slot_rank = jnp.sum(earlier.astype(jnp.int32), axis=1)
    matches = (owner_of[None, None, :] == jnp.arange(replicas, dtype=jnp.int32)[:, None, None]) & (
        slot_rank[None, None, :] == jnp.arange(slot_count, dtype=jnp.int32)[None, :, None]
    )
    slot_table = jnp.sum(
        matches.astype(jnp.int32) * jnp.arange(column_blocks, dtype=jnp.int32)[None, None, :],
        axis=2,
    )
    slot_live = jnp.any(matches, axis=2)
    my_table = lax.dynamic_index_in_dim(slot_table, replica, 0, keepdims=False)
    my_live = lax.dynamic_index_in_dim(slot_live, replica, 0, keepdims=False)
    live_float = my_live.astype(jnp.float32)[:, None, None]
    by_owner = jnp.take(local_grads, slot_table.reshape(-1), axis=0, mode="clip").reshape(
        (replicas, slot_count) + local_grads.shape[1:]
    )
    received = lax.all_to_all(by_owner, "dp", 0, 0, tiled=True)
    owned_grad = jnp.sum(received.astype(jnp.float32), axis=0) * live_float
    left = stats_left[0, 0]
    right = stats_right[0, 0]
    moment = second_moment[0, 0]
    weights = master[0, 0]
    global_block = column * column_blocks + my_table
    ends = jnp.cumsum(weight_blocks)
    weight_id = jnp.sum((global_block[:, None] >= ends[None, :]).astype(jnp.int32), axis=1)
    member = (
        weight_id[:, None] == jnp.arange(weight_blocks.shape[0], dtype=jnp.int32)[None, :]
    ).astype(jnp.float32) * my_live.astype(jnp.float32)[:, None]
    vnew = BETA * moment + (1.0 - BETA) * owned_grad * owned_grad
    adam = owned_grad / (jnp.sqrt(vnew) + ADAM_EPS)
    adam_terms = jnp.sum(member * jnp.sum(adam * adam, axis=(1, 2))[:, None], axis=0)
    highest = lax.Precision.HIGHEST
    lnew = BETA * left + (1.0 - BETA) * jnp.einsum(
        "sij,skj->sik", owned_grad, owned_grad, precision=highest
    )
    rnew = BETA * right + (1.0 - BETA) * jnp.einsum(
        "sji,sjk->sik", owned_grad, owned_grad, precision=highest
    )
    grad_half = owned_grad.astype(jnp.bfloat16)
    inner = jnp.einsum(
        "sij,sjk->sik", root_left[0, 0], grad_half, preferred_element_type=jnp.float32
    ).astype(jnp.bfloat16)
    precond = jnp.einsum(
        "sij,sjk->sik", inner, root_right[0, 0], preferred_element_type=jnp.float32
    )
    prec_terms = jnp.sum(member * jnp.sum(precond * precond, axis=(1, 2))[:, None], axis=0)
    norms = mesh_sum(jnp.stack([adam_terms, prec_terms]))
    norm_adam = norms[0]
    norm_prec = norms[1]
    scales = jnp.sqrt(norm_adam / (norm_prec + NORM_EPS))
    slot_scale = jnp.sum(member * scales[None, :], axis=1)
    wnew = weights - RATE * slot_scale[:, None, None] * precond
    live_mask = my_live[:, None, None]
    out_left = jnp.where(live_mask, lnew, left)
    out_right = jnp.where(live_mask, rnew, right)
    out_moment = jnp.where(live_mask, vnew, moment)
    out_master = jnp.where(live_mask, wnew, weights)
    regathered = gather_blocks(out_master.astype(jnp.bfloat16), owner_of, slot_rank, replica)
    return (
        out_left[None, None],
        out_right[None, None],
        out_moment[None, None],
        out_master[None, None],
        regathered,
    )


def solution(mesh):
    in_specs = (
        P("dp", "shard", None, None),
        P("shard", None),
        P(),
        P("dp", "shard", None, None, None),
        P("dp", "shard", None, None, None),
        P("dp", "shard", None, None, None),
        P("dp", "shard", None, None, None),
        P("dp", "shard", None, None, None),
        P("dp", "shard", None, None, None),
    )
    out_specs = (
        P("dp", "shard", None, None, None),
        P("dp", "shard", None, None, None),
        P("dp", "shard", None, None, None),
        P("dp", "shard", None, None, None),
        P("shard", None, None),
    )
    return jax.shard_map(local, mesh=mesh, in_specs=in_specs, out_specs=out_specs, check_vma=False)
```

```python
import jax
import jax.numpy as jnp
from jax import lax
from jax.experimental import pallas as pl
from jax.experimental.pallas import tpu as pltpu
from jax.sharding import PartitionSpec as P

BETA = 0.95
RATE = 0.3
ADAM_EPS = 1e-08
NORM_EPS = 1e-06


def butterfly_sum(x, axis):
    size = lax.axis_size(axis)
    if size & (size - 1):
        return lax.psum(x, axis)
    step = 1
    while step < size:
        x = x + lax.ppermute(x, axis, [(i, i ^ step) for i in range(size)])
        step *= 2
    return x


def gather_blocks(mine, owner_of, slot_rank, replica):
    size = lax.axis_size("dp")
    slot_count = mine.shape[0]
    if size % 2 or size < 4:
        gathered = lax.all_gather(mine, "dp", axis=0, tiled=True)
        return jnp.take(gathered, owner_of * slot_count + slot_rank, axis=0)
    chips = size // 2
    rightward = [(i, i + 2) for i in range(size - 2)]
    leftward = [(i + 2, i) for i in range(size - 2)]
    partner = [(i, i ^ 1) for i in range(size)]
    from_left = [None] * chips
    from_right = [None] * chips
    from_left[0] = mine
    from_right[0] = mine
    near_left = [None] * chips
    near_right = [None] * chips
    near_left[0] = lax.ppermute(mine, "dp", partner)
    near_right[0] = near_left[0]
    for step in range(1, chips):
        from_left[step] = lax.ppermute(from_left[step - 1], "dp", rightward)
        from_right[step] = lax.ppermute(from_right[step - 1], "dp", leftward)
        near_left[step] = lax.ppermute(from_left[step], "dp", partner)
        near_right[step] = lax.ppermute(from_right[step], "dp", partner)
    pieces = from_left[::-1] + from_right[1:] + near_left[::-1] + near_right[1:]
    chip, core = replica // 2, replica % 2
    owner_chip, owner_core = owner_of // 2, owner_of % 2
    offset = owner_chip - chip + chips - 1
    which = jnp.where(owner_core == core, 0, 1)
    source = jnp.clip(which * (2 * chips - 1) + offset, 0, len(pieces) - 1)
    table = jnp.stack([source, jnp.clip(slot_rank, 0, slot_count - 1)], axis=1).astype(jnp.int32)
    return pick_blocks(table, pieces)


def pick_kernel(table_ref, *refs):
    pieces, out_ref, sems = refs[:-2], refs[-2], refs[-1]

    def start(block, carry):
        for index, piece in enumerate(pieces):
            @pl.when(table_ref[block, 0] == index)
            def _():
                pltpu.make_async_copy(piece.at[table_ref[block, 1]], out_ref.at[block], sems.at[block]).start()

        return carry

    def finish(block, carry):
        pltpu.make_async_copy(pieces[0].at[0], out_ref.at[block], sems.at[block]).wait()
        return carry

    lax.fori_loop(0, out_ref.shape[0], start, 0)
    lax.fori_loop(0, out_ref.shape[0], finish, 0)


def pick_blocks(table, pieces):
    blocks = table.shape[0]
    return pl.pallas_call(
        pick_kernel,
        out_shape=jax.ShapeDtypeStruct((blocks,) + pieces[0].shape[1:], pieces[0].dtype),
        in_specs=[pl.BlockSpec(memory_space=pltpu.SMEM)] + [pl.BlockSpec(memory_space=pl.ANY)] * len(pieces),
        out_specs=pl.BlockSpec(memory_space=pltpu.VMEM),
        scratch_shapes=[pltpu.SemaphoreType.DMA((blocks,))],
    )(table, *pieces)


def local(
    grad_partials,
    owners,
    weight_blocks,
    stats_left,
    stats_right,
    root_left,
    root_right,
    second_moment,
    master,
):
    replica = lax.axis_index("dp")
    column = lax.axis_index("shard")
    replicas = lax.axis_size("dp")
    local_grads = grad_partials[0]
    column_blocks = local_grads.shape[0]
    slot_count = stats_left.shape[2]
    owner_of = owners[:, 0]
    block_ids = jnp.arange(column_blocks, dtype=jnp.int32)
    earlier = (owner_of[None, :] == owner_of[:, None]) & (block_ids[None, :] < block_ids[:, None])
    slot_rank = jnp.sum(earlier.astype(jnp.int32), axis=1)
    matches = (owner_of[None, None, :] == jnp.arange(replicas, dtype=jnp.int32)[:, None, None]) & (
        slot_rank[None, None, :] == jnp.arange(slot_count, dtype=jnp.int32)[None, :, None]
    )
    slot_table = jnp.sum(
        matches.astype(jnp.int32) * jnp.arange(column_blocks, dtype=jnp.int32)[None, None, :],
        axis=2,
    )
    slot_live = jnp.any(matches, axis=2)
    my_table = lax.dynamic_index_in_dim(slot_table, replica, 0, keepdims=False)
    my_live = lax.dynamic_index_in_dim(slot_live, replica, 0, keepdims=False)
    live_float = my_live.astype(jnp.float32)[:, None, None]
    by_owner = jnp.take(local_grads, slot_table.reshape(-1), axis=0, mode="clip").reshape(
        (replicas, slot_count) + local_grads.shape[1:]
    )
    received = lax.all_to_all(by_owner, "dp", 0, 0, tiled=True)
    owned_grad = jnp.sum(received.astype(jnp.float32), axis=0) * live_float
    left = stats_left[0, 0]
    right = stats_right[0, 0]
    moment = second_moment[0, 0]
    weights = master[0, 0]
    global_block = column * column_blocks + my_table
    ends = jnp.cumsum(weight_blocks)
    weight_id = jnp.sum((global_block[:, None] >= ends[None, :]).astype(jnp.int32), axis=1)
    member = (
        weight_id[:, None] == jnp.arange(weight_blocks.shape[0], dtype=jnp.int32)[None, :]
    ).astype(jnp.float32) * my_live.astype(jnp.float32)[:, None]
    vnew = BETA * moment + (1.0 - BETA) * owned_grad * owned_grad
    adam = owned_grad / (jnp.sqrt(vnew) + ADAM_EPS)
    adam_terms = jnp.sum(member * jnp.sum(adam * adam, axis=(1, 2))[:, None], axis=0)
    highest = lax.Precision.HIGHEST
    lnew = BETA * left + (1.0 - BETA) * jnp.einsum(
        "sij,skj->sik", owned_grad, owned_grad, precision=highest
    )
    rnew = BETA * right + (1.0 - BETA) * jnp.einsum(
        "sji,sjk->sik", owned_grad, owned_grad, precision=highest
    )
    grad_half = owned_grad.astype(jnp.bfloat16)
    inner = jnp.einsum(
        "sij,sjk->sik", root_left[0, 0], grad_half, preferred_element_type=jnp.float32
    ).astype(jnp.bfloat16)
    precond = jnp.einsum(
        "sij,sjk->sik", inner, root_right[0, 0], preferred_element_type=jnp.float32
    )
    prec_terms = jnp.sum(member * jnp.sum(precond * precond, axis=(1, 2))[:, None], axis=0)
    partial_norms = butterfly_sum(jnp.stack([adam_terms, prec_terms]), "dp")
    partial_norms, lnew, rnew = lax.optimization_barrier((partial_norms, lnew, rnew))
    norms = butterfly_sum(partial_norms, "shard")
    norm_adam = norms[0]
    norm_prec = norms[1]
    scales = jnp.sqrt(norm_adam / (norm_prec + NORM_EPS))
    slot_scale = jnp.sum(member * scales[None, :], axis=1)
    wnew = weights - RATE * slot_scale[:, None, None] * precond
    live_mask = my_live[:, None, None]
    out_left = jnp.where(live_mask, lnew, left)
    out_right = jnp.where(live_mask, rnew, right)
    out_moment = jnp.where(live_mask, vnew, moment)
    out_master = jnp.where(live_mask, wnew, weights)
    regathered = gather_blocks(out_master.astype(jnp.bfloat16), owner_of, slot_rank, replica)
    return (
        out_left[None, None],
        out_right[None, None],
        out_moment[None, None],
        out_master[None, None],
        regathered,
    )


def solution(mesh):
    in_specs = (
        P("dp", "shard", None, None),
        P("shard", None),
        P(),
        P("dp", "shard", None, None, None),
        P("dp", "shard", None, None, None),
        P("dp", "shard", None, None, None),
        P("dp", "shard", None, None, None),
        P("dp", "shard", None, None, None),
        P("dp", "shard", None, None, None),
    )
    out_specs = (
        P("dp", "shard", None, None, None),
        P("dp", "shard", None, None, None),
        P("dp", "shard", None, None, None),
        P("dp", "shard", None, None, None),
        P("shard", None, None),
    )
    return jax.shard_map(local, mesh=mesh, in_specs=in_specs, out_specs=out_specs, check_vma=False)
```

```python
import jax
import jax.numpy as jnp
from jax import lax
from jax.experimental import pallas as pl
from jax.experimental.pallas import tpu as pltpu
from jax.sharding import PartitionSpec as P

BETA = 0.95
RATE = 0.3
ADAM_EPS = 1e-08
NORM_EPS = 1e-06


def butterfly_sum(x, axis):
    size = lax.axis_size(axis)
    if size & (size - 1):
        return lax.psum(x, axis)
    step = 1
    while step < size:
        x = x + lax.ppermute(x, axis, [(i, i ^ step) for i in range(size)])
        step *= 2
    return x


def gather_blocks(mine, owner_of, slot_rank, replica):
    size = lax.axis_size("dp")
    slot_count = mine.shape[0]
    if size % 2 or size < 4:
        gathered = lax.all_gather(mine, "dp", axis=0, tiled=True)
        return jnp.take(gathered, owner_of * slot_count + slot_rank, axis=0)
    chips = size // 2
    rightward = [(i, i + 2) for i in range(size - 2)]
    leftward = [(i + 2, i) for i in range(size - 2)]
    partner = [(i, i ^ 1) for i in range(size)]
    from_left = [None] * chips
    from_right = [None] * chips
    from_left[0] = mine
    from_right[0] = mine
    for step in range(1, chips):
        from_left[step] = lax.ppermute(from_left[step - 1], "dp", rightward)
        from_right[step] = lax.ppermute(from_right[step - 1], "dp", leftward)
    near_left = [None] * chips
    near_right = [None] * chips
    for step in range(chips):
        later = min(step + 1, chips - 1)
        left, right, _, _ = lax.optimization_barrier(
            (from_left[step], from_right[step], from_left[later], from_right[later])
        )
        near_left[step] = lax.ppermute(left, "dp", partner)
        near_right[step] = lax.ppermute(right, "dp", partner) if step else near_left[0]
    pieces = from_left[::-1] + from_right[1:] + near_left[::-1] + near_right[1:]
    chip, core = replica // 2, replica % 2
    owner_chip, owner_core = owner_of // 2, owner_of % 2
    offset = owner_chip - chip + chips - 1
    which = jnp.where(owner_core == core, 0, 1)
    source = jnp.clip(which * (2 * chips - 1) + offset, 0, len(pieces) - 1)
    table = jnp.stack([source, jnp.clip(slot_rank, 0, slot_count - 1)], axis=1).astype(jnp.int32)
    return pick_blocks(table, pieces)


def pick_kernel(table_ref, *refs):
    pieces, out_ref, sems = refs[:-2], refs[-2], refs[-1]

    def start(block, carry):
        for index, piece in enumerate(pieces):
            @pl.when(table_ref[block, 0] == index)
            def _():
                pltpu.make_async_copy(piece.at[table_ref[block, 1]], out_ref.at[block], sems.at[block]).start()

        return carry

    def finish(block, carry):
        pltpu.make_async_copy(pieces[0].at[0], out_ref.at[block], sems.at[block]).wait()
        return carry

    lax.fori_loop(0, out_ref.shape[0], start, 0)
    lax.fori_loop(0, out_ref.shape[0], finish, 0)


def pick_blocks(table, pieces):
    blocks = table.shape[0]
    return pl.pallas_call(
        pick_kernel,
        out_shape=jax.ShapeDtypeStruct((blocks,) + pieces[0].shape[1:], pieces[0].dtype),
        in_specs=[pl.BlockSpec(memory_space=pltpu.SMEM)] + [pl.BlockSpec(memory_space=pl.ANY)] * len(pieces),
        out_specs=pl.BlockSpec(memory_space=pltpu.VMEM),
        scratch_shapes=[pltpu.SemaphoreType.DMA((blocks,))],
    )(table, *pieces)


def local(
    grad_partials,
    owners,
    weight_blocks,
    stats_left,
    stats_right,
    root_left,
    root_right,
    second_moment,
    master,
):
    replica = lax.axis_index("dp")
    column = lax.axis_index("shard")
    replicas = lax.axis_size("dp")
    local_grads = grad_partials[0]
    column_blocks = local_grads.shape[0]
    slot_count = stats_left.shape[2]
    owner_of = owners[:, 0]
    block_ids = jnp.arange(column_blocks, dtype=jnp.int32)
    earlier = (owner_of[None, :] == owner_of[:, None]) & (block_ids[None, :] < block_ids[:, None])
    slot_rank = jnp.sum(earlier.astype(jnp.int32), axis=1)
    matches = (owner_of[None, None, :] == jnp.arange(replicas, dtype=jnp.int32)[:, None, None]) & (
        slot_rank[None, None, :] == jnp.arange(slot_count, dtype=jnp.int32)[None, :, None]
    )
    slot_table = jnp.sum(
        matches.astype(jnp.int32) * jnp.arange(column_blocks, dtype=jnp.int32)[None, None, :],
        axis=2,
    )
    slot_live = jnp.any(matches, axis=2)
    my_table = lax.dynamic_index_in_dim(slot_table, replica, 0, keepdims=False)
    my_live = lax.dynamic_index_in_dim(slot_live, replica, 0, keepdims=False)
    live_float = my_live.astype(jnp.float32)[:, None, None]
    by_owner = jnp.take(local_grads, slot_table.reshape(-1), axis=0, mode="clip").reshape(
        (replicas, slot_count) + local_grads.shape[1:]
    )
    received = lax.all_to_all(by_owner, "dp", 0, 0, tiled=True)
    owned_grad = jnp.sum(received.astype(jnp.float32), axis=0) * live_float
    left = stats_left[0, 0]
    right = stats_right[0, 0]
    moment = second_moment[0, 0]
    weights = master[0, 0]
    global_block = column * column_blocks + my_table
    ends = jnp.cumsum(weight_blocks)
    weight_id = jnp.sum((global_block[:, None] >= ends[None, :]).astype(jnp.int32), axis=1)
    member = (
        weight_id[:, None] == jnp.arange(weight_blocks.shape[0], dtype=jnp.int32)[None, :]
    ).astype(jnp.float32) * my_live.astype(jnp.float32)[:, None]
    vnew = BETA * moment + (1.0 - BETA) * owned_grad * owned_grad
    adam = owned_grad / (jnp.sqrt(vnew) + ADAM_EPS)
    adam_terms = jnp.sum(member * jnp.sum(adam * adam, axis=(1, 2))[:, None], axis=0)
    highest = lax.Precision.HIGHEST
    lnew = BETA * left + (1.0 - BETA) * jnp.einsum(
        "sij,skj->sik", owned_grad, owned_grad, precision=highest
    )
    rnew = BETA * right + (1.0 - BETA) * jnp.einsum(
        "sji,sjk->sik", owned_grad, owned_grad, precision=highest
    )
    grad_half = owned_grad.astype(jnp.bfloat16)
    inner = jnp.einsum(
        "sij,sjk->sik", root_left[0, 0], grad_half, preferred_element_type=jnp.float32
    ).astype(jnp.bfloat16)
    precond = jnp.einsum(
        "sij,sjk->sik", inner, root_right[0, 0], preferred_element_type=jnp.float32
    )
    prec_terms = jnp.sum(member * jnp.sum(precond * precond, axis=(1, 2))[:, None], axis=0)
    norms = butterfly_sum(butterfly_sum(jnp.stack([adam_terms, prec_terms]), "dp"), "shard")
    norm_adam = norms[0]
    norm_prec = norms[1]
    scales = jnp.sqrt(norm_adam / (norm_prec + NORM_EPS))
    slot_scale = jnp.sum(member * scales[None, :], axis=1)
    wnew = weights - RATE * slot_scale[:, None, None] * precond
    live_mask = my_live[:, None, None]
    out_left = jnp.where(live_mask, lnew, left)
    out_right = jnp.where(live_mask, rnew, right)
    out_moment = jnp.where(live_mask, vnew, moment)
    out_master = jnp.where(live_mask, wnew, weights)
    regathered = gather_blocks(out_master.astype(jnp.bfloat16), owner_of, slot_rank, replica)
    return (
        out_left[None, None],
        out_right[None, None],
        out_moment[None, None],
        out_master[None, None],
        regathered,
    )


def solution(mesh):
    in_specs = (
        P("dp", "shard", None, None),
        P("shard", None),
        P(),
        P("dp", "shard", None, None, None),
        P("dp", "shard", None, None, None),
        P("dp", "shard", None, None, None),
        P("dp", "shard", None, None, None),
        P("dp", "shard", None, None, None),
        P("dp", "shard", None, None, None),
    )
    out_specs = (
        P("dp", "shard", None, None, None),
        P("dp", "shard", None, None, None),
        P("dp", "shard", None, None, None),
        P("dp", "shard", None, None, None),
        P("shard", None, None),
    )
    return jax.shard_map(local, mesh=mesh, in_specs=in_specs, out_specs=out_specs, check_vma=False)
```

```python
import jax
import jax.numpy as jnp
from jax import lax
from jax.experimental import pallas as pl
from jax.experimental.pallas import tpu as pltpu
from jax.sharding import PartitionSpec as P

BETA = 0.95
RATE = 0.3
ADAM_EPS = 1e-08
NORM_EPS = 1e-06


def butterfly_sum(x, axis):
    size = lax.axis_size(axis)
    if size & (size - 1):
        return lax.psum(x, axis)
    step = 1
    while step < size:
        x = x + lax.ppermute(x, axis, [(i, i ^ step) for i in range(size)])
        step *= 2
    return x


def gather_blocks(mine, owner_of, slot_rank, replica):
    size = lax.axis_size("dp")
    slot_count = mine.shape[0]
    if size % 2 or size < 4:
        gathered = lax.all_gather(mine, "dp", axis=0, tiled=True)
        return jnp.take(gathered, owner_of * slot_count + slot_rank, axis=0)
    chips = size // 2
    partner = [(i, i ^ 1) for i in range(size)]
    line = [(i, i + 2 - 4 * (i % 2)) for i in range(size) if 0 <= i + 2 - 4 * (i % 2) < size]
    chain = [jnp.concatenate([mine, lax.ppermute(mine, "dp", partner)])]
    for step in range(1, chips):
        chain.append(lax.ppermute(chain[-1], "dp", line))
    beside = [lax.ppermute(piece, "dp", partner) for piece in chain[1:]]
    pieces = chain + beside
    chip, core = replica // 2, replica % 2
    owner_chip, owner_core = owner_of // 2, owner_of % 2
    ahead = owner_chip - chip
    own_line = (ahead == 0) | ((core == 0) & (ahead < 0)) | ((core == 1) & (ahead > 0))
    step = jnp.abs(ahead)
    source = jnp.clip(jnp.where(own_line, step, chips - 1 + step), 0, len(pieces) - 1)
    sender = jnp.where(own_line, core, 1 - core)
    place = jnp.where(owner_core == sender, 0, slot_count) + slot_rank
    table = jnp.stack([source, jnp.clip(place, 0, 2 * slot_count - 1)], axis=1).astype(jnp.int32)
    return pick_blocks(table, pieces)


def pick_kernel(table_ref, *refs):
    pieces, out_ref, sems = refs[:-2], refs[-2], refs[-1]

    def start(block, carry):
        for index, piece in enumerate(pieces):
            @pl.when(table_ref[block, 0] == index)
            def _():
                pltpu.make_async_copy(piece.at[table_ref[block, 1]], out_ref.at[block], sems.at[block]).start()

        return carry

    def finish(block, carry):
        pltpu.make_async_copy(pieces[0].at[0], out_ref.at[block], sems.at[block]).wait()
        return carry

    lax.fori_loop(0, out_ref.shape[0], start, 0)
    lax.fori_loop(0, out_ref.shape[0], finish, 0)


def pick_blocks(table, pieces):
    blocks = table.shape[0]
    return pl.pallas_call(
        pick_kernel,
        out_shape=jax.ShapeDtypeStruct((blocks,) + pieces[0].shape[1:], pieces[0].dtype),
        in_specs=[pl.BlockSpec(memory_space=pltpu.SMEM)] + [pl.BlockSpec(memory_space=pl.ANY)] * len(pieces),
        out_specs=pl.BlockSpec(memory_space=pltpu.VMEM),
        scratch_shapes=[pltpu.SemaphoreType.DMA((blocks,))],
    )(table, *pieces)


def local(
    grad_partials,
    owners,
    weight_blocks,
    stats_left,
    stats_right,
    root_left,
    root_right,
    second_moment,
    master,
):
    replica = lax.axis_index("dp")
    column = lax.axis_index("shard")
    replicas = lax.axis_size("dp")
    local_grads = grad_partials[0]
    column_blocks = local_grads.shape[0]
    slot_count = stats_left.shape[2]
    owner_of = owners[:, 0]
    block_ids = jnp.arange(column_blocks, dtype=jnp.int32)
    earlier = (owner_of[None, :] == owner_of[:, None]) & (block_ids[None, :] < block_ids[:, None])
    slot_rank = jnp.sum(earlier.astype(jnp.int32), axis=1)
    matches = (owner_of[None, None, :] == jnp.arange(replicas, dtype=jnp.int32)[:, None, None]) & (
        slot_rank[None, None, :] == jnp.arange(slot_count, dtype=jnp.int32)[None, :, None]
    )
    slot_table = jnp.sum(
        matches.astype(jnp.int32) * jnp.arange(column_blocks, dtype=jnp.int32)[None, None, :],
        axis=2,
    )
    slot_live = jnp.any(matches, axis=2)
    my_table = lax.dynamic_index_in_dim(slot_table, replica, 0, keepdims=False)
    my_live = lax.dynamic_index_in_dim(slot_live, replica, 0, keepdims=False)
    live_float = my_live.astype(jnp.float32)[:, None, None]
    by_owner = jnp.take(local_grads, slot_table.reshape(-1), axis=0, mode="clip").reshape(
        (replicas, slot_count) + local_grads.shape[1:]
    )
    received = lax.all_to_all(by_owner, "dp", 0, 0, tiled=True)
    owned_grad = jnp.sum(received.astype(jnp.float32), axis=0) * live_float
    left = stats_left[0, 0]
    right = stats_right[0, 0]
    moment = second_moment[0, 0]
    weights = master[0, 0]
    global_block = column * column_blocks + my_table
    ends = jnp.cumsum(weight_blocks)
    weight_id = jnp.sum((global_block[:, None] >= ends[None, :]).astype(jnp.int32), axis=1)
    member = (
        weight_id[:, None] == jnp.arange(weight_blocks.shape[0], dtype=jnp.int32)[None, :]
    ).astype(jnp.float32) * my_live.astype(jnp.float32)[:, None]
    vnew = BETA * moment + (1.0 - BETA) * owned_grad * owned_grad
    adam = owned_grad / (jnp.sqrt(vnew) + ADAM_EPS)
    adam_terms = jnp.sum(member * jnp.sum(adam * adam, axis=(1, 2))[:, None], axis=0)
    highest = lax.Precision.HIGHEST
    lnew = BETA * left + (1.0 - BETA) * jnp.einsum(
        "sij,skj->sik", owned_grad, owned_grad, precision=highest
    )
    rnew = BETA * right + (1.0 - BETA) * jnp.einsum(
        "sji,sjk->sik", owned_grad, owned_grad, precision=highest
    )
    grad_half = owned_grad.astype(jnp.bfloat16)
    inner = jnp.einsum(
        "sij,sjk->sik", root_left[0, 0], grad_half, preferred_element_type=jnp.float32
    ).astype(jnp.bfloat16)
    precond = jnp.einsum(
        "sij,sjk->sik", inner, root_right[0, 0], preferred_element_type=jnp.float32
    )
    prec_terms = jnp.sum(member * jnp.sum(precond * precond, axis=(1, 2))[:, None], axis=0)
    norms = butterfly_sum(butterfly_sum(jnp.stack([adam_terms, prec_terms]), "dp"), "shard")
    norm_adam = norms[0]
    norm_prec = norms[1]
    scales = jnp.sqrt(norm_adam / (norm_prec + NORM_EPS))
    slot_scale = jnp.sum(member * scales[None, :], axis=1)
    wnew = weights - RATE * slot_scale[:, None, None] * precond
    live_mask = my_live[:, None, None]
    out_left = jnp.where(live_mask, lnew, left)
    out_right = jnp.where(live_mask, rnew, right)
    out_moment = jnp.where(live_mask, vnew, moment)
    out_master = jnp.where(live_mask, wnew, weights)
    regathered = gather_blocks(out_master.astype(jnp.bfloat16), owner_of, slot_rank, replica)
    return (
        out_left[None, None],
        out_right[None, None],
        out_moment[None, None],
        out_master[None, None],
        regathered,
    )


def solution(mesh):
    in_specs = (
        P("dp", "shard", None, None),
        P("shard", None),
        P(),
        P("dp", "shard", None, None, None),
        P("dp", "shard", None, None, None),
        P("dp", "shard", None, None, None),
        P("dp", "shard", None, None, None),
        P("dp", "shard", None, None, None),
        P("dp", "shard", None, None, None),
    )
    out_specs = (
        P("dp", "shard", None, None, None),
        P("dp", "shard", None, None, None),
        P("dp", "shard", None, None, None),
        P("dp", "shard", None, None, None),
        P("shard", None, None),
    )
    return jax.shard_map(local, mesh=mesh, in_specs=in_specs, out_specs=out_specs, check_vma=False)
```

```python
import jax
import jax.numpy as jnp
from jax import lax
from jax.experimental import pallas as pl
from jax.experimental.pallas import tpu as pltpu
from jax.sharding import PartitionSpec as P

BETA = 0.95
RATE = 0.3
ADAM_EPS = 1e-08
NORM_EPS = 1e-06


def butterfly_sum(x, axis):
    size = lax.axis_size(axis)
    if size & (size - 1):
        return lax.psum(x, axis)
    step = 1
    while step < size:
        x = x + lax.ppermute(x, axis, [(i, i ^ step) for i in range(size)])
        step *= 2
    return x


def gather_blocks(mine, owner_of, slot_rank, replica):
    size = lax.axis_size("dp")
    slot_count = mine.shape[0]
    if size % 2 or size < 4:
        gathered = lax.all_gather(mine, "dp", axis=0, tiled=True)
        return jnp.take(gathered, owner_of * slot_count + slot_rank, axis=0)
    if slot_count > 1:
        parts = [gather_blocks(mine[slot:slot + 1], owner_of, jnp.zeros_like(slot_rank), replica) for slot in range(slot_count)]
        picked = parts[0]
        for slot in range(1, slot_count):
            picked = jnp.where((slot_rank == slot)[:, None, None], parts[slot], picked)
        return picked
    chips = size // 2
    rightward = [(i, i + 2) for i in range(size - 2)]
    leftward = [(i + 2, i) for i in range(size - 2)]
    partner = [(i, i ^ 1) for i in range(size)]
    from_left = [None] * chips
    from_right = [None] * chips
    from_left[0] = mine
    from_right[0] = mine
    near_left = [None] * chips
    near_right = [None] * chips
    near_left[0] = lax.ppermute(mine, "dp", partner)
    near_right[0] = near_left[0]
    for step in range(1, chips):
        from_left[step] = lax.ppermute(from_left[step - 1], "dp", rightward)
        from_right[step] = lax.ppermute(from_right[step - 1], "dp", leftward)
        near_left[step] = lax.ppermute(from_left[step], "dp", partner)
        near_right[step] = lax.ppermute(from_right[step], "dp", partner)
    pieces = from_left[::-1] + from_right[1:] + near_left[::-1] + near_right[1:]
    chip, core = replica // 2, replica % 2
    owner_chip, owner_core = owner_of // 2, owner_of % 2
    offset = owner_chip - chip + chips - 1
    which = jnp.where(owner_core == core, 0, 1)
    source = jnp.clip(which * (2 * chips - 1) + offset, 0, len(pieces) - 1)
    table = jnp.stack([source, jnp.clip(slot_rank, 0, slot_count - 1)], axis=1).astype(jnp.int32)
    return pick_blocks(table, pieces)


def pick_kernel(table_ref, *refs):
    pieces, out_ref, sems = refs[:-2], refs[-2], refs[-1]

    def start(block, carry):
        for index, piece in enumerate(pieces):
            @pl.when(table_ref[block, 0] == index)
            def _():
                pltpu.make_async_copy(piece.at[table_ref[block, 1]], out_ref.at[block], sems.at[block]).start()

        return carry

    def finish(block, carry):
        pltpu.make_async_copy(pieces[0].at[0], out_ref.at[block], sems.at[block]).wait()
        return carry

    lax.fori_loop(0, out_ref.shape[0], start, 0)
    lax.fori_loop(0, out_ref.shape[0], finish, 0)


def pick_blocks(table, pieces):
    blocks = table.shape[0]
    return pl.pallas_call(
        pick_kernel,
        out_shape=jax.ShapeDtypeStruct((blocks,) + pieces[0].shape[1:], pieces[0].dtype),
        in_specs=[pl.BlockSpec(memory_space=pltpu.SMEM)] + [pl.BlockSpec(memory_space=pl.ANY)] * len(pieces),
        out_specs=pl.BlockSpec(memory_space=pltpu.VMEM),
        scratch_shapes=[pltpu.SemaphoreType.DMA((blocks,))],
    )(table, *pieces)


def local(
    grad_partials,
    owners,
    weight_blocks,
    stats_left,
    stats_right,
    root_left,
    root_right,
    second_moment,
    master,
):
    replica = lax.axis_index("dp")
    column = lax.axis_index("shard")
    replicas = lax.axis_size("dp")
    local_grads = grad_partials[0]
    column_blocks = local_grads.shape[0]
    slot_count = stats_left.shape[2]
    owner_of = owners[:, 0]
    block_ids = jnp.arange(column_blocks, dtype=jnp.int32)
    earlier = (owner_of[None, :] == owner_of[:, None]) & (block_ids[None, :] < block_ids[:, None])
    slot_rank = jnp.sum(earlier.astype(jnp.int32), axis=1)
    matches = (owner_of[None, None, :] == jnp.arange(replicas, dtype=jnp.int32)[:, None, None]) & (
        slot_rank[None, None, :] == jnp.arange(slot_count, dtype=jnp.int32)[None, :, None]
    )
    slot_table = jnp.sum(
        matches.astype(jnp.int32) * jnp.arange(column_blocks, dtype=jnp.int32)[None, None, :],
        axis=2,
    )
    slot_live = jnp.any(matches, axis=2)
    my_table = lax.dynamic_index_in_dim(slot_table, replica, 0, keepdims=False)
    my_live = lax.dynamic_index_in_dim(slot_live, replica, 0, keepdims=False)
    live_float = my_live.astype(jnp.float32)[:, None, None]
    by_owner = jnp.take(local_grads, slot_table.reshape(-1), axis=0, mode="clip").reshape(
        (replicas, slot_count) + local_grads.shape[1:]
    )
    received = lax.all_to_all(by_owner, "dp", 0, 0, tiled=True)
    owned_grad = jnp.sum(received.astype(jnp.float32), axis=0) * live_float
    left = stats_left[0, 0]
    right = stats_right[0, 0]
    moment = second_moment[0, 0]
    weights = master[0, 0]
    global_block = column * column_blocks + my_table
    ends = jnp.cumsum(weight_blocks)
    weight_id = jnp.sum((global_block[:, None] >= ends[None, :]).astype(jnp.int32), axis=1)
    member = (
        weight_id[:, None] == jnp.arange(weight_blocks.shape[0], dtype=jnp.int32)[None, :]
    ).astype(jnp.float32) * my_live.astype(jnp.float32)[:, None]
    vnew = BETA * moment + (1.0 - BETA) * owned_grad * owned_grad
    adam = owned_grad / (jnp.sqrt(vnew) + ADAM_EPS)
    adam_terms = jnp.sum(member * jnp.sum(adam * adam, axis=(1, 2))[:, None], axis=0)
    highest = lax.Precision.HIGHEST
    lnew = BETA * left + (1.0 - BETA) * jnp.einsum(
        "sij,skj->sik", owned_grad, owned_grad, precision=highest
    )
    rnew = BETA * right + (1.0 - BETA) * jnp.einsum(
        "sji,sjk->sik", owned_grad, owned_grad, precision=highest
    )
    grad_half = owned_grad.astype(jnp.bfloat16)
    inner = jnp.einsum(
        "sij,sjk->sik", root_left[0, 0], grad_half, preferred_element_type=jnp.float32
    ).astype(jnp.bfloat16)
    precond = jnp.einsum(
        "sij,sjk->sik", inner, root_right[0, 0], preferred_element_type=jnp.float32
    )
    prec_terms = jnp.sum(member * jnp.sum(precond * precond, axis=(1, 2))[:, None], axis=0)
    norms = butterfly_sum(butterfly_sum(jnp.stack([adam_terms, prec_terms]), "dp"), "shard")
    norm_adam = norms[0]
    norm_prec = norms[1]
    scales = jnp.sqrt(norm_adam / (norm_prec + NORM_EPS))
    slot_scale = jnp.sum(member * scales[None, :], axis=1)
    wnew = weights - RATE * slot_scale[:, None, None] * precond
    live_mask = my_live[:, None, None]
    out_left = jnp.where(live_mask, lnew, left)
    out_right = jnp.where(live_mask, rnew, right)
    out_moment = jnp.where(live_mask, vnew, moment)
    out_master = jnp.where(live_mask, wnew, weights)
    regathered = gather_blocks(out_master.astype(jnp.bfloat16), owner_of, slot_rank, replica)
    return (
        out_left[None, None],
        out_right[None, None],
        out_moment[None, None],
        out_master[None, None],
        regathered,
    )


def solution(mesh):
    in_specs = (
        P("dp", "shard", None, None),
        P("shard", None),
        P(),
        P("dp", "shard", None, None, None),
        P("dp", "shard", None, None, None),
        P("dp", "shard", None, None, None),
        P("dp", "shard", None, None, None),
        P("dp", "shard", None, None, None),
        P("dp", "shard", None, None, None),
    )
    out_specs = (
        P("dp", "shard", None, None, None),
        P("dp", "shard", None, None, None),
        P("dp", "shard", None, None, None),
        P("dp", "shard", None, None, None),
        P("shard", None, None),
    )
    return jax.shard_map(local, mesh=mesh, in_specs=in_specs, out_specs=out_specs, check_vma=False)
```

```python
import jax
import jax.numpy as jnp
from jax import lax
from jax.experimental import pallas as pl
from jax.experimental.pallas import tpu as pltpu
from jax.sharding import PartitionSpec as P

BETA = 0.95
RATE = 0.3
ADAM_EPS = 1e-08
NORM_EPS = 1e-06


def butterfly_sum(x, axis):
    size = lax.axis_size(axis)
    if size & (size - 1):
        return lax.psum(x, axis)
    step = 1
    while step < size:
        x = x + lax.ppermute(x, axis, [(i, i ^ step) for i in range(size)])
        step *= 2
    return x


def gather_blocks(mine, owner_of, slot_rank, replica):
    size = lax.axis_size("dp")
    slot_count = mine.shape[0]
    if size % 2 or size < 4:
        gathered = lax.all_gather(mine, "dp", axis=0, tiled=True)
        return jnp.take(gathered, owner_of * slot_count + slot_rank, axis=0)
    chips = size // 2
    rightward = [(i, i + 2) for i in range(size - 2)]
    leftward = [(i + 2, i) for i in range(size - 2)]
    partner = [(i, i ^ 1) for i in range(size)]
    from_left = [None] * chips
    from_right = [None] * chips
    from_left[0] = mine
    from_right[0] = mine
    beside = [lax.ppermute(mine, "dp", partner)]
    for step in range(1, chips):
        from_left[step] = lax.ppermute(from_left[step - 1], "dp", rightward)
        from_right[step] = lax.ppermute(from_right[step - 1], "dp", leftward)
        both = jnp.concatenate([from_left[step], from_right[step]])
        beside.append(lax.ppermute(both, "dp", partner))
    pieces = from_left[::-1] + from_right[1:] + beside
    chip, core = replica // 2, replica % 2
    owner_chip, owner_core = owner_of // 2, owner_of % 2
    ahead = owner_chip - chip
    rank = jnp.clip(slot_rank, 0, slot_count - 1)
    same = owner_core == core
    source = jnp.where(same, ahead + chips - 1, 2 * chips - 1 + jnp.abs(ahead))
    place = jnp.where(same | (ahead <= 0), rank, slot_count + rank)
    source = jnp.clip(source, 0, len(pieces) - 1)
    table = jnp.stack([source, place], axis=1).astype(jnp.int32)
    return pick_blocks(table, pieces)


def pick_kernel(table_ref, *refs):
    pieces, out_ref, sems = refs[:-2], refs[-2], refs[-1]

    def start(block, carry):
        for index, piece in enumerate(pieces):
            @pl.when(table_ref[block, 0] == index)
            def _():
                pltpu.make_async_copy(piece.at[table_ref[block, 1]], out_ref.at[block], sems.at[block]).start()

        return carry

    def finish(block, carry):
        pltpu.make_async_copy(pieces[0].at[0], out_ref.at[block], sems.at[block]).wait()
        return carry

    lax.fori_loop(0, out_ref.shape[0], start, 0)
    lax.fori_loop(0, out_ref.shape[0], finish, 0)


def pick_blocks(table, pieces):
    blocks = table.shape[0]
    return pl.pallas_call(
        pick_kernel,
        out_shape=jax.ShapeDtypeStruct((blocks,) + pieces[0].shape[1:], pieces[0].dtype),
        in_specs=[pl.BlockSpec(memory_space=pltpu.SMEM)] + [pl.BlockSpec(memory_space=pl.ANY)] * len(pieces),
        out_specs=pl.BlockSpec(memory_space=pltpu.VMEM),
        scratch_shapes=[pltpu.SemaphoreType.DMA((blocks,))],
    )(table, *pieces)


def local(
    grad_partials,
    owners,
    weight_blocks,
    stats_left,
    stats_right,
    root_left,
    root_right,
    second_moment,
    master,
):
    replica = lax.axis_index("dp")
    column = lax.axis_index("shard")
    replicas = lax.axis_size("dp")
    local_grads = grad_partials[0]
    column_blocks = local_grads.shape[0]
    slot_count = stats_left.shape[2]
    owner_of = owners[:, 0]
    block_ids = jnp.arange(column_blocks, dtype=jnp.int32)
    earlier = (owner_of[None, :] == owner_of[:, None]) & (block_ids[None, :] < block_ids[:, None])
    slot_rank = jnp.sum(earlier.astype(jnp.int32), axis=1)
    matches = (owner_of[None, None, :] == jnp.arange(replicas, dtype=jnp.int32)[:, None, None]) & (
        slot_rank[None, None, :] == jnp.arange(slot_count, dtype=jnp.int32)[None, :, None]
    )
    slot_table = jnp.sum(
        matches.astype(jnp.int32) * jnp.arange(column_blocks, dtype=jnp.int32)[None, None, :],
        axis=2,
    )
    slot_live = jnp.any(matches, axis=2)
    my_table = lax.dynamic_index_in_dim(slot_table, replica, 0, keepdims=False)
    my_live = lax.dynamic_index_in_dim(slot_live, replica, 0, keepdims=False)
    live_float = my_live.astype(jnp.float32)[:, None, None]
    by_owner = jnp.take(local_grads, slot_table.reshape(-1), axis=0, mode="clip").reshape(
        (replicas, slot_count) + local_grads.shape[1:]
    )
    received = lax.all_to_all(by_owner, "dp", 0, 0, tiled=True)
    owned_grad = jnp.sum(received.astype(jnp.float32), axis=0) * live_float
    left = stats_left[0, 0]
    right = stats_right[0, 0]
    moment = second_moment[0, 0]
    weights = master[0, 0]
    global_block = column * column_blocks + my_table
    ends = jnp.cumsum(weight_blocks)
    weight_id = jnp.sum((global_block[:, None] >= ends[None, :]).astype(jnp.int32), axis=1)
    member = (
        weight_id[:, None] == jnp.arange(weight_blocks.shape[0], dtype=jnp.int32)[None, :]
    ).astype(jnp.float32) * my_live.astype(jnp.float32)[:, None]
    vnew = BETA * moment + (1.0 - BETA) * owned_grad * owned_grad
    adam = owned_grad / (jnp.sqrt(vnew) + ADAM_EPS)
    adam_terms = jnp.sum(member * jnp.sum(adam * adam, axis=(1, 2))[:, None], axis=0)
    highest = lax.Precision.HIGHEST
    lnew = BETA * left + (1.0 - BETA) * jnp.einsum(
        "sij,skj->sik", owned_grad, owned_grad, precision=highest
    )
    rnew = BETA * right + (1.0 - BETA) * jnp.einsum(
        "sji,sjk->sik", owned_grad, owned_grad, precision=highest
    )
    grad_half = owned_grad.astype(jnp.bfloat16)
    inner = jnp.einsum(
        "sij,sjk->sik", root_left[0, 0], grad_half, preferred_element_type=jnp.float32
    ).astype(jnp.bfloat16)
    precond = jnp.einsum(
        "sij,sjk->sik", inner, root_right[0, 0], preferred_element_type=jnp.float32
    )
    prec_terms = jnp.sum(member * jnp.sum(precond * precond, axis=(1, 2))[:, None], axis=0)
    norms = butterfly_sum(butterfly_sum(jnp.stack([adam_terms, prec_terms]), "dp"), "shard")
    norm_adam = norms[0]
    norm_prec = norms[1]
    scales = jnp.sqrt(norm_adam / (norm_prec + NORM_EPS))
    slot_scale = jnp.sum(member * scales[None, :], axis=1)
    wnew = weights - RATE * slot_scale[:, None, None] * precond
    live_mask = my_live[:, None, None]
    out_left = jnp.where(live_mask, lnew, left)
    out_right = jnp.where(live_mask, rnew, right)
    out_moment = jnp.where(live_mask, vnew, moment)
    out_master = jnp.where(live_mask, wnew, weights)
    regathered = gather_blocks(out_master.astype(jnp.bfloat16), owner_of, slot_rank, replica)
    return (
        out_left[None, None],
        out_right[None, None],
        out_moment[None, None],
        out_master[None, None],
        regathered,
    )


def solution(mesh):
    in_specs = (
        P("dp", "shard", None, None),
        P("shard", None),
        P(),
        P("dp", "shard", None, None, None),
        P("dp", "shard", None, None, None),
        P("dp", "shard", None, None, None),
        P("dp", "shard", None, None, None),
        P("dp", "shard", None, None, None),
        P("dp", "shard", None, None, None),
    )
    out_specs = (
        P("dp", "shard", None, None, None),
        P("dp", "shard", None, None, None),
        P("dp", "shard", None, None, None),
        P("dp", "shard", None, None, None),
        P("shard", None, None),
    )
    return jax.shard_map(local, mesh=mesh, in_specs=in_specs, out_specs=out_specs, check_vma=False)
```

```python
import jax
import jax.numpy as jnp
from jax import lax
from jax.experimental import pallas as pl
from jax.experimental.pallas import tpu as pltpu
from jax.sharding import PartitionSpec as P

BETA = 0.95
RATE = 0.3
ADAM_EPS = 1e-08
NORM_EPS = 1e-06


def butterfly_sum(x, axis):
    size = lax.axis_size(axis)
    if size & (size - 1):
        return lax.psum(x, axis)
    step = 1
    while step < size:
        x = x + lax.ppermute(x, axis, [(i, i ^ step) for i in range(size)])
        step *= 2
    return x


def gather_blocks(mine, owner_of, slot_rank, replica):
    size = lax.axis_size("dp")
    slot_count = mine.shape[0]
    if size % 2 or size < 4:
        gathered = lax.all_gather(mine, "dp", axis=0, tiled=True)
        return jnp.take(gathered, owner_of * slot_count + slot_rank, axis=0)
    chips = size // 2
    rightward = [(i, i + 2) for i in range(size - 2)]
    leftward = [(i + 2, i) for i in range(size - 2)]
    partner = [(i, i ^ 1) for i in range(size)]
    from_left = [None] * chips
    from_right = [None] * chips
    from_left[0] = mine
    from_right[0] = mine
    near_left = [None] * chips
    near_right = [None] * chips
    near_left[0] = lax.ppermute(mine, "dp", partner)
    near_right[0] = near_left[0]
    for step in range(1, chips):
        from_left[step] = lax.ppermute(from_left[step - 1], "dp", rightward)
        from_right[step] = lax.ppermute(from_right[step - 1], "dp", leftward)
        near_left[step] = lax.ppermute(from_left[step], "dp", partner)
        near_right[step] = lax.ppermute(from_right[step], "dp", partner)
    pieces = from_left[::-1] + from_right[1:] + near_left[::-1] + near_right[1:]
    chip, core = replica // 2, replica % 2
    owner_chip, owner_core = owner_of // 2, owner_of % 2
    offset = owner_chip - chip + chips - 1
    which = jnp.where(owner_core == core, 0, 1)
    source = jnp.clip(which * (2 * chips - 1) + offset, 0, len(pieces) - 1)
    table = jnp.stack([source, jnp.clip(slot_rank, 0, slot_count - 1)], axis=1).astype(jnp.int32)
    return pick_blocks(table, pieces)


def pick_kernel(table_ref, *refs):
    pieces, out_ref, sems = refs[:-2], refs[-2], refs[-1]

    def start(block, carry):
        for index, piece in enumerate(pieces):
            @pl.when(table_ref[block, 0] == index)
            def _():
                pltpu.make_async_copy(piece.at[table_ref[block, 1]], out_ref.at[block], sems.at[block]).start()

        return carry

    def finish(block, carry):
        pltpu.make_async_copy(pieces[0].at[0], out_ref.at[block], sems.at[block]).wait()
        return carry

    lax.fori_loop(0, out_ref.shape[0], start, 0)
    lax.fori_loop(0, out_ref.shape[0], finish, 0)


def pick_blocks(table, pieces):
    blocks = table.shape[0]
    return pl.pallas_call(
        pick_kernel,
        out_shape=jax.ShapeDtypeStruct((blocks,) + pieces[0].shape[1:], pieces[0].dtype),
        in_specs=[pl.BlockSpec(memory_space=pltpu.SMEM)] + [pl.BlockSpec(memory_space=pl.ANY)] * len(pieces),
        out_specs=pl.BlockSpec(memory_space=pltpu.VMEM),
        scratch_shapes=[pltpu.SemaphoreType.DMA((blocks,))],
    )(table, *pieces)


def local(
    grad_partials,
    owners,
    weight_blocks,
    stats_left,
    stats_right,
    root_left,
    root_right,
    second_moment,
    master,
):
    replica = lax.axis_index("dp")
    column = lax.axis_index("shard")
    replicas = lax.axis_size("dp")
    local_grads = grad_partials[0]
    column_blocks = local_grads.shape[0]
    slot_count = stats_left.shape[2]
    owner_of = owners[:, 0]
    block_ids = jnp.arange(column_blocks, dtype=jnp.int32)
    earlier = (owner_of[None, :] == owner_of[:, None]) & (block_ids[None, :] < block_ids[:, None])
    slot_rank = jnp.sum(earlier.astype(jnp.int32), axis=1)
    matches = (owner_of[None, None, :] == jnp.arange(replicas, dtype=jnp.int32)[:, None, None]) & (
        slot_rank[None, None, :] == jnp.arange(slot_count, dtype=jnp.int32)[None, :, None]
    )
    slot_table = jnp.sum(
        matches.astype(jnp.int32) * jnp.arange(column_blocks, dtype=jnp.int32)[None, None, :],
        axis=2,
    )
    slot_live = jnp.any(matches, axis=2)
    my_table = lax.dynamic_index_in_dim(slot_table, replica, 0, keepdims=False)
    my_live = lax.dynamic_index_in_dim(slot_live, replica, 0, keepdims=False)
    live_float = my_live.astype(jnp.float32)[:, None, None]
    by_owner = jnp.take(local_grads, slot_table.reshape(-1), axis=0, mode="clip").reshape(
        (replicas, slot_count) + local_grads.shape[1:]
    )
    received = lax.all_to_all(by_owner, "dp", 0, 0, tiled=True)
    owned_grad = jnp.sum(received.astype(jnp.float32), axis=0) * live_float
    left = stats_left[0, 0]
    right = stats_right[0, 0]
    moment = second_moment[0, 0]
    weights = master[0, 0]
    global_block = column * column_blocks + my_table
    ends = jnp.cumsum(weight_blocks)
    weight_id = jnp.sum((global_block[:, None] >= ends[None, :]).astype(jnp.int32), axis=1)
    member = (
        weight_id[:, None] == jnp.arange(weight_blocks.shape[0], dtype=jnp.int32)[None, :]
    ).astype(jnp.float32) * my_live.astype(jnp.float32)[:, None]
    vnew = BETA * moment + (1.0 - BETA) * owned_grad * owned_grad
    adam = owned_grad / (jnp.sqrt(vnew) + ADAM_EPS)
    adam_terms = jnp.sum(member * jnp.sum(adam * adam, axis=(1, 2))[:, None], axis=0)
    highest = lax.Precision.HIGHEST
    lnew = BETA * left + (1.0 - BETA) * jnp.einsum(
        "sij,skj->sik", owned_grad, owned_grad, precision=highest
    )
    rnew = BETA * right + (1.0 - BETA) * jnp.einsum(
        "sji,sjk->sik", owned_grad, owned_grad, precision=highest
    )
    grad_half = owned_grad.astype(jnp.bfloat16)
    inner = jnp.einsum(
        "sij,sjk->sik", root_left[0, 0], grad_half, preferred_element_type=jnp.float32
    ).astype(jnp.bfloat16)
    precond = jnp.einsum(
        "sij,sjk->sik", inner, root_right[0, 0], preferred_element_type=jnp.float32
    )
    prec_terms = jnp.sum(member * jnp.sum(precond * precond, axis=(1, 2))[:, None], axis=0)
    norms = butterfly_sum(butterfly_sum(jnp.stack([adam_terms, prec_terms]), "shard"), "dp")
    norm_adam = norms[0]
    norm_prec = norms[1]
    scales = jnp.sqrt(norm_adam / (norm_prec + NORM_EPS))
    slot_scale = jnp.sum(member * scales[None, :], axis=1)
    wnew = weights - RATE * slot_scale[:, None, None] * precond
    live_mask = my_live[:, None, None]
    out_left = jnp.where(live_mask, lnew, left)
    out_right = jnp.where(live_mask, rnew, right)
    out_moment = jnp.where(live_mask, vnew, moment)
    out_master = jnp.where(live_mask, wnew, weights)
    regathered = gather_blocks(out_master.astype(jnp.bfloat16), owner_of, slot_rank, replica)
    return (
        out_left[None, None],
        out_right[None, None],
        out_moment[None, None],
        out_master[None, None],
        regathered,
    )


def solution(mesh):
    in_specs = (
        P("dp", "shard", None, None),
        P("shard", None),
        P(),
        P("dp", "shard", None, None, None),
        P("dp", "shard", None, None, None),
        P("dp", "shard", None, None, None),
        P("dp", "shard", None, None, None),
        P("dp", "shard", None, None, None),
        P("dp", "shard", None, None, None),
    )
    out_specs = (
        P("dp", "shard", None, None, None),
        P("dp", "shard", None, None, None),
        P("dp", "shard", None, None, None),
        P("dp", "shard", None, None, None),
        P("shard", None, None),
    )
    return jax.shard_map(local, mesh=mesh, in_specs=in_specs, out_specs=out_specs, check_vma=False)
```

```python
import jax
import jax.numpy as jnp
from jax import lax
from jax.experimental import pallas as pl
from jax.experimental.pallas import tpu as pltpu
from jax.sharding import PartitionSpec as P

BETA = 0.95
RATE = 0.3
ADAM_EPS = 1e-08
NORM_EPS = 1e-06


def butterfly_sum(x, axis):
    size = lax.axis_size(axis)
    if size & (size - 1):
        return lax.psum(x, axis)
    step = size // 2
    while step:
        x = x + lax.ppermute(x, axis, [(i, i ^ step) for i in range(size)])
        step //= 2
    return x


def gather_blocks(mine, owner_of, slot_rank, replica):
    size = lax.axis_size("dp")
    slot_count = mine.shape[0]
    if size % 2 or size < 4:
        gathered = lax.all_gather(mine, "dp", axis=0, tiled=True)
        return jnp.take(gathered, owner_of * slot_count + slot_rank, axis=0)
    chips = size // 2
    rightward = [(i, i + 2) for i in range(size - 2)]
    leftward = [(i + 2, i) for i in range(size - 2)]
    partner = [(i, i ^ 1) for i in range(size)]
    from_left = [None] * chips
    from_right = [None] * chips
    from_left[0] = mine
    from_right[0] = mine
    near_left = [None] * chips
    near_right = [None] * chips
    near_left[0] = lax.ppermute(mine, "dp", partner)
    near_right[0] = near_left[0]
    for step in range(1, chips):
        from_left[step] = lax.ppermute(from_left[step - 1], "dp", rightward)
        from_right[step] = lax.ppermute(from_right[step - 1], "dp", leftward)
        near_left[step] = lax.ppermute(from_left[step], "dp", partner)
        near_right[step] = lax.ppermute(from_right[step], "dp", partner)
    pieces = from_left[::-1] + from_right[1:] + near_left[::-1] + near_right[1:]
    chip, core = replica // 2, replica % 2
    owner_chip, owner_core = owner_of // 2, owner_of % 2
    offset = owner_chip - chip + chips - 1
    which = jnp.where(owner_core == core, 0, 1)
    source = jnp.clip(which * (2 * chips - 1) + offset, 0, len(pieces) - 1)
    table = jnp.stack([source, jnp.clip(slot_rank, 0, slot_count - 1)], axis=1).astype(jnp.int32)
    return pick_blocks(table, pieces)


def pick_kernel(table_ref, *refs):
    pieces, out_ref, sems = refs[:-2], refs[-2], refs[-1]

    def start(block, carry):
        for index, piece in enumerate(pieces):
            @pl.when(table_ref[block, 0] == index)
            def _():
                pltpu.make_async_copy(piece.at[table_ref[block, 1]], out_ref.at[block], sems.at[block]).start()

        return carry

    def finish(block, carry):
        pltpu.make_async_copy(pieces[0].at[0], out_ref.at[block], sems.at[block]).wait()
        return carry

    lax.fori_loop(0, out_ref.shape[0], start, 0)
    lax.fori_loop(0, out_ref.shape[0], finish, 0)


def pick_blocks(table, pieces):
    blocks = table.shape[0]
    return pl.pallas_call(
        pick_kernel,
        out_shape=jax.ShapeDtypeStruct((blocks,) + pieces[0].shape[1:], pieces[0].dtype),
        in_specs=[pl.BlockSpec(memory_space=pltpu.SMEM)] + [pl.BlockSpec(memory_space=pl.ANY)] * len(pieces),
        out_specs=pl.BlockSpec(memory_space=pltpu.VMEM),
        scratch_shapes=[pltpu.SemaphoreType.DMA((blocks,))],
    )(table, *pieces)


def local(
    grad_partials,
    owners,
    weight_blocks,
    stats_left,
    stats_right,
    root_left,
    root_right,
    second_moment,
    master,
):
    replica = lax.axis_index("dp")
    column = lax.axis_index("shard")
    replicas = lax.axis_size("dp")
    local_grads = grad_partials[0]
    column_blocks = local_grads.shape[0]
    slot_count = stats_left.shape[2]
    owner_of = owners[:, 0]
    block_ids = jnp.arange(column_blocks, dtype=jnp.int32)
    earlier = (owner_of[None, :] == owner_of[:, None]) & (block_ids[None, :] < block_ids[:, None])
    slot_rank = jnp.sum(earlier.astype(jnp.int32), axis=1)
    matches = (owner_of[None, None, :] == jnp.arange(replicas, dtype=jnp.int32)[:, None, None]) & (
        slot_rank[None, None, :] == jnp.arange(slot_count, dtype=jnp.int32)[None, :, None]
    )
    slot_table = jnp.sum(
        matches.astype(jnp.int32) * jnp.arange(column_blocks, dtype=jnp.int32)[None, None, :],
        axis=2,
    )
    slot_live = jnp.any(matches, axis=2)
    my_table = lax.dynamic_index_in_dim(slot_table, replica, 0, keepdims=False)
    my_live = lax.dynamic_index_in_dim(slot_live, replica, 0, keepdims=False)
    live_float = my_live.astype(jnp.float32)[:, None, None]
    by_owner = jnp.take(local_grads, slot_table.reshape(-1), axis=0, mode="clip").reshape(
        (replicas, slot_count) + local_grads.shape[1:]
    )
    received = lax.all_to_all(by_owner, "dp", 0, 0, tiled=True)
    owned_grad = jnp.sum(received.astype(jnp.float32), axis=0) * live_float
    left = stats_left[0, 0]
    right = stats_right[0, 0]
    moment = second_moment[0, 0]
    weights = master[0, 0]
    global_block = column * column_blocks + my_table
    ends = jnp.cumsum(weight_blocks)
    weight_id = jnp.sum((global_block[:, None] >= ends[None, :]).astype(jnp.int32), axis=1)
    member = (
        weight_id[:, None] == jnp.arange(weight_blocks.shape[0], dtype=jnp.int32)[None, :]
    ).astype(jnp.float32) * my_live.astype(jnp.float32)[:, None]
    vnew = BETA * moment + (1.0 - BETA) * owned_grad * owned_grad
    adam = owned_grad / (jnp.sqrt(vnew) + ADAM_EPS)
    adam_terms = jnp.sum(member * jnp.sum(adam * adam, axis=(1, 2))[:, None], axis=0)
    highest = lax.Precision.HIGHEST
    lnew = BETA * left + (1.0 - BETA) * jnp.einsum(
        "sij,skj->sik", owned_grad, owned_grad, precision=highest
    )
    rnew = BETA * right + (1.0 - BETA) * jnp.einsum(
        "sji,sjk->sik", owned_grad, owned_grad, precision=highest
    )
    grad_half = owned_grad.astype(jnp.bfloat16)
    inner = jnp.einsum(
        "sij,sjk->sik", root_left[0, 0], grad_half, preferred_element_type=jnp.float32
    ).astype(jnp.bfloat16)
    precond = jnp.einsum(
        "sij,sjk->sik", inner, root_right[0, 0], preferred_element_type=jnp.float32
    )
    prec_terms = jnp.sum(member * jnp.sum(precond * precond, axis=(1, 2))[:, None], axis=0)
    norms = butterfly_sum(butterfly_sum(jnp.stack([adam_terms, prec_terms]), "shard"), "dp")
    norm_adam = norms[0]
    norm_prec = norms[1]
    scales = jnp.sqrt(norm_adam / (norm_prec + NORM_EPS))
    slot_scale = jnp.sum(member * scales[None, :], axis=1)
    wnew = weights - RATE * slot_scale[:, None, None] * precond
    live_mask = my_live[:, None, None]
    out_left = jnp.where(live_mask, lnew, left)
    out_right = jnp.where(live_mask, rnew, right)
    out_moment = jnp.where(live_mask, vnew, moment)
    out_master = jnp.where(live_mask, wnew, weights)
    regathered = gather_blocks(out_master.astype(jnp.bfloat16), owner_of, slot_rank, replica)
    return (
        out_left[None, None],
        out_right[None, None],
        out_moment[None, None],
        out_master[None, None],
        regathered,
    )


def solution(mesh):
    in_specs = (
        P("dp", "shard", None, None),
        P("shard", None),
        P(),
        P("dp", "shard", None, None, None),
        P("dp", "shard", None, None, None),
        P("dp", "shard", None, None, None),
        P("dp", "shard", None, None, None),
        P("dp", "shard", None, None, None),
        P("dp", "shard", None, None, None),
    )
    out_specs = (
        P("dp", "shard", None, None, None),
        P("dp", "shard", None, None, None),
        P("dp", "shard", None, None, None),
        P("dp", "shard", None, None, None),
        P("shard", None, None),
    )
    return jax.shard_map(local, mesh=mesh, in_specs=in_specs, out_specs=out_specs, check_vma=False)
```

```python
import jax
import jax.numpy as jnp
from jax import lax
from jax.experimental import pallas as pl
from jax.experimental.pallas import tpu as pltpu
from jax.sharding import PartitionSpec as P

BETA = 0.95
RATE = 0.3
ADAM_EPS = 1e-08
NORM_EPS = 1e-06


def butterfly_sum(x, axis):
    size = lax.axis_size(axis)
    if size & (size - 1):
        return lax.psum(x, axis)
    step = 1
    while step < size:
        x = x + lax.ppermute(x, axis, [(i, i ^ step) for i in range(size)])
        step *= 2
    return x


def gather_blocks(mine, owner_of, slot_rank, replica):
    size = lax.axis_size("dp")
    slot_count = mine.shape[0]
    if size % 2 or size < 4:
        gathered = lax.all_gather(mine, "dp", axis=0, tiled=True)
        return jnp.take(gathered, owner_of * slot_count + slot_rank, axis=0)
    chips = size // 2
    rightward = [(i, i + 2) for i in range(size - 2)]
    leftward = [(i + 2, i) for i in range(size - 2)]
    partner = [(i, i ^ 1) for i in range(size)]
    from_left = [None] * chips
    from_right = [None] * chips
    from_left[0] = mine
    from_right[0] = mine
    near_left = [None] * chips
    near_right = [None] * chips
    near_left[0] = lax.ppermute(mine, "dp", partner)
    near_right[0] = near_left[0]
    for step in range(1, chips):
        from_left[step] = lax.ppermute(from_left[step - 1], "dp", rightward)
        from_right[step] = lax.ppermute(from_right[step - 1], "dp", leftward)
        near_left[step] = lax.ppermute(from_left[step], "dp", partner)
        near_right[step] = lax.ppermute(from_right[step], "dp", partner)
    pieces = from_left[::-1] + from_right[1:] + near_left[::-1] + near_right[1:]
    chip, core = replica // 2, replica % 2
    owner_chip, owner_core = owner_of // 2, owner_of % 2
    offset = owner_chip - chip + chips - 1
    which = jnp.where(owner_core == core, 0, 1)
    source = jnp.clip(which * (2 * chips - 1) + offset, 0, len(pieces) - 1)
    table = jnp.stack([source, jnp.clip(slot_rank, 0, slot_count - 1)], axis=1).astype(jnp.int32)
    return pick_blocks(table, pieces)


def pick_kernel(table_ref, *refs):
    pieces, out_ref, sems = refs[:-2], refs[-2], refs[-1]

    def start(block, carry):
        for index, piece in enumerate(pieces):
            @pl.when(table_ref[block, 0] == index)
            def _():
                pltpu.make_async_copy(piece.at[table_ref[block, 1]], out_ref.at[block], sems.at[block]).start()

        return carry

    def finish(block, carry):
        pltpu.make_async_copy(pieces[0].at[0], out_ref.at[block], sems.at[block]).wait()
        return carry

    lax.fori_loop(0, out_ref.shape[0], start, 0)
    lax.fori_loop(0, out_ref.shape[0], finish, 0)


def pick_blocks(table, pieces):
    blocks = table.shape[0]
    return pl.pallas_call(
        pick_kernel,
        out_shape=jax.ShapeDtypeStruct((blocks,) + pieces[0].shape[1:], pieces[0].dtype),
        in_specs=[pl.BlockSpec(memory_space=pltpu.SMEM)] + [pl.BlockSpec(memory_space=pl.ANY)] * len(pieces),
        out_specs=pl.BlockSpec(memory_space=pltpu.VMEM),
        scratch_shapes=[pltpu.SemaphoreType.DMA((blocks,))],
    )(table, *pieces)


def local(
    grad_partials,
    owners,
    weight_blocks,
    stats_left,
    stats_right,
    root_left,
    root_right,
    second_moment,
    master,
):
    replica = lax.axis_index("dp")
    column = lax.axis_index("shard")
    replicas = lax.axis_size("dp")
    local_grads = grad_partials[0]
    column_blocks = local_grads.shape[0]
    slot_count = stats_left.shape[2]
    owner_of = owners[:, 0]
    block_ids = jnp.arange(column_blocks, dtype=jnp.int32)
    earlier = (owner_of[None, :] == owner_of[:, None]) & (block_ids[None, :] < block_ids[:, None])
    slot_rank = jnp.sum(earlier.astype(jnp.int32), axis=1)
    matches = (owner_of[None, None, :] == jnp.arange(replicas, dtype=jnp.int32)[:, None, None]) & (
        slot_rank[None, None, :] == jnp.arange(slot_count, dtype=jnp.int32)[None, :, None]
    )
    slot_table = jnp.sum(
        matches.astype(jnp.int32) * jnp.arange(column_blocks, dtype=jnp.int32)[None, None, :],
        axis=2,
    )
    slot_live = jnp.any(matches, axis=2)
    if slot_count == 2:
        owned = owner_of[None, :] == jnp.arange(replicas, dtype=jnp.int32)[:, None]
        count = jnp.sum(owned.astype(jnp.int32), axis=1)
        first = jnp.min(jnp.where(owned, block_ids[None, :], column_blocks), axis=1)
        last = jnp.max(jnp.where(owned, block_ids[None, :], -1), axis=1)
        slot_live = jnp.stack([count >= 1, count >= 2], axis=1)
        slot_table = jnp.where(slot_live, jnp.stack([first, last], axis=1), 0)
    my_table = lax.dynamic_index_in_dim(slot_table, replica, 0, keepdims=False)
    my_live = lax.dynamic_index_in_dim(slot_live, replica, 0, keepdims=False)
    live_float = my_live.astype(jnp.float32)[:, None, None]
    by_owner = jnp.take(local_grads, slot_table.reshape(-1), axis=0, mode="clip").reshape(
        (replicas, slot_count) + local_grads.shape[1:]
    )
    received = lax.all_to_all(by_owner, "dp", 0, 0, tiled=True)
    owned_grad = jnp.sum(received.astype(jnp.float32), axis=0) * live_float
    left = stats_left[0, 0]
    right = stats_right[0, 0]
    moment = second_moment[0, 0]
    weights = master[0, 0]
    global_block = column * column_blocks + my_table
    ends = jnp.cumsum(weight_blocks)
    weight_id = jnp.sum((global_block[:, None] >= ends[None, :]).astype(jnp.int32), axis=1)
    member = (
        weight_id[:, None] == jnp.arange(weight_blocks.shape[0], dtype=jnp.int32)[None, :]
    ).astype(jnp.float32) * my_live.astype(jnp.float32)[:, None]
    vnew = BETA * moment + (1.0 - BETA) * owned_grad * owned_grad
    adam = owned_grad / (jnp.sqrt(vnew) + ADAM_EPS)
    adam_terms = jnp.sum(member * jnp.sum(adam * adam, axis=(1, 2))[:, None], axis=0)
    highest = lax.Precision.HIGHEST
    lnew = BETA * left + (1.0 - BETA) * jnp.einsum(
        "sij,skj->sik", owned_grad, owned_grad, precision=highest
    )
    rnew = BETA * right + (1.0 - BETA) * jnp.einsum(
        "sji,sjk->sik", owned_grad, owned_grad, precision=highest
    )
    grad_half = owned_grad.astype(jnp.bfloat16)
    inner = jnp.einsum(
        "sij,sjk->sik", root_left[0, 0], grad_half, preferred_element_type=jnp.float32
    ).astype(jnp.bfloat16)
    precond = jnp.einsum(
        "sij,sjk->sik", inner, root_right[0, 0], preferred_element_type=jnp.float32
    )
    prec_terms = jnp.sum(member * jnp.sum(precond * precond, axis=(1, 2))[:, None], axis=0)
    norms = butterfly_sum(butterfly_sum(jnp.stack([adam_terms, prec_terms]), "shard"), "dp")
    norm_adam = norms[0]
    norm_prec = norms[1]
    scales = jnp.sqrt(norm_adam / (norm_prec + NORM_EPS))
    slot_scale = jnp.sum(member * scales[None, :], axis=1)
    wnew = weights - RATE * slot_scale[:, None, None] * precond
    live_mask = my_live[:, None, None]
    out_left = jnp.where(live_mask, lnew, left)
    out_right = jnp.where(live_mask, rnew, right)
    out_moment = jnp.where(live_mask, vnew, moment)
    out_master = jnp.where(live_mask, wnew, weights)
    regathered = gather_blocks(out_master.astype(jnp.bfloat16), owner_of, slot_rank, replica)
    return (
        out_left[None, None],
        out_right[None, None],
        out_moment[None, None],
        out_master[None, None],
        regathered,
    )


def solution(mesh):
    in_specs = (
        P("dp", "shard", None, None),
        P("shard", None),
        P(),
        P("dp", "shard", None, None, None),
        P("dp", "shard", None, None, None),
        P("dp", "shard", None, None, None),
        P("dp", "shard", None, None, None),
        P("dp", "shard", None, None, None),
        P("dp", "shard", None, None, None),
    )
    out_specs = (
        P("dp", "shard", None, None, None),
        P("dp", "shard", None, None, None),
        P("dp", "shard", None, None, None),
        P("dp", "shard", None, None, None),
        P("shard", None, None),
    )
    return jax.shard_map(local, mesh=mesh, in_specs=in_specs, out_specs=out_specs, check_vma=False)
```

```python
import jax
import jax.numpy as jnp
from jax import lax
from jax.experimental import pallas as pl
from jax.experimental.pallas import tpu as pltpu
from jax.sharding import PartitionSpec as P

BETA = 0.95
RATE = 0.3
ADAM_EPS = 1e-08
NORM_EPS = 1e-06


def butterfly_sum(x, axis):
    size = lax.axis_size(axis)
    if size & (size - 1):
        return lax.psum(x, axis)
    step = 1
    while step < size:
        x = x + lax.ppermute(x, axis, [(i, i ^ step) for i in range(size)])
        step *= 2
    return x


def gather_blocks(mine, owner_of, slot_rank, replica):
    size = lax.axis_size("dp")
    slot_count = mine.shape[0]
    if size % 2 or size < 4:
        gathered = lax.all_gather(mine, "dp", axis=0, tiled=True)
        return jnp.take(gathered, owner_of * slot_count + slot_rank, axis=0)
    chips = size // 2
    rightward = [(i, i + 2) for i in range(size - 2)]
    leftward = [(i + 2, i) for i in range(size - 2)]
    partner = [(i, i ^ 1) for i in range(size)]
    from_left = [None] * chips
    from_right = [None] * chips
    from_left[0] = mine
    from_right[0] = mine
    near_left = [None] * chips
    near_right = [None] * chips
    near_left[0] = lax.ppermute(mine, "dp", partner)
    near_right[0] = near_left[0]
    for step in range(1, chips):
        from_left[step] = lax.ppermute(from_left[step - 1], "dp", rightward)
        from_right[step] = lax.ppermute(from_right[step - 1], "dp", leftward)
        near_left[step] = lax.ppermute(from_left[step], "dp", partner)
        near_right[step] = lax.ppermute(from_right[step], "dp", partner)
    pieces = from_left[::-1] + from_right[1:] + near_left[::-1] + near_right[1:]
    chip, core = replica // 2, replica % 2
    owner_chip, owner_core = owner_of // 2, owner_of % 2
    offset = owner_chip - chip + chips - 1
    which = jnp.where(owner_core == core, 0, 1)
    source = jnp.clip(which * (2 * chips - 1) + offset, 0, len(pieces) - 1)
    table = jnp.stack([source, jnp.clip(slot_rank, 0, slot_count - 1)], axis=1).astype(jnp.int32)
    return pick_blocks(table, pieces)


def pick_kernel(table_ref, *refs):
    pieces, out_ref, sems = refs[:-2], refs[-2], refs[-1]

    def start(block, carry):
        for index, piece in enumerate(pieces):
            @pl.when(table_ref[block, 0] == index)
            def _():
                pltpu.make_async_copy(piece.at[table_ref[block, 1]], out_ref.at[block], sems.at[block]).start()

        return carry

    def finish(block, carry):
        pltpu.make_async_copy(pieces[0].at[0], out_ref.at[block], sems.at[block]).wait()
        return carry

    lax.fori_loop(0, out_ref.shape[0], start, 0)
    lax.fori_loop(0, out_ref.shape[0], finish, 0)


def pick_blocks(table, pieces):
    blocks = table.shape[0]
    return pl.pallas_call(
        pick_kernel,
        out_shape=jax.ShapeDtypeStruct((blocks,) + pieces[0].shape[1:], pieces[0].dtype),
        in_specs=[pl.BlockSpec(memory_space=pltpu.SMEM)] + [pl.BlockSpec(memory_space=pl.ANY)] * len(pieces),
        out_specs=pl.BlockSpec(memory_space=pltpu.VMEM),
        scratch_shapes=[pltpu.SemaphoreType.DMA((blocks,))],
    )(table, *pieces)


def local(
    grad_partials,
    owners,
    weight_blocks,
    stats_left,
    stats_right,
    root_left,
    root_right,
    second_moment,
    master,
):
    replica = lax.axis_index("dp")
    column = lax.axis_index("shard")
    replicas = lax.axis_size("dp")
    local_grads = grad_partials[0]
    column_blocks = local_grads.shape[0]
    slot_count = stats_left.shape[2]
    owner_of = owners[:, 0]
    block_ids = jnp.arange(column_blocks, dtype=jnp.int32)
    earlier = (owner_of[None, :] == owner_of[:, None]) & (block_ids[None, :] < block_ids[:, None])
    slot_rank = jnp.sum(earlier.astype(jnp.int32), axis=1)
    matches = (owner_of[None, None, :] == jnp.arange(replicas, dtype=jnp.int32)[:, None, None]) & (
        slot_rank[None, None, :] == jnp.arange(slot_count, dtype=jnp.int32)[None, :, None]
    )
    slot_table = jnp.sum(
        matches.astype(jnp.int32) * jnp.arange(column_blocks, dtype=jnp.int32)[None, None, :],
        axis=2,
    )
    slot_live = jnp.any(matches, axis=2)
    if slot_count == 2:
        owned = owner_of[None, :] == jnp.arange(replicas, dtype=jnp.int32)[:, None]
        count = jnp.sum(owned.astype(jnp.int32), axis=1)
        first = jnp.min(jnp.where(owned, block_ids[None, :], column_blocks), axis=1)
        last = jnp.max(jnp.where(owned, block_ids[None, :], -1), axis=1)
        slot_live = jnp.stack([count >= 1, count >= 2], axis=1)
        slot_table = jnp.where(slot_live, jnp.stack([first, last], axis=1), 0)
    my_table = lax.dynamic_index_in_dim(slot_table, replica, 0, keepdims=False)
    my_live = lax.dynamic_index_in_dim(slot_live, replica, 0, keepdims=False)
    live_float = my_live.astype(jnp.float32)[:, None, None]
    by_owner = jnp.take(local_grads, slot_table.reshape(-1), axis=0, mode="clip").reshape(
        (replicas, slot_count) + local_grads.shape[1:]
    )
    received = lax.all_to_all(by_owner, "dp", 0, 0, tiled=True)
    owned_grad = jnp.sum(received.astype(jnp.float32), axis=0) * live_float
    left = stats_left[0, 0]
    right = stats_right[0, 0]
    moment = second_moment[0, 0]
    weights = master[0, 0]
    global_block = column * column_blocks + my_table
    ends = jnp.cumsum(weight_blocks)
    weight_id = jnp.sum((global_block[:, None] >= ends[None, :]).astype(jnp.int32), axis=1)
    member = (
        weight_id[:, None] == jnp.arange(weight_blocks.shape[0], dtype=jnp.int32)[None, :]
    ).astype(jnp.float32) * my_live.astype(jnp.float32)[:, None]
    vnew = BETA * moment + (1.0 - BETA) * owned_grad * owned_grad
    adam = owned_grad / (jnp.sqrt(vnew) + ADAM_EPS)
    adam_terms = jnp.sum(member * jnp.sum(adam * adam, axis=(1, 2))[:, None], axis=0)
    highest = lax.Precision.HIGHEST
    lnew = BETA * left + (1.0 - BETA) * jnp.einsum(
        "sij,skj->sik", owned_grad, owned_grad, precision=highest
    )
    rnew = BETA * right + (1.0 - BETA) * jnp.einsum(
        "sji,sjk->sik", owned_grad, owned_grad, precision=highest
    )
    grad_half = owned_grad.astype(jnp.bfloat16)
    inner = jnp.einsum(
        "sij,sjk->sik", root_left[0, 0], grad_half, preferred_element_type=jnp.float32
    ).astype(jnp.bfloat16)
    precond = jnp.einsum(
        "sij,sjk->sik", inner, root_right[0, 0], preferred_element_type=jnp.float32
    )
    prec_terms = jnp.sum(member * jnp.sum(precond * precond, axis=(1, 2))[:, None], axis=0)
    norms = butterfly_sum(butterfly_sum(jnp.stack([adam_terms, prec_terms]), "shard"), "dp")
    norm_adam = norms[0]
    norm_prec = norms[1]
    scales = jnp.sqrt(norm_adam / (norm_prec + NORM_EPS))
    slot_scale = jnp.sum(member * scales[None, :], axis=1)
    wnew = weights - RATE * slot_scale[:, None, None] * precond
    live_mask = my_live[:, None, None]
    out_left = jnp.where(live_mask, lnew, left)
    out_right = jnp.where(live_mask, rnew, right)
    out_moment = jnp.where(live_mask, vnew, moment)
    out_master = jnp.where(live_mask, wnew, weights)
    regathered = gather_blocks(wnew.astype(jnp.bfloat16), owner_of, slot_rank, replica)
    return (
        out_left[None, None],
        out_right[None, None],
        out_moment[None, None],
        out_master[None, None],
        regathered,
    )


def solution(mesh):
    in_specs = (
        P("dp", "shard", None, None),
        P("shard", None),
        P(),
        P("dp", "shard", None, None, None),
        P("dp", "shard", None, None, None),
        P("dp", "shard", None, None, None),
        P("dp", "shard", None, None, None),
        P("dp", "shard", None, None, None),
        P("dp", "shard", None, None, None),
    )
    out_specs = (
        P("dp", "shard", None, None, None),
        P("dp", "shard", None, None, None),
        P("dp", "shard", None, None, None),
        P("dp", "shard", None, None, None),
        P("shard", None, None),
    )
    return jax.shard_map(local, mesh=mesh, in_specs=in_specs, out_specs=out_specs, check_vma=False)
```
